256 devices in a mesh: dp: 8 (over z), seq: 32 (over y, x, core).
Axes of the slice: x: 4, y: 4, z: 8, core: 2. Of those that a mesh axis runs over, the one named last changes fastest.
Arguments:
- queries: bfloat16 [8, 8192, 1024], P('dp', 'seq'), may hold values from -150 to 150
- keys: bfloat16 [8, 8192, 1024], P('dp', 'seq'), may hold values from -5 to 5
- values: bfloat16 [8, 8192, 1024], P('dp', 'seq'), may hold values from -5 to 5
- out_weight: bfloat16 [1024, 1024], replicated, may hold values from -0.1875 to 0.1875
- out_grad: bfloat16 [8, 8192, 1024], P('dp', 'seq'), may hold values from -6 to 6
- pooled: int32 [8, 8192], P('dp', 'seq'), may hold values from 0 to 1, as said below
Outputs:
- query_grad: bfloat16 [8, 8192, 1024], P('dp', 'seq')
- key_grad: bfloat16 [8, 8192, 1024], P('dp', 'seq')
- value_grad: bfloat16 [8, 8192, 1024], P('dp', 'seq')
- weight_grad: float32 [1024, 1024], P('seq')
The draws below stay inside these ranges and needn't reach their ends.
Inputs may be any that keep to these rules, and one draw needn't show every extreme that they name: Every stream has at least one block of 128 tokens in which no token has pooled = 1.
All inputs are finite; a program needn't handle non-finite values.
Results may differ from the reference program's by a relative error of at most 0.035.
Values may be sent and summed in bfloat16 or wider, within the bound.
No kernel may reach another device: no remote copies, remote signals or barrier semaphores. Data moves between devices by JAX's collectives and lax.ppermute only.
A program may use at most 128 MiB of HBM per device.

```python
import math
import jax
import jax.numpy as jnp
from jax import lax

HEADS = 16
HEAD_DIM = 64
BLOCK = 128
D = 1024
STREAMS = 8
SEQ = 8192


def block_structured(key, salt, block_weight, noise_weight):
    block_key = jax.random.fold_in(key, salt)
    noise_key = jax.random.fold_in(key, salt + 1)
    block_part = jax.random.truncated_normal(block_key, -3.0, 3.0, (STREAMS, SEQ // BLOCK, 1, D), jnp.float32)
    noise_part = jax.random.truncated_normal(noise_key, -3.0, 3.0, (STREAMS, SEQ // BLOCK, BLOCK, D), jnp.float32)
    mixed = block_weight * block_part + noise_weight * noise_part
    return mixed.reshape(STREAMS, SEQ, D)


def key_field(key):
    field = block_structured(key, 101, 0.5, 0.85)
    return field


def draw_keys(key, part):
    return key_field(key).astype(jnp.bfloat16)


def draw_values(key, part):
    return block_structured(key, 202, 0.8, 0.6).astype(jnp.bfloat16)


def draw_queries(key, part):
    noise_key = jax.random.fold_in(key, 303)
    base = 2.0 * jax.random.truncated_normal(noise_key, -3.0, 3.0, (STREAMS, SEQ, D), jnp.float32)
    return base.astype(jnp.bfloat16)


def draw_pooled(key, part):
    block_count = SEQ // BLOCK
    token_draw = jax.random.randint(jax.random.fold_in(key, 404), (STREAMS, block_count, BLOCK), 0, 32)
    token_bits = (token_draw == 0).astype(jnp.int32)
    emptied = jax.random.randint(jax.random.fold_in(key, 405), (STREAMS, 1), 0, block_count)
    extra = jax.random.randint(jax.random.fold_in(key, 406), (STREAMS, block_count), 0, 8)
    block_ids = jnp.arange(block_count)[None, :]
    keep = ((block_ids != emptied) & (extra != 0)).astype(jnp.int32)
    return (token_bits * keep[:, :, None]).reshape(STREAMS, SEQ).astype(jnp.int32)


def spiked(drawn, own_key, source, target, shards_of, factor):
    def block_of(dim):
        return (jnp.arange(drawn.shape[dim]) // (drawn.shape[dim] // shards_of)).reshape((-1,) + (1,) * (drawn.ndim - 1 - dim))

    one_side = jax.random.permutation(own_key, shards_of)[block_of(target)]
    second = (block_of(target) + shards_of // 2) % shards_of
    return jnp.where((block_of(source) == one_side) | (block_of(source) == second), factor * drawn, drawn)


def levels(key, dims, split, least, top_value):
    def one(axis_at, blocks):
        steps = jax.random.uniform(jax.random.fold_in(jax.random.fold_in(key, 6), axis_at), (blocks,), jnp.float32, least / len(split), top_value / len(split))
        return jnp.repeat(jnp.exp(steps), dims[axis_at] // blocks).reshape((-1,) + (1,) * (len(dims) - axis_at - 1))

    gain = one(*split[0])
    for cut in split[1:]:
        gain = gain * one(*cut)
    return gain


def normal_values(own_key, extent, width, limit, cuts=(), kind=jnp.bfloat16):
    values = width * jax.random.normal(own_key, extent, jnp.float32)
    if cuts:
        values = values * levels(own_key, extent, cuts, -0.22, 0.18)
    return jnp.clip(values, -limit, limit).astype(kind)


def bell_draw_with(rng, extent, scale, most, shards, heavy, dtype=jnp.bfloat16):
    result = scale * jax.random.normal(rng, extent, jnp.float32)
    if shards:
        result = result * levels(rng, extent, shards, -0.22, 0.18)
    return jnp.clip(spiked(result, jax.random.fold_in(rng, 3), *heavy), -most, most).astype(dtype)


def setup_inputs(seed: int = 0) -> dict:
    key_list = jax.random.split(jax.random.key(seed), 7)
    queries = draw_queries(jax.random.fold_in(key_list[6], 71), 0)
    keys = draw_keys(jax.random.fold_in(key_list[6], 71), 0)
    values = draw_values(jax.random.fold_in(key_list[6], 71), 0)
    out_weight = normal_values(key_list[3], (D, D), D ** -0.5, 0.1875)
    out_grad = bell_draw_with(key_list[4], (STREAMS, SEQ, D), 1.0, 6.0, ((0, 8), (1, 32)), (1, 2, 32, 2.75))
    pooled = draw_pooled(jax.random.fold_in(key_list[6], 71), 0)
    return dict(queries=queries, keys=keys, values=values, out_weight=out_weight, out_grad=out_grad, pooled=pooled)


def to_bf16(numbers):
    return lax.optimization_barrier(numbers.astype(jnp.bfloat16)).astype(jnp.float32)

def windows(rows, block_count):
    padded = jnp.pad(rows.reshape(block_count, BLOCK, -1), ((1, 1), (0, 0), (0, 0)))
    return jnp.concatenate([padded[:-2], padded[1:-1], padded[2:]], axis=1)

def unwindow(grads, block_count):
    parts = grads.reshape(block_count, 3, BLOCK, grads.shape[-1])
    edge_zero = jnp.zeros((1, BLOCK, grads.shape[-1]), jnp.float32)
    summed = parts[:, 1] + jnp.concatenate([parts[1:, 0], edge_zero], axis=0)
    summed = summed + jnp.concatenate([edge_zero, parts[:-1, 2]], axis=0)
    return summed.reshape(block_count * BLOCK, grads.shape[-1])

def head_pass(query_h, key_h, value_h, grad_h, coarse_kh, coarse_vh, counts):
    block_count = counts.shape[0]
    score_scale = 1.0 / math.sqrt(HEAD_DIM)
    query_blk = query_h.astype(jnp.float32).reshape(block_count, BLOCK, HEAD_DIM)
    grad_blk = grad_h.astype(jnp.float32).reshape(block_count, BLOCK, HEAD_DIM)
    key_win = windows(key_h.astype(jnp.float32), block_count)
    value_win = windows(value_h.astype(jnp.float32), block_count)
    coarse_k = coarse_kh.astype(jnp.float32)
    coarse_v = coarse_vh.astype(jnp.float32)
    block_ids = jnp.arange(block_count)
    offsets = jnp.repeat(jnp.arange(3) - 1, BLOCK)
    key_blocks = block_ids[:, None] + offsets[None, :]
    fine_ok = (key_blocks >= 0) & (key_blocks < block_count)
    far_ok = jnp.abs(block_ids[:, None] - block_ids[None, :]) >= 2
    fine_s = jnp.einsum('nqe,nke->nqk', query_blk, key_win) * score_scale
    coarse_s = jnp.einsum('nqe,ce->nqc', query_blk, coarse_k) * score_scale
    fine_s = jnp.where(fine_ok[:, None, :], fine_s, -jnp.inf)
    coarse_s = jnp.where(far_ok[:, None, :], coarse_s, -jnp.inf)
    row_top = jnp.maximum(lax.optimization_barrier(jnp.max(fine_s, axis=-1)), lax.optimization_barrier(jnp.max(coarse_s, axis=-1)))[..., None]
    fine_e = jnp.exp(fine_s - row_top)
    coarse_e = counts[None, None, :] * jnp.exp(coarse_s - row_top)
    row_total = lax.optimization_barrier(jnp.sum(fine_e, axis=-1, keepdims=True)) + lax.optimization_barrier(jnp.sum(coarse_e, axis=-1, keepdims=True))
    fine_w = fine_e / row_total
    coarse_w = coarse_e / row_total
    fine_wb = to_bf16(fine_w)
    coarse_wb = to_bf16(coarse_w)
    attended = to_bf16(jnp.einsum('nqk,nke->nqe', fine_wb, value_win) + jnp.einsum('nqc,ce->nqe', coarse_wb, coarse_v))
    fine_dot = jnp.einsum('nqe,nke->nqk', grad_blk, value_win)
    coarse_dot = jnp.einsum('nqe,ce->nqc', grad_blk, coarse_v)
    delta_rows = lax.optimization_barrier(jnp.sum(grad_blk * attended, axis=-1, keepdims=True))
    fine_ds = to_bf16(fine_w * (fine_dot - delta_rows))
    coarse_ds = to_bf16(coarse_w * (coarse_dot - delta_rows))
    query_grad = (jnp.einsum('nqk,nke->nqe', fine_ds, key_win) + jnp.einsum('nqc,ce->nqe', coarse_ds, coarse_k)) * score_scale
    key_grad = unwindow(jnp.einsum('nqk,nqe->nke', fine_ds, query_blk) * score_scale, block_count)
    value_grad = unwindow(jnp.einsum('nqk,nqe->nke', fine_wb, grad_blk), block_count)
    coarse_kg = jnp.einsum('nqc,nqe->ce', coarse_ds, query_blk) * score_scale
    coarse_vg = jnp.einsum('nqc,nqe->ce', coarse_wb, grad_blk)
    return (attended.reshape(-1, HEAD_DIM), query_grad.reshape(-1, HEAD_DIM), key_grad, value_grad, coarse_kg, coarse_vg)

def by_head(rows):
    return rows.reshape(rows.shape[0], HEADS, HEAD_DIM).transpose(1, 0, 2)

def join_heads(stacked):
    return stacked.transpose(1, 0, 2).reshape(stacked.shape[1], D)

def stream_pass(operands, out_weight):
    query_rows, key_rows, value_rows, grad_out, pooled_row = operands
    block_count = SEQ // BLOCK
    pooled_mask = pooled_row.astype(jnp.float32).reshape(block_count, BLOCK)
    counts = lax.optimization_barrier(jnp.sum(pooled_mask, axis=1))
    divisor = jnp.maximum(counts, 1.0)
    key_sum = jnp.einsum('nb,nbd->nd', pooled_mask, key_rows.astype(jnp.float32).reshape(block_count, BLOCK, D))
    value_sum = jnp.einsum('nb,nbd->nd', pooled_mask, value_rows.astype(jnp.float32).reshape(block_count, BLOCK, D))
    coarse_keys = (key_sum / divisor[:, None]).astype(jnp.bfloat16)
    coarse_values = (value_sum / divisor[:, None]).astype(jnp.bfloat16)
    attended_grad = jnp.dot(grad_out, out_weight, preferred_element_type=jnp.float32).astype(jnp.bfloat16)

    def one_head(pieces):
        return head_pass(pieces[0], pieces[1], pieces[2], pieces[3], pieces[4], pieces[5], counts)
    outputs = lax.map(one_head, (by_head(query_rows), by_head(key_rows), by_head(value_rows), by_head(attended_grad), by_head(coarse_keys), by_head(coarse_values)))
    attended = join_heads(outputs[0]).astype(jnp.bfloat16)
    query_grad = join_heads(outputs[1]).astype(jnp.bfloat16)
    spread = pooled_row.astype(jnp.float32)[:, None]
    key_extra = jnp.repeat(join_heads(outputs[4]) / divisor[:, None], BLOCK, axis=0) * spread
    value_extra = jnp.repeat(join_heads(outputs[5]) / divisor[:, None], BLOCK, axis=0) * spread
    key_grad = (join_heads(outputs[2]) + key_extra).astype(jnp.bfloat16)
    value_grad = (join_heads(outputs[3]) + value_extra).astype(jnp.bfloat16)
    weight_term = jnp.dot(grad_out.T, attended, preferred_element_type=jnp.float32)
    return (query_grad, key_grad, value_grad, weight_term)

def reference(queries, keys, values, out_weight, out_grad, pooled):

    def one_stream(operands):
        return stream_pass(operands, out_weight)
    query_grad, key_grad, value_grad, weight_terms = lax.map(one_stream, (queries, keys, values, out_grad, pooled))
    weight_grad = lax.optimization_barrier(jnp.sum(weight_terms, axis=0)) / math.sqrt(SEQ)
    return (query_grad, key_grad, value_grad, weight_grad)
```

```python
import math

import jax
import jax.numpy as jnp
from jax import lax
from jax.sharding import PartitionSpec as P

HEADS = 16
HEAD_DIM = 64
BLOCK = 128


def padded_2(block, sides, width):
    for axis, dim in sides:
        count = lax.axis_size(axis)
        forward = [(i, i + 1) for i in range(count - 1)]
        backward = [(target, source) for source, target in forward]
        low = lax.ppermute(
            lax.slice_in_dim(block, block.shape[dim] - width, None, axis=dim), axis, forward
        )
        high = lax.ppermute(lax.slice_in_dim(block, 0, width, axis=dim), axis, backward)
        block = jnp.concatenate([low, block, high], axis=dim)
    return block


def from_behind(value, axis, steps):
    count = lax.axis_size(axis)
    leading, last = (max(0, -steps), min(count, count - steps))
    return lax.ppermute(value, axis, [(source, source + steps) for source in range(leading, last)])


def xor_pairs(count, bit):
    return [(source, source ^ (1 << bit)) for source in range(count)]


def own_bit(axis, bit):
    return (lax.axis_index(axis) // (1 << bit)) % 2


def doubling_gather(piece, axis):
    count = lax.axis_size(axis)
    bits = count.bit_length() - 1
    held = piece
    for done, bit in enumerate(reversed(range(bits))):
        other = lax.ppermute(held, axis, xor_pairs(count, bit))
        mine_low = own_bit(axis, bit) == 0
        low = jnp.where(mine_low, held, other)
        high = jnp.where(mine_low, other, held)
        held = jnp.stack([low, high], axis=done)
    return held.reshape((count,) + piece.shape)


def halving_scatter(stack, axis):
    count = lax.axis_size(axis)
    bits = count.bit_length() - 1
    held = stack.reshape((2,) * bits + stack.shape[1:])
    for bit in range(bits):
        dim = bits - 1 - bit
        mine = own_bit(axis, bit)
        keep = lax.dynamic_index_in_dim(held, mine, dim, keepdims=False)
        send = lax.dynamic_index_in_dim(held, 1 - mine, dim, keepdims=False)
        held = keep + lax.ppermute(send, axis, xor_pairs(count, bit))
    return held


def block_windows(padded, local_blocks):
    return jnp.concatenate(
        [padded[0:local_blocks], padded[1 : local_blocks + 1], padded[2 : local_blocks + 2]], axis=1
    )


def fold_windows(grads, local_blocks):
    parts = grads.reshape((local_blocks, 3, BLOCK) + grads.shape[2:])
    edge_zero = jnp.zeros((1,) + parts.shape[2:], jnp.float32)
    left_part = jnp.concatenate([parts[:, 0], edge_zero, edge_zero], axis=0)
    middle = jnp.concatenate([edge_zero, parts[:, 1], edge_zero], axis=0)
    right_part = jnp.concatenate([edge_zero, edge_zero, parts[:, 2]], axis=0)
    return left_part + middle + right_part


def per_device(queries, keys, values, out_weight, out_grad, pooled):
    query_rows = queries[0]
    key_rows = keys[0]
    value_rows = values[0]
    grad_out = out_grad[0]
    tokens, model_width = query_rows.shape
    local_blocks = tokens // BLOCK
    seq_devices = lax.axis_size("seq")
    seq_index = lax.axis_index("seq")
    all_blocks = local_blocks * seq_devices
    score_scale = 1.0 / math.sqrt(HEAD_DIM)
    pooled_mask = pooled[0].reshape(local_blocks, BLOCK).astype(jnp.float32)
    counts = jnp.sum(pooled_mask, axis=1)
    divisor = jnp.maximum(counts, 1.0)
    pooled_bf = pooled_mask.astype(jnp.bfloat16)
    key_sum = jnp.einsum(
        "nb,nbd->nd",
        pooled_bf,
        key_rows.reshape(local_blocks, BLOCK, model_width),
        preferred_element_type=jnp.float32,
    )
    value_sum = jnp.einsum(
        "nb,nbd->nd",
        pooled_bf,
        value_rows.reshape(local_blocks, BLOCK, model_width),
        preferred_element_type=jnp.float32,
    )
    coarse_keys = (key_sum / divisor[:, None]).astype(jnp.bfloat16)
    coarse_values = (value_sum / divisor[:, None]).astype(jnp.bfloat16)
    count_cols = jnp.broadcast_to(counts.astype(jnp.bfloat16)[:, None], (local_blocks, 128))
    packed = jnp.concatenate([coarse_keys, coarse_values, count_cols], axis=1)
    gathered = doubling_gather(packed, "seq").reshape(all_blocks, packed.shape[1])
    gathered_keys = gathered[:, :model_width]
    gathered_values = gathered[:, model_width : 2 * model_width]
    gathered_counts = gathered[:, 2 * model_width].astype(jnp.float32)
    paired = jnp.stack([key_rows, value_rows])
    extended = padded_2(paired, (("seq", 1),), BLOCK)
    padded_kv = extended.reshape(2, local_blocks + 2, BLOCK, HEADS, HEAD_DIM)
    key_win = block_windows(padded_kv[0], local_blocks)
    value_win = block_windows(padded_kv[1], local_blocks)
    query_blk = query_rows.reshape(local_blocks, BLOCK, HEADS, HEAD_DIM)
    coarse_kh = gathered_keys.reshape(all_blocks, HEADS, HEAD_DIM)
    coarse_vh = gathered_values.reshape(all_blocks, HEADS, HEAD_DIM)
    local_ids = seq_index * local_blocks + jnp.arange(local_blocks)
    offsets = jnp.repeat(jnp.arange(3) - 1, BLOCK)
    key_blocks = local_ids[:, None] + offsets[None, :]
    fine_ok = (key_blocks >= 0) & (key_blocks < all_blocks)
    far_ok = jnp.abs(local_ids[:, None] - jnp.arange(all_blocks)[None, :]) >= 2
    fine_s = (
        jnp.einsum("nqhe,nkhe->nhqk", query_blk, key_win, preferred_element_type=jnp.float32)
        * score_scale
    )
    coarse_s = (
        jnp.einsum("nqhe,che->nhqc", query_blk, coarse_kh, preferred_element_type=jnp.float32)
        * score_scale
    )
    fine_s = jnp.where(fine_ok[:, None, None, :], fine_s, -jnp.inf)
    coarse_s = jnp.where(far_ok[:, None, None, :], coarse_s, -jnp.inf)
    row_top = jnp.maximum(jnp.max(fine_s, axis=-1), jnp.max(coarse_s, axis=-1))[..., None]
    fine_e = jnp.exp(fine_s - row_top)
    coarse_e = gathered_counts * jnp.exp(coarse_s - row_top)
    row_total = jnp.sum(fine_e, axis=-1, keepdims=True) + jnp.sum(coarse_e, axis=-1, keepdims=True)
    fine_w = fine_e / row_total
    coarse_w = coarse_e / row_total
    fine_wb = fine_w.astype(jnp.bfloat16)
    coarse_wb = coarse_w.astype(jnp.bfloat16)
    attended = (
        jnp.einsum("nhqk,nkhe->nqhe", fine_wb, value_win, preferred_element_type=jnp.float32)
        + jnp.einsum("nhqc,che->nqhe", coarse_wb, coarse_vh, preferred_element_type=jnp.float32)
    ).astype(jnp.bfloat16)
    attended_rows = attended.reshape(tokens, model_width)
    attended_grad = jnp.dot(grad_out, out_weight, preferred_element_type=jnp.float32).astype(
        jnp.bfloat16
    )
    grad_norm = 1.0 / math.sqrt(seq_devices * tokens)
    full_term = (
        jnp.einsum("to,ti->oi", grad_out, attended_rows, preferred_element_type=jnp.float32)
        * grad_norm
    )
    seq_part = lax.psum_scatter(full_term, "seq", scatter_dimension=0, tiled=True)
    full_term, attended_grad = lax.optimization_barrier((full_term, attended_grad))
    grad_blk = attended_grad.reshape(local_blocks, BLOCK, HEADS, HEAD_DIM)
    fine_dot = jnp.einsum(
        "nqhe,nkhe->nhqk", grad_blk, value_win, preferred_element_type=jnp.float32
    )
    coarse_dot = jnp.einsum(
        "nqhe,che->nhqc", grad_blk, coarse_vh, preferred_element_type=jnp.float32
    )
    delta_rows = jnp.einsum(
        "nqhe,nqhe->nhq", grad_blk, attended, preferred_element_type=jnp.float32
    )[..., None]
    fine_ds = (fine_w * (fine_dot - delta_rows)).astype(jnp.bfloat16)
    coarse_ds = (coarse_w * (coarse_dot - delta_rows)).astype(jnp.bfloat16)
    query_grad = (
        jnp.einsum("nhqk,nkhe->nqhe", fine_ds, key_win, preferred_element_type=jnp.float32)
        + jnp.einsum("nhqc,che->nqhe", coarse_ds, coarse_kh, preferred_element_type=jnp.float32)
    ) * score_scale
    query_grad = query_grad.astype(jnp.bfloat16).reshape(1, tokens, model_width)
    key_win_grad = (
        jnp.einsum("nhqk,nqhe->nkhe", fine_ds, query_blk, preferred_element_type=jnp.float32)
        * score_scale
    )
    value_win_grad = jnp.einsum(
        "nhqk,nqhe->nkhe", fine_wb, grad_blk, preferred_element_type=jnp.float32
    )
    key_ext = fold_windows(key_win_grad, local_blocks).reshape(local_blocks + 2, BLOCK, model_width)
    value_ext = fold_windows(value_win_grad, local_blocks).reshape(
        local_blocks + 2, BLOCK, model_width
    )
    edge_first = jnp.stack([key_ext[0], value_ext[0]])
    edge_last = jnp.stack([key_ext[local_blocks + 1], value_ext[local_blocks + 1]])
    from_right = from_behind(edge_first, "seq", -1)
    from_left = from_behind(edge_last, "seq", 1)
    zeros_mid = jnp.zeros((2, local_blocks - 1, BLOCK, model_width), jnp.float32)
    boundary = jnp.concatenate([from_left[:, None], zeros_mid], axis=1) + jnp.concatenate(
        [zeros_mid, from_right[:, None]], axis=1
    )
    coarse_key_all = (
        jnp.einsum("nhqc,nqhe->che", coarse_ds, query_blk, preferred_element_type=jnp.float32)
        * score_scale
    )
    coarse_value_all = jnp.einsum(
        "nhqc,nqhe->che", coarse_wb, grad_blk, preferred_element_type=jnp.float32
    )
    coarse_all = jnp.concatenate(
        [
            coarse_key_all.reshape(all_blocks, model_width),
            coarse_value_all.reshape(all_blocks, model_width),
        ],
        axis=1,
    )
    owned_grads = halving_scatter(
        coarse_all.reshape(seq_devices, local_blocks, 2 * model_width), "seq"
    )
    owned_keys = owned_grads[:, :model_width] / divisor[:, None]
    owned_values = owned_grads[:, model_width:] / divisor[:, None]
    spread_keys = owned_keys[:, None, :] * pooled_mask[:, :, None]
    spread_values = owned_values[:, None, :] * pooled_mask[:, :, None]
    key_grad = (
        (key_ext[1 : local_blocks + 1] + boundary[0] + spread_keys)
        .astype(jnp.bfloat16)
        .reshape(1, tokens, model_width)
    )
    value_grad = (
        (value_ext[1 : local_blocks + 1] + boundary[1] + spread_values)
        .astype(jnp.bfloat16)
        .reshape(1, tokens, model_width)
    )
    weight_grad = lax.psum(seq_part, "dp")
    return (query_grad, key_grad, value_grad, weight_grad)


def solution(mesh):
    placed = (
        P("dp", "seq", None),
        P("dp", "seq", None),
        P("dp", "seq", None),
        P(),
        P("dp", "seq", None),
        P("dp", "seq"),
    )
    return jax.shard_map(
        per_device,
        mesh=mesh,
        in_specs=placed,
        out_specs=(
            P("dp", "seq", None),
            P("dp", "seq", None),
            P("dp", "seq", None),
            P("seq", None),
        ),
        check_vma=False,
    )
```

```python
import math

import jax
import jax.numpy as jnp
from jax import lax
from jax.sharding import PartitionSpec as P

HEADS = 16
HEAD_DIM = 64
BLOCK = 128


def padded_2(block, sides, width):
    for axis, dim in sides:
        count = lax.axis_size(axis)
        forward = [(i, i + 1) for i in range(count - 1)]
        backward = [(target, source) for source, target in forward]
        low = lax.ppermute(
            lax.slice_in_dim(block, block.shape[dim] - width, None, axis=dim), axis, forward
        )
        high = lax.ppermute(lax.slice_in_dim(block, 0, width, axis=dim), axis, backward)
        block = jnp.concatenate([low, block, high], axis=dim)
    return block


def from_behind(value, axis, steps):
    count = lax.axis_size(axis)
    leading, last = (max(0, -steps), min(count, count - steps))
    return lax.ppermute(value, axis, [(source, source + steps) for source in range(leading, last)])


def xor_pairs(count, bit):
    return [(source, source ^ (1 << bit)) for source in range(count)]


def own_bit(axis, bit):
    return (lax.axis_index(axis) // (1 << bit)) % 2


def doubling_gather(piece, axis):
    count = lax.axis_size(axis)
    bits = count.bit_length() - 1
    held = piece
    for done, bit in enumerate(reversed(range(bits))):
        other = lax.ppermute(held, axis, xor_pairs(count, bit))
        mine_low = own_bit(axis, bit) == 0
        low = jnp.where(mine_low, held, other)
        high = jnp.where(mine_low, other, held)
        held = jnp.stack([low, high], axis=done)
    return held.reshape((count,) + piece.shape)


def halving_scatter(stack, axis):
    count = lax.axis_size(axis)
    bits = count.bit_length() - 1
    held = stack.reshape((2,) * bits + stack.shape[1:])
    for bit in range(bits):
        dim = bits - 1 - bit
        mine = own_bit(axis, bit)
        keep = lax.dynamic_index_in_dim(held, mine, dim, keepdims=False)
        send = lax.dynamic_index_in_dim(held, 1 - mine, dim, keepdims=False)
        held = keep + lax.ppermute(send, axis, xor_pairs(count, bit))
    return held


def doubling_sum(value, axis):
    count = lax.axis_size(axis)
    for bit in range(count.bit_length() - 1):
        value = value + lax.ppermute(value, axis, xor_pairs(count, bit))
    return value


def block_windows(padded, local_blocks):
    return jnp.concatenate(
        [padded[0:local_blocks], padded[1 : local_blocks + 1], padded[2 : local_blocks + 2]], axis=1
    )


def fold_windows(grads, local_blocks):
    parts = grads.reshape((local_blocks, 3, BLOCK) + grads.shape[2:])
    edge_zero = jnp.zeros((1,) + parts.shape[2:], jnp.float32)
    left_part = jnp.concatenate([parts[:, 0], edge_zero, edge_zero], axis=0)
    middle = jnp.concatenate([edge_zero, parts[:, 1], edge_zero], axis=0)
    right_part = jnp.concatenate([edge_zero, edge_zero, parts[:, 2]], axis=0)
    return left_part + middle + right_part


def per_device(queries, keys, values, out_weight, out_grad, pooled):
    query_rows = queries[0]
    key_rows = keys[0]
    value_rows = values[0]
    grad_out = out_grad[0]
    tokens, model_width = query_rows.shape
    local_blocks = tokens // BLOCK
    seq_devices = lax.axis_size("seq")
    seq_index = lax.axis_index("seq")
    all_blocks = local_blocks * seq_devices
    score_scale = 1.0 / math.sqrt(HEAD_DIM)
    pooled_mask = pooled[0].reshape(local_blocks, BLOCK).astype(jnp.float32)
    counts = jnp.sum(pooled_mask, axis=1)
    divisor = jnp.maximum(counts, 1.0)
    pooled_bf = pooled_mask.astype(jnp.bfloat16)
    key_sum = jnp.einsum(
        "nb,nbd->nd",
        pooled_bf,
        key_rows.reshape(local_blocks, BLOCK, model_width),
        preferred_element_type=jnp.float32,
    )
    value_sum = jnp.einsum(
        "nb,nbd->nd",
        pooled_bf,
        value_rows.reshape(local_blocks, BLOCK, model_width),
        preferred_element_type=jnp.float32,
    )
    coarse_keys = (key_sum / divisor[:, None]).astype(jnp.bfloat16)
    coarse_values = (value_sum / divisor[:, None]).astype(jnp.bfloat16)
    count_cols = jnp.broadcast_to(counts.astype(jnp.bfloat16)[:, None], (local_blocks, 128))
    packed = jnp.concatenate([coarse_keys, coarse_values, count_cols], axis=1)
    gathered = doubling_gather(packed, "seq").reshape(all_blocks, packed.shape[1])
    gathered_keys = gathered[:, :model_width]
    gathered_values = gathered[:, model_width : 2 * model_width]
    gathered_counts = gathered[:, 2 * model_width].astype(jnp.float32)
    paired = jnp.stack([key_rows, value_rows])
    extended = padded_2(paired, (("seq", 1),), BLOCK)
    padded_kv = extended.reshape(2, local_blocks + 2, BLOCK, HEADS, HEAD_DIM)
    key_win = block_windows(padded_kv[0], local_blocks)
    value_win = block_windows(padded_kv[1], local_blocks)
    query_blk = query_rows.reshape(local_blocks, BLOCK, HEADS, HEAD_DIM)
    coarse_kh = gathered_keys.reshape(all_blocks, HEADS, HEAD_DIM)
    coarse_vh = gathered_values.reshape(all_blocks, HEADS, HEAD_DIM)
    local_ids = seq_index * local_blocks + jnp.arange(local_blocks)
    offsets = jnp.repeat(jnp.arange(3) - 1, BLOCK)
    key_blocks = local_ids[:, None] + offsets[None, :]
    fine_ok = (key_blocks >= 0) & (key_blocks < all_blocks)
    far_ok = jnp.abs(local_ids[:, None] - jnp.arange(all_blocks)[None, :]) >= 2
    fine_s = (
        jnp.einsum("nqhe,nkhe->nhqk", query_blk, key_win, preferred_element_type=jnp.float32)
        * score_scale
    )
    coarse_s = (
        jnp.einsum("nqhe,che->nhqc", query_blk, coarse_kh, preferred_element_type=jnp.float32)
        * score_scale
    )
    fine_s = jnp.where(fine_ok[:, None, None, :], fine_s, -jnp.inf)
    coarse_s = jnp.where(far_ok[:, None, None, :], coarse_s, -jnp.inf)
    row_top = jnp.maximum(jnp.max(fine_s, axis=-1), jnp.max(coarse_s, axis=-1))[..., None]
    fine_e = jnp.exp(fine_s - row_top)
    coarse_e = gathered_counts * jnp.exp(coarse_s - row_top)
    row_total = jnp.sum(fine_e, axis=-1, keepdims=True) + jnp.sum(coarse_e, axis=-1, keepdims=True)
    fine_w = fine_e / row_total
    coarse_w = coarse_e / row_total
    fine_wb = fine_w.astype(jnp.bfloat16)
    coarse_wb = coarse_w.astype(jnp.bfloat16)
    attended = (
        jnp.einsum("nhqk,nkhe->nqhe", fine_wb, value_win, preferred_element_type=jnp.float32)
        + jnp.einsum("nhqc,che->nqhe", coarse_wb, coarse_vh, preferred_element_type=jnp.float32)
    ).astype(jnp.bfloat16)
    attended_rows = attended.reshape(tokens, model_width)
    attended_grad = jnp.dot(grad_out, out_weight, preferred_element_type=jnp.float32).astype(
        jnp.bfloat16
    )
    grad_norm = 1.0 / math.sqrt(seq_devices * tokens)
    full_term = (
        jnp.einsum("to,ti->oi", grad_out, attended_rows, preferred_element_type=jnp.float32)
        * grad_norm
    )
    seq_part = lax.psum_scatter(full_term, "seq", scatter_dimension=0, tiled=True)
    full_term, attended_grad = lax.optimization_barrier((full_term, attended_grad))
    grad_blk = attended_grad.reshape(local_blocks, BLOCK, HEADS, HEAD_DIM)
    fine_dot = jnp.einsum(
        "nqhe,nkhe->nhqk", grad_blk, value_win, preferred_element_type=jnp.float32
    )
    coarse_dot = jnp.einsum(
        "nqhe,che->nhqc", grad_blk, coarse_vh, preferred_element_type=jnp.float32
    )
    delta_rows = jnp.einsum(
        "nqhe,nqhe->nhq", grad_blk, attended, preferred_element_type=jnp.float32
    )[..., None]
    fine_ds = (fine_w * (fine_dot - delta_rows)).astype(jnp.bfloat16)
    coarse_ds = (coarse_w * (coarse_dot - delta_rows)).astype(jnp.bfloat16)
    query_grad = (
        jnp.einsum("nhqk,nkhe->nqhe", fine_ds, key_win, preferred_element_type=jnp.float32)
        + jnp.einsum("nhqc,che->nqhe", coarse_ds, coarse_kh, preferred_element_type=jnp.float32)
    ) * score_scale
    query_grad = query_grad.astype(jnp.bfloat16).reshape(1, tokens, model_width)
    key_win_grad = (
        jnp.einsum("nhqk,nqhe->nkhe", fine_ds, query_blk, preferred_element_type=jnp.float32)
        * score_scale
    )
    value_win_grad = jnp.einsum(
        "nhqk,nqhe->nkhe", fine_wb, grad_blk, preferred_element_type=jnp.float32
    )
    key_ext = fold_windows(key_win_grad, local_blocks).reshape(local_blocks + 2, BLOCK, model_width)
    value_ext = fold_windows(value_win_grad, local_blocks).reshape(
        local_blocks + 2, BLOCK, model_width
    )
    edge_first = jnp.stack([key_ext[0], value_ext[0]])
    edge_last = jnp.stack([key_ext[local_blocks + 1], value_ext[local_blocks + 1]])
    from_right = from_behind(edge_first, "seq", -1)
    from_left = from_behind(edge_last, "seq", 1)
    zeros_mid = jnp.zeros((2, local_blocks - 1, BLOCK, model_width), jnp.float32)
    boundary = jnp.concatenate([from_left[:, None], zeros_mid], axis=1) + jnp.concatenate(
        [zeros_mid, from_right[:, None]], axis=1
    )
    coarse_key_all = (
        jnp.einsum("nhqc,nqhe->che", coarse_ds, query_blk, preferred_element_type=jnp.float32)
        * score_scale
    )
    coarse_value_all = jnp.einsum(
        "nhqc,nqhe->che", coarse_wb, grad_blk, preferred_element_type=jnp.float32
    )
    coarse_all = jnp.concatenate(
        [
            coarse_key_all.reshape(all_blocks, model_width),
            coarse_value_all.reshape(all_blocks, model_width),
        ],
        axis=1,
    )
    owned_grads = halving_scatter(
        coarse_all.reshape(seq_devices, local_blocks, 2 * model_width), "seq"
    )
    owned_keys = owned_grads[:, :model_width] / divisor[:, None]
    owned_values = owned_grads[:, model_width:] / divisor[:, None]
    spread_keys = owned_keys[:, None, :] * pooled_mask[:, :, None]
    spread_values = owned_values[:, None, :] * pooled_mask[:, :, None]
    key_grad = (
        (key_ext[1 : local_blocks + 1] + boundary[0] + spread_keys)
        .astype(jnp.bfloat16)
        .reshape(1, tokens, model_width)
    )
    value_grad = (
        (value_ext[1 : local_blocks + 1] + boundary[1] + spread_values)
        .astype(jnp.bfloat16)
        .reshape(1, tokens, model_width)
    )
    weight_grad = doubling_sum(seq_part, "dp")
    return (query_grad, key_grad, value_grad, weight_grad)


def solution(mesh):
    placed = (
        P("dp", "seq", None),
        P("dp", "seq", None),
        P("dp", "seq", None),
        P(),
        P("dp", "seq", None),
        P("dp", "seq"),
    )
    return jax.shard_map(
        per_device,
        mesh=mesh,
        in_specs=placed,
        out_specs=(
            P("dp", "seq", None),
            P("dp", "seq", None),
            P("dp", "seq", None),
            P("seq", None),
        ),
        check_vma=False,
    )
```

```python
import math

import jax
import jax.numpy as jnp
from jax import lax
from jax.sharding import PartitionSpec as P

HEADS = 16
HEAD_DIM = 64
BLOCK = 128


def padded_2(block, sides, width):
    for axis, dim in sides:
        count = lax.axis_size(axis)
        forward = [(i, i + 1) for i in range(count - 1)]
        backward = [(target, source) for source, target in forward]
        low = lax.ppermute(
            lax.slice_in_dim(block, block.shape[dim] - width, None, axis=dim), axis, forward
        )
        high = lax.ppermute(lax.slice_in_dim(block, 0, width, axis=dim), axis, backward)
        block = jnp.concatenate([low, block, high], axis=dim)
    return block


def from_behind(value, axis, steps):
    count = lax.axis_size(axis)
    leading, last = (max(0, -steps), min(count, count - steps))
    return lax.ppermute(value, axis, [(source, source + steps) for source in range(leading, last)])


def xor_pairs(count, bit):
    return [(source, source ^ (1 << bit)) for source in range(count)]


def own_bit(axis, bit):
    return (lax.axis_index(axis) // (1 << bit)) % 2


def doubling_gather(piece, axis):
    count = lax.axis_size(axis)
    bits = count.bit_length() - 1
    held = piece
    for done, bit in enumerate(reversed(range(bits))):
        other = lax.ppermute(held, axis, xor_pairs(count, bit))
        mine_low = own_bit(axis, bit) == 0
        low = jnp.where(mine_low, held, other)
        high = jnp.where(mine_low, other, held)
        held = jnp.stack([low, high], axis=done)
    return held.reshape((count,) + piece.shape)


def halving_scatter(stack, axis):
    count = lax.axis_size(axis)
    bits = count.bit_length() - 1
    held = stack.reshape((2,) * bits + stack.shape[1:])
    for bit in range(bits):
        dim = bits - 1 - bit
        mine = own_bit(axis, bit)
        keep = lax.dynamic_index_in_dim(held, mine, dim, keepdims=False)
        send = lax.dynamic_index_in_dim(held, 1 - mine, dim, keepdims=False)
        held = keep + lax.ppermute(send, axis, xor_pairs(count, bit))
    return held


def doubling_sum(value, axis):
    count = lax.axis_size(axis)
    for bit in range(count.bit_length() - 1):
        value = value + lax.ppermute(value, axis, xor_pairs(count, bit))
    return value


def shift_pairs(count, shift):
    return [(source, (source + shift) % count) for source in range(count)]


def spread_gather(piece, axis):
    count = lax.axis_size(axis)
    me = lax.axis_index(axis)
    arrived = [piece] + [
        lax.ppermute(piece, axis, shift_pairs(count, shift)) for shift in range(1, count)
    ]
    by_shift = jnp.stack(arrived)
    return jnp.take(by_shift, (me - jnp.arange(count)) % count, axis=0)


def spread_scatter(stack, axis):
    count = lax.axis_size(axis)
    me = lax.axis_index(axis)
    total = lax.dynamic_index_in_dim(stack, me, 0, keepdims=False)
    for shift in range(1, count):
        send = lax.dynamic_index_in_dim(stack, (me + shift) % count, 0, keepdims=False)
        total = total + lax.ppermute(send, axis, shift_pairs(count, shift))
    return total


def block_windows(padded, local_blocks):
    return jnp.concatenate(
        [padded[0:local_blocks], padded[1 : local_blocks + 1], padded[2 : local_blocks + 2]], axis=1
    )


def fold_windows(grads, local_blocks):
    parts = grads.reshape((local_blocks, 3, BLOCK) + grads.shape[2:])
    edge_zero = jnp.zeros((1,) + parts.shape[2:], jnp.float32)
    left_part = jnp.concatenate([parts[:, 0], edge_zero, edge_zero], axis=0)
    middle = jnp.concatenate([edge_zero, parts[:, 1], edge_zero], axis=0)
    right_part = jnp.concatenate([edge_zero, edge_zero, parts[:, 2]], axis=0)
    return left_part + middle + right_part


def per_device(queries, keys, values, out_weight, out_grad, pooled):
    query_rows = queries[0]
    key_rows = keys[0]
    value_rows = values[0]
    grad_out = out_grad[0]
    tokens, model_width = query_rows.shape
    local_blocks = tokens // BLOCK
    seq_devices = lax.axis_size("seq")
    seq_index = lax.axis_index("seq")
    all_blocks = local_blocks * seq_devices
    score_scale = 1.0 / math.sqrt(HEAD_DIM)
    pooled_mask = pooled[0].reshape(local_blocks, BLOCK).astype(jnp.float32)
    counts = jnp.sum(pooled_mask, axis=1)
    divisor = jnp.maximum(counts, 1.0)
    pooled_bf = pooled_mask.astype(jnp.bfloat16)
    key_sum = jnp.einsum(
        "nb,nbd->nd",
        pooled_bf,
        key_rows.reshape(local_blocks, BLOCK, model_width),
        preferred_element_type=jnp.float32,
    )
    value_sum = jnp.einsum(
        "nb,nbd->nd",
        pooled_bf,
        value_rows.reshape(local_blocks, BLOCK, model_width),
        preferred_element_type=jnp.float32,
    )
    coarse_keys = (key_sum / divisor[:, None]).astype(jnp.bfloat16)
    coarse_values = (value_sum / divisor[:, None]).astype(jnp.bfloat16)
    count_cols = jnp.broadcast_to(counts.astype(jnp.bfloat16)[:, None], (local_blocks, 128))
    packed = jnp.concatenate([coarse_keys, coarse_values, count_cols], axis=1)
    gathered = spread_gather(packed, "seq").reshape(all_blocks, packed.shape[1])
    gathered_keys = gathered[:, :model_width]
    gathered_values = gathered[:, model_width : 2 * model_width]
    gathered_counts = gathered[:, 2 * model_width].astype(jnp.float32)
    paired = jnp.stack([key_rows, value_rows])
    extended = padded_2(paired, (("seq", 1),), BLOCK)
    padded_kv = extended.reshape(2, local_blocks + 2, BLOCK, HEADS, HEAD_DIM)
    key_win = block_windows(padded_kv[0], local_blocks)
    value_win = block_windows(padded_kv[1], local_blocks)
    query_blk = query_rows.reshape(local_blocks, BLOCK, HEADS, HEAD_DIM)
    coarse_kh = gathered_keys.reshape(all_blocks, HEADS, HEAD_DIM)
    coarse_vh = gathered_values.reshape(all_blocks, HEADS, HEAD_DIM)
    local_ids = seq_index * local_blocks + jnp.arange(local_blocks)
    offsets = jnp.repeat(jnp.arange(3) - 1, BLOCK)
    key_blocks = local_ids[:, None] + offsets[None, :]
    fine_ok = (key_blocks >= 0) & (key_blocks < all_blocks)
    far_ok = jnp.abs(local_ids[:, None] - jnp.arange(all_blocks)[None, :]) >= 2
    fine_s = (
        jnp.einsum("nqhe,nkhe->nhqk", query_blk, key_win, preferred_element_type=jnp.float32)
        * score_scale
    )
    coarse_s = (
        jnp.einsum("nqhe,che->nhqc", query_blk, coarse_kh, preferred_element_type=jnp.float32)
        * score_scale
    )
    fine_s = jnp.where(fine_ok[:, None, None, :], fine_s, -jnp.inf)
    coarse_s = jnp.where(far_ok[:, None, None, :], coarse_s, -jnp.inf)
    row_top = jnp.maximum(jnp.max(fine_s, axis=-1), jnp.max(coarse_s, axis=-1))[..., None]
    fine_e = jnp.exp(fine_s - row_top)
    coarse_e = gathered_counts * jnp.exp(coarse_s - row_top)
    row_total = jnp.sum(fine_e, axis=-1, keepdims=True) + jnp.sum(coarse_e, axis=-1, keepdims=True)
    fine_w = fine_e / row_total
    coarse_w = coarse_e / row_total
    fine_wb = fine_w.astype(jnp.bfloat16)
    coarse_wb = coarse_w.astype(jnp.bfloat16)
    attended = (
        jnp.einsum("nhqk,nkhe->nqhe", fine_wb, value_win, preferred_element_type=jnp.float32)
        + jnp.einsum("nhqc,che->nqhe", coarse_wb, coarse_vh, preferred_element_type=jnp.float32)
    ).astype(jnp.bfloat16)
    attended_rows = attended.reshape(tokens, model_width)
    attended_grad = jnp.dot(grad_out, out_weight, preferred_element_type=jnp.float32).astype(
        jnp.bfloat16
    )
    grad_norm = 1.0 / math.sqrt(seq_devices * tokens)
    full_term = (
        jnp.einsum("to,ti->oi", grad_out, attended_rows, preferred_element_type=jnp.float32)
        * grad_norm
    )
    piece_rows = model_width // seq_devices
    seq_part = lax.psum_scatter(full_term, "seq", scatter_dimension=0, tiled=True)
    full_term, attended_grad = lax.optimization_barrier((full_term, attended_grad))
    grad_blk = attended_grad.reshape(local_blocks, BLOCK, HEADS, HEAD_DIM)
    fine_dot = jnp.einsum(
        "nqhe,nkhe->nhqk", grad_blk, value_win, preferred_element_type=jnp.float32
    )
    coarse_dot = jnp.einsum(
        "nqhe,che->nhqc", grad_blk, coarse_vh, preferred_element_type=jnp.float32
    )
    delta_rows = jnp.einsum(
        "nqhe,nqhe->nhq", grad_blk, attended, preferred_element_type=jnp.float32
    )[..., None]
    fine_ds = (fine_w * (fine_dot - delta_rows)).astype(jnp.bfloat16)
    coarse_ds = (coarse_w * (coarse_dot - delta_rows)).astype(jnp.bfloat16)
    query_grad = (
        jnp.einsum("nhqk,nkhe->nqhe", fine_ds, key_win, preferred_element_type=jnp.float32)
        + jnp.einsum("nhqc,che->nqhe", coarse_ds, coarse_kh, preferred_element_type=jnp.float32)
    ) * score_scale
    query_grad = query_grad.astype(jnp.bfloat16).reshape(1, tokens, model_width)
    key_win_grad = (
        jnp.einsum("nhqk,nqhe->nkhe", fine_ds, query_blk, preferred_element_type=jnp.float32)
        * score_scale
    )
    value_win_grad = jnp.einsum(
        "nhqk,nqhe->nkhe", fine_wb, grad_blk, preferred_element_type=jnp.float32
    )
    key_ext = fold_windows(key_win_grad, local_blocks).reshape(local_blocks + 2, BLOCK, model_width)
    value_ext = fold_windows(value_win_grad, local_blocks).reshape(
        local_blocks + 2, BLOCK, model_width
    )
    edge_first = jnp.stack([key_ext[0], value_ext[0]])
    edge_last = jnp.stack([key_ext[local_blocks + 1], value_ext[local_blocks + 1]])
    from_right = from_behind(edge_first, "seq", -1)
    from_left = from_behind(edge_last, "seq", 1)
    zeros_mid = jnp.zeros((2, local_blocks - 1, BLOCK, model_width), jnp.float32)
    boundary = jnp.concatenate([from_left[:, None], zeros_mid], axis=1) + jnp.concatenate(
        [zeros_mid, from_right[:, None]], axis=1
    )
    coarse_key_all = (
        jnp.einsum("nhqc,nqhe->che", coarse_ds, query_blk, preferred_element_type=jnp.float32)
        * score_scale
    )
    coarse_value_all = jnp.einsum(
        "nhqc,nqhe->che", coarse_wb, grad_blk, preferred_element_type=jnp.float32
    )
    coarse_all = jnp.concatenate(
        [
            coarse_key_all.reshape(all_blocks, model_width),
            coarse_value_all.reshape(all_blocks, model_width),
        ],
        axis=1,
    )
    owned_grads = spread_scatter(
        coarse_all.reshape(seq_devices, local_blocks, 2 * model_width), "seq"
    )
    owned_keys = owned_grads[:, :model_width] / divisor[:, None]
    owned_values = owned_grads[:, model_width:] / divisor[:, None]
    spread_keys = owned_keys[:, None, :] * pooled_mask[:, :, None]
    spread_values = owned_values[:, None, :] * pooled_mask[:, :, None]
    key_grad = (
        (key_ext[1 : local_blocks + 1] + boundary[0] + spread_keys)
        .astype(jnp.bfloat16)
        .reshape(1, tokens, model_width)
    )
    value_grad = (
        (value_ext[1 : local_blocks + 1] + boundary[1] + spread_values)
        .astype(jnp.bfloat16)
        .reshape(1, tokens, model_width)
    )
    dp_devices = lax.axis_size("dp")
    dp_rows = spread_scatter(seq_part.reshape(dp_devices, -1, model_width), "dp")
    weight_grad = spread_gather(dp_rows, "dp").reshape(piece_rows, model_width)
    return (query_grad, key_grad, value_grad, weight_grad)


def solution(mesh):
    placed = (
        P("dp", "seq", None),
        P("dp", "seq", None),
        P("dp", "seq", None),
        P(),
        P("dp", "seq", None),
        P("dp", "seq"),
    )
    return jax.shard_map(
        per_device,
        mesh=mesh,
        in_specs=placed,
        out_specs=(
            P("dp", "seq", None),
            P("dp", "seq", None),
            P("dp", "seq", None),
            P("seq", None),
        ),
        check_vma=False,
    )
```

```python
import math

import jax
import jax.numpy as jnp
from jax import lax
from jax.sharding import PartitionSpec as P

HEADS = 16
HEAD_DIM = 64
BLOCK = 128


def padded_2(block, sides, width):
    for axis, dim in sides:
        count = lax.axis_size(axis)
        forward = [(i, i + 1) for i in range(count - 1)]
        backward = [(target, source) for source, target in forward]
        low = lax.ppermute(
            lax.slice_in_dim(block, block.shape[dim] - width, None, axis=dim), axis, forward
        )
        high = lax.ppermute(lax.slice_in_dim(block, 0, width, axis=dim), axis, backward)
        block = jnp.concatenate([low, block, high], axis=dim)
    return block


def from_behind(value, axis, steps):
    count = lax.axis_size(axis)
    leading, last = (max(0, -steps), min(count, count - steps))
    return lax.ppermute(value, axis, [(source, source + steps) for source in range(leading, last)])


def xor_pairs(count, bit):
    return [(source, source ^ (1 << bit)) for source in range(count)]


def own_bit(axis, bit):
    return (lax.axis_index(axis) // (1 << bit)) % 2


def doubling_gather(piece, axis):
    count = lax.axis_size(axis)
    bits = count.bit_length() - 1
    held = piece
    for done, bit in enumerate(reversed(range(bits))):
        other = lax.ppermute(held, axis, xor_pairs(count, bit))
        mine_low = own_bit(axis, bit) == 0
        low = jnp.where(mine_low, held, other)
        high = jnp.where(mine_low, other, held)
        held = jnp.stack([low, high], axis=done)
    return held.reshape((count,) + piece.shape)


def halving_scatter(stack, axis):
    count = lax.axis_size(axis)
    bits = count.bit_length() - 1
    held = stack.reshape((2,) * bits + stack.shape[1:])
    for bit in range(bits):
        dim = bits - 1 - bit
        mine = own_bit(axis, bit)
        keep = lax.dynamic_index_in_dim(held, mine, dim, keepdims=False)
        send = lax.dynamic_index_in_dim(held, 1 - mine, dim, keepdims=False)
        held = keep + lax.ppermute(send, axis, xor_pairs(count, bit))
    return held


def doubling_sum(value, axis):
    count = lax.axis_size(axis)
    for bit in range(count.bit_length() - 1):
        value = value + lax.ppermute(value, axis, xor_pairs(count, bit))
    return value


def block_windows(padded, local_blocks):
    return jnp.concatenate(
        [padded[0:local_blocks], padded[1 : local_blocks + 1], padded[2 : local_blocks + 2]], axis=1
    )


def fold_windows(grads, local_blocks):
    parts = grads.reshape((local_blocks, 3, BLOCK) + grads.shape[2:])
    edge_zero = jnp.zeros((1,) + parts.shape[2:], jnp.float32)
    left_part = jnp.concatenate([parts[:, 0], edge_zero, edge_zero], axis=0)
    middle = jnp.concatenate([edge_zero, parts[:, 1], edge_zero], axis=0)
    right_part = jnp.concatenate([edge_zero, edge_zero, parts[:, 2]], axis=0)
    return left_part + middle + right_part


def per_device(queries, keys, values, out_weight, out_grad, pooled):
    query_rows = queries[0]
    key_rows = keys[0]
    value_rows = values[0]
    grad_out = out_grad[0]
    tokens, model_width = query_rows.shape
    local_blocks = tokens // BLOCK
    seq_devices = lax.axis_size("seq")
    seq_index = lax.axis_index("seq")
    all_blocks = local_blocks * seq_devices
    score_scale = 1.0 / math.sqrt(HEAD_DIM)
    pooled_mask = pooled[0].reshape(local_blocks, BLOCK).astype(jnp.float32)
    counts = jnp.sum(pooled_mask, axis=1)
    divisor = jnp.maximum(counts, 1.0)
    pooled_bf = pooled_mask.astype(jnp.bfloat16)
    key_sum = jnp.einsum(
        "nb,nbd->nd",
        pooled_bf,
        key_rows.reshape(local_blocks, BLOCK, model_width),
        preferred_element_type=jnp.float32,
    )
    value_sum = jnp.einsum(
        "nb,nbd->nd",
        pooled_bf,
        value_rows.reshape(local_blocks, BLOCK, model_width),
        preferred_element_type=jnp.float32,
    )
    coarse_keys = (key_sum / divisor[:, None]).astype(jnp.bfloat16)
    coarse_values = (value_sum / divisor[:, None]).astype(jnp.bfloat16)
    count_cols = jnp.broadcast_to(counts.astype(jnp.bfloat16)[:, None], (local_blocks, 128))
    packed = jnp.concatenate([coarse_keys, coarse_values, count_cols], axis=1)
    gathered = doubling_gather(packed, "seq").reshape(all_blocks, packed.shape[1])
    gathered_keys = gathered[:, :model_width]
    gathered_values = gathered[:, model_width : 2 * model_width]
    gathered_counts = gathered[:, 2 * model_width].astype(jnp.float32)
    paired = jnp.stack([key_rows, value_rows])
    extended = padded_2(paired, (("seq", 1),), BLOCK)
    padded_kv = extended.reshape(2, local_blocks + 2, BLOCK, HEADS, HEAD_DIM)
    key_win = block_windows(padded_kv[0], local_blocks)
    value_win = block_windows(padded_kv[1], local_blocks)
    query_blk = query_rows.reshape(local_blocks, BLOCK, HEADS, HEAD_DIM)
    coarse_kh = gathered_keys.reshape(all_blocks, HEADS, HEAD_DIM)
    coarse_vh = gathered_values.reshape(all_blocks, HEADS, HEAD_DIM)
    local_ids = seq_index * local_blocks + jnp.arange(local_blocks)
    offsets = jnp.repeat(jnp.arange(3) - 1, BLOCK)
    key_blocks = local_ids[:, None] + offsets[None, :]
    fine_ok = (key_blocks >= 0) & (key_blocks < all_blocks)
    far_ok = jnp.abs(local_ids[:, None] - jnp.arange(all_blocks)[None, :]) >= 2
    fine_s = (
        jnp.einsum("nqhe,nkhe->nhqk", query_blk, key_win, preferred_element_type=jnp.float32)
        * score_scale
    )
    coarse_s = (
        jnp.einsum("nqhe,che->nhqc", query_blk, coarse_kh, preferred_element_type=jnp.float32)
        * score_scale
    )
    fine_s = jnp.where(fine_ok[:, None, None, :], fine_s, -jnp.inf)
    coarse_s = jnp.where(far_ok[:, None, None, :], coarse_s, -jnp.inf)
    row_top = jnp.maximum(jnp.max(fine_s, axis=-1), jnp.max(coarse_s, axis=-1))[..., None]
    fine_e = jnp.exp(fine_s - row_top)
    coarse_e = gathered_counts * jnp.exp(coarse_s - row_top)
    row_total = jnp.sum(fine_e, axis=-1, keepdims=True) + jnp.sum(coarse_e, axis=-1, keepdims=True)
    fine_w = fine_e / row_total
    coarse_w = coarse_e / row_total
    fine_wb = fine_w.astype(jnp.bfloat16)
    coarse_wb = coarse_w.astype(jnp.bfloat16)
    attended = (
        jnp.einsum("nhqk,nkhe->nqhe", fine_wb, value_win, preferred_element_type=jnp.float32)
        + jnp.einsum("nhqc,che->nqhe", coarse_wb, coarse_vh, preferred_element_type=jnp.float32)
    ).astype(jnp.bfloat16)
    attended_rows = attended.reshape(tokens, model_width)
    attended_grad = jnp.dot(grad_out, out_weight, preferred_element_type=jnp.float32).astype(
        jnp.bfloat16
    )
    grad_norm = 1.0 / math.sqrt(seq_devices * tokens)
    full_term = (
        jnp.einsum("to,ti->oi", grad_out, attended_rows, preferred_element_type=jnp.float32)
        * grad_norm
    )
    seq_part = lax.psum_scatter(full_term, "seq", scatter_dimension=0, tiled=True)
    full_term, attended_grad = lax.optimization_barrier((full_term, attended_grad))
    grad_blk = attended_grad.reshape(local_blocks, BLOCK, HEADS, HEAD_DIM)
    fine_dot = jnp.einsum(
        "nqhe,nkhe->nhqk", grad_blk, value_win, preferred_element_type=jnp.float32
    )
    coarse_dot = jnp.einsum(
        "nqhe,che->nhqc", grad_blk, coarse_vh, preferred_element_type=jnp.float32
    )
    delta_rows = jnp.einsum(
        "nqhe,nqhe->nhq", grad_blk, attended, preferred_element_type=jnp.float32
    )[..., None]
    fine_ds = (fine_w * (fine_dot - delta_rows)).astype(jnp.bfloat16)
    coarse_ds = (coarse_w * (coarse_dot - delta_rows)).astype(jnp.bfloat16)
    query_grad = (
        jnp.einsum("nhqk,nkhe->nqhe", fine_ds, key_win, preferred_element_type=jnp.float32)
        + jnp.einsum("nhqc,che->nqhe", coarse_ds, coarse_kh, preferred_element_type=jnp.float32)
    ) * score_scale
    query_grad = query_grad.astype(jnp.bfloat16).reshape(1, tokens, model_width)
    key_win_grad = (
        jnp.einsum("nhqk,nqhe->nkhe", fine_ds, query_blk, preferred_element_type=jnp.float32)
        * score_scale
    )
    value_win_grad = jnp.einsum(
        "nhqk,nqhe->nkhe", fine_wb, grad_blk, preferred_element_type=jnp.float32
    )
    key_ext = fold_windows(key_win_grad, local_blocks).reshape(local_blocks + 2, BLOCK, model_width)
    value_ext = fold_windows(value_win_grad, local_blocks).reshape(
        local_blocks + 2, BLOCK, model_width
    )
    edge_first = jnp.stack([key_ext[0], value_ext[0]])
    edge_last = jnp.stack([key_ext[local_blocks + 1], value_ext[local_blocks + 1]])
    from_right = from_behind(edge_first, "seq", -1)
    from_left = from_behind(edge_last, "seq", 1)
    zeros_mid = jnp.zeros((2, local_blocks - 1, BLOCK, model_width), jnp.float32)
    boundary = jnp.concatenate([from_left[:, None], zeros_mid], axis=1) + jnp.concatenate(
        [zeros_mid, from_right[:, None]], axis=1
    )
    coarse_key_all = (
        jnp.einsum("nhqc,nqhe->che", coarse_ds, query_blk, preferred_element_type=jnp.float32)
        * score_scale
    )
    coarse_value_all = jnp.einsum(
        "nhqc,nqhe->che", coarse_wb, grad_blk, preferred_element_type=jnp.float32
    )
    coarse_all = jnp.concatenate(
        [
            coarse_key_all.reshape(all_blocks, model_width),
            coarse_value_all.reshape(all_blocks, model_width),
        ],
        axis=1,
    )
    owned_grads = halving_scatter(
        coarse_all.reshape(seq_devices, local_blocks, 2 * model_width), "seq"
    )
    owned_keys = owned_grads[:, :model_width] / divisor[:, None]
    owned_values = owned_grads[:, model_width:] / divisor[:, None]
    spread_keys = owned_keys[:, None, :] * pooled_mask[:, :, None]
    spread_values = owned_values[:, None, :] * pooled_mask[:, :, None]
    key_grad = (
        (key_ext[1 : local_blocks + 1] + boundary[0] + spread_keys)
        .astype(jnp.bfloat16)
        .reshape(1, tokens, model_width)
    )
    value_grad = (
        (value_ext[1 : local_blocks + 1] + boundary[1] + spread_values)
        .astype(jnp.bfloat16)
        .reshape(1, tokens, model_width)
    )
    dp_devices = lax.axis_size("dp")
    dp_rows = halving_scatter(seq_part.reshape(dp_devices, -1, model_width), "dp")
    weight_grad = doubling_gather(dp_rows, "dp").reshape(-1, model_width)
    return (query_grad, key_grad, value_grad, weight_grad)


def solution(mesh):
    placed = (
        P("dp", "seq", None),
        P("dp", "seq", None),
        P("dp", "seq", None),
        P(),
        P("dp", "seq", None),
        P("dp", "seq"),
    )
    return jax.shard_map(
        per_device,
        mesh=mesh,
        in_specs=placed,
        out_specs=(
            P("dp", "seq", None),
            P("dp", "seq", None),
            P("dp", "seq", None),
            P("seq", None),
        ),
        check_vma=False,
    )
```

```python
import math

import jax
import jax.numpy as jnp
from jax import lax
from jax.experimental import pallas as pl
from jax.experimental.pallas import tpu as pltpu
from jax.sharding import PartitionSpec as P

HEADS = 16
HEAD_DIM = 64
BLOCK = 128


def padded_2(block, sides, width):
    for axis, dim in sides:
        count = lax.axis_size(axis)
        forward = [(i, i + 1) for i in range(count - 1)]
        backward = [(target, source) for source, target in forward]
        low = lax.ppermute(
            lax.slice_in_dim(block, block.shape[dim] - width, None, axis=dim), axis, forward
        )
        high = lax.ppermute(lax.slice_in_dim(block, 0, width, axis=dim), axis, backward)
        block = jnp.concatenate([low, block, high], axis=dim)
    return block


def from_behind(value, axis, steps):
    count = lax.axis_size(axis)
    leading, last = (max(0, -steps), min(count, count - steps))
    return lax.ppermute(value, axis, [(source, source + steps) for source in range(leading, last)])


def xor_pairs(count, bit):
    return [(source, source ^ (1 << bit)) for source in range(count)]


def own_bit(axis, bit):
    return (lax.axis_index(axis) // (1 << bit)) % 2


def doubling_gather(piece, axis):
    count = lax.axis_size(axis)
    bits = count.bit_length() - 1
    held = piece
    for done, bit in enumerate(reversed(range(bits))):
        other = lax.ppermute(held, axis, xor_pairs(count, bit))
        mine_low = own_bit(axis, bit) == 0
        low = jnp.where(mine_low, held, other)
        high = jnp.where(mine_low, other, held)
        held = jnp.stack([low, high], axis=done)
    return held.reshape((count,) + piece.shape)


def halving_scatter(stack, axis):
    count = lax.axis_size(axis)
    bits = count.bit_length() - 1
    held = stack.reshape((2,) * bits + stack.shape[1:])
    for bit in range(bits):
        dim = bits - 1 - bit
        mine = own_bit(axis, bit)
        keep = lax.dynamic_index_in_dim(held, mine, dim, keepdims=False)
        send = lax.dynamic_index_in_dim(held, 1 - mine, dim, keepdims=False)
        held = keep + lax.ppermute(send, axis, xor_pairs(count, bit))
    return held


def doubling_sum(value, axis):
    count = lax.axis_size(axis)
    for bit in range(count.bit_length() - 1):
        value = value + lax.ppermute(value, axis, xor_pairs(count, bit))
    return value


def forward_kernel(q_ref, k_ref, v_ref, ck_ref, cv_ref, counts_ref, fine_ref, far_ref,
                   att_ref, top_ref, total_ref):
    score_scale = 1.0 / math.sqrt(HEAD_DIM)
    lanes = q_ref.shape[1]
    low_lanes = lax.broadcasted_iota(jnp.int32, (BLOCK, lanes), 1) < HEAD_DIM
    coarse_k = ck_ref[...]
    coarse_v = cv_ref[...]
    counts = counts_ref[...]
    contract_last = (((1,), (1,)), ((), ()))
    for block in range(q_ref.shape[0] // BLOCK):
        query = q_ref[pl.ds(block * BLOCK, BLOCK), :]
        key_win = k_ref[pl.ds(block * BLOCK, 3 * BLOCK), :]
        value_win = v_ref[pl.ds(block * BLOCK, 3 * BLOCK), :]
        fine_ok = fine_ref[pl.ds(block, 1), :] > 0
        far_ok = far_ref[pl.ds(block, 1), :] > 0
        halves = []
        for half in range(2):
            own = low_lanes if half == 0 else jnp.logical_not(low_lanes)
            query_h = jnp.where(own, query, jnp.zeros_like(query))
            fine_s = lax.dot_general(query_h, key_win, contract_last,
                                     preferred_element_type=jnp.float32) * score_scale
            coarse_s = lax.dot_general(query_h, coarse_k, contract_last,
                                       preferred_element_type=jnp.float32) * score_scale
            fine_s = jnp.where(fine_ok, fine_s, -jnp.inf)
            coarse_s = jnp.where(far_ok, coarse_s, -jnp.inf)
            top = jnp.maximum(jnp.max(fine_s, axis=1, keepdims=True),
                              jnp.max(coarse_s, axis=1, keepdims=True))
            fine_e = jnp.exp(fine_s - top)
            coarse_e = counts * jnp.exp(coarse_s - top)
            total = (jnp.sum(fine_e, axis=1, keepdims=True)
                     + jnp.sum(coarse_e, axis=1, keepdims=True))
            fine_w = (fine_e / total).astype(jnp.bfloat16)
            coarse_w = (coarse_e / total).astype(jnp.bfloat16)
            att = (jnp.dot(fine_w, value_win, preferred_element_type=jnp.float32)
                   + jnp.dot(coarse_w, coarse_v, preferred_element_type=jnp.float32))
            halves.append((att, top, total))
        rows = pl.ds(block * BLOCK, BLOCK)
        att_ref[rows, :] = jnp.where(low_lanes, halves[0][0], halves[1][0]).astype(att_ref.dtype)
        top_ref[rows, :] = jnp.where(low_lanes, halves[0][1], halves[1][1])
        total_ref[rows, :] = jnp.where(low_lanes, halves[0][2], halves[1][2])


def attention_forward(query_rows, padded_k, padded_v, coarse_k, coarse_v, counts, fine_ok, far_ok):
    tokens, width = query_rows.shape
    lanes = 2 * HEAD_DIM
    by_pair = lambda rows: pl.BlockSpec((rows, lanes), lambda pair: (0, pair))
    whole = lambda shape: pl.BlockSpec(shape, lambda pair: (0, 0))
    stat = jax.ShapeDtypeStruct((tokens, width), jnp.float32)
    return pl.pallas_call(
        forward_kernel,
        grid=(width // lanes,),
        in_specs=[
            by_pair(tokens),
            by_pair(padded_k.shape[0]),
            by_pair(padded_v.shape[0]),
            by_pair(coarse_k.shape[0]),
            by_pair(coarse_v.shape[0]),
            whole(counts.shape),
            whole(fine_ok.shape),
            whole(far_ok.shape),
        ],
        out_specs=[by_pair(tokens), by_pair(tokens), by_pair(tokens)],
        out_shape=[jax.ShapeDtypeStruct((tokens, width), jnp.bfloat16), stat, stat],
    )(query_rows, padded_k, padded_v, coarse_k, coarse_v, counts, fine_ok, far_ok)


def block_windows(padded, local_blocks):
    return jnp.concatenate(
        [padded[0:local_blocks], padded[1 : local_blocks + 1], padded[2 : local_blocks + 2]], axis=1
    )


def fold_windows(grads, local_blocks):
    parts = grads.reshape((local_blocks, 3, BLOCK) + grads.shape[2:])
    edge_zero = jnp.zeros((1,) + parts.shape[2:], jnp.float32)
    left_part = jnp.concatenate([parts[:, 0], edge_zero, edge_zero], axis=0)
    middle = jnp.concatenate([edge_zero, parts[:, 1], edge_zero], axis=0)
    right_part = jnp.concatenate([edge_zero, edge_zero, parts[:, 2]], axis=0)
    return left_part + middle + right_part


def per_device(queries, keys, values, out_weight, out_grad, pooled):
    query_rows = queries[0]
    key_rows = keys[0]
    value_rows = values[0]
    grad_out = out_grad[0]
    tokens, model_width = query_rows.shape
    local_blocks = tokens // BLOCK
    seq_devices = lax.axis_size("seq")
    seq_index = lax.axis_index("seq")
    all_blocks = local_blocks * seq_devices
    score_scale = 1.0 / math.sqrt(HEAD_DIM)
    pooled_mask = pooled[0].reshape(local_blocks, BLOCK).astype(jnp.float32)
    counts = jnp.sum(pooled_mask, axis=1)
    divisor = jnp.maximum(counts, 1.0)
    pooled_bf = pooled_mask.astype(jnp.bfloat16)
    key_sum = jnp.einsum(
        "nb,nbd->nd",
        pooled_bf,
        key_rows.reshape(local_blocks, BLOCK, model_width),
        preferred_element_type=jnp.float32,
    )
    value_sum = jnp.einsum(
        "nb,nbd->nd",
        pooled_bf,
        value_rows.reshape(local_blocks, BLOCK, model_width),
        preferred_element_type=jnp.float32,
    )
    coarse_keys = (key_sum / divisor[:, None]).astype(jnp.bfloat16)
    coarse_values = (value_sum / divisor[:, None]).astype(jnp.bfloat16)
    count_cols = jnp.broadcast_to(counts.astype(jnp.bfloat16)[:, None], (local_blocks, 128))
    packed = jnp.concatenate([coarse_keys, coarse_values, count_cols], axis=1)
    gathered = doubling_gather(packed, "seq").reshape(all_blocks, packed.shape[1])
    gathered_keys = gathered[:, :model_width]
    gathered_values = gathered[:, model_width : 2 * model_width]
    gathered_counts = gathered[:, 2 * model_width].astype(jnp.float32)
    paired = jnp.stack([key_rows, value_rows])
    extended = padded_2(paired, (("seq", 1),), BLOCK)
    padded_kv = extended.reshape(2, local_blocks + 2, BLOCK, HEADS, HEAD_DIM)
    key_win = block_windows(padded_kv[0], local_blocks)
    value_win = block_windows(padded_kv[1], local_blocks)
    query_blk = query_rows.reshape(local_blocks, BLOCK, HEADS, HEAD_DIM)
    coarse_kh = gathered_keys.reshape(all_blocks, HEADS, HEAD_DIM)
    coarse_vh = gathered_values.reshape(all_blocks, HEADS, HEAD_DIM)
    local_ids = seq_index * local_blocks + jnp.arange(local_blocks)
    offsets = jnp.repeat(jnp.arange(3) - 1, BLOCK)
    key_blocks = local_ids[:, None] + offsets[None, :]
    fine_ok = (key_blocks >= 0) & (key_blocks < all_blocks)
    far_ok = jnp.abs(local_ids[:, None] - jnp.arange(all_blocks)[None, :]) >= 2
    fine_s = (
        jnp.einsum("nqhe,nkhe->nhqk", query_blk, key_win, preferred_element_type=jnp.float32)
        * score_scale
    )
    coarse_s = (
        jnp.einsum("nqhe,che->nhqc", query_blk, coarse_kh, preferred_element_type=jnp.float32)
        * score_scale
    )
    fine_s = jnp.where(fine_ok[:, None, None, :], fine_s, -jnp.inf)
    coarse_s = jnp.where(far_ok[:, None, None, :], coarse_s, -jnp.inf)
    padded_rows = extended.reshape(2, (local_blocks + 2) * BLOCK, model_width)
    attended_rows, top_rows, total_rows = attention_forward(
        query_rows,
        padded_rows[0],
        padded_rows[1],
        gathered_keys,
        gathered_values,
        gathered_counts[None, :],
        fine_ok.astype(jnp.float32),
        far_ok.astype(jnp.float32),
    )
    attended = attended_rows.reshape(local_blocks, BLOCK, HEADS, HEAD_DIM)
    head_stat = lambda rows: rows.reshape(local_blocks, BLOCK, HEADS, HEAD_DIM)[..., 0].transpose(0, 2, 1)[..., None]
    row_top = head_stat(top_rows)
    row_total = head_stat(total_rows)
    fine_w = jnp.exp(fine_s - row_top) / row_total
    coarse_w = gathered_counts * jnp.exp(coarse_s - row_top) / row_total
    fine_wb = fine_w.astype(jnp.bfloat16)
    coarse_wb = coarse_w.astype(jnp.bfloat16)
    attended_grad = jnp.dot(grad_out, out_weight, preferred_element_type=jnp.float32).astype(
        jnp.bfloat16
    )
    grad_norm = 1.0 / math.sqrt(seq_devices * tokens)
    full_term = (
        jnp.einsum("to,ti->oi", grad_out, attended_rows, preferred_element_type=jnp.float32)
        * grad_norm
    )
    seq_part = lax.psum_scatter(full_term, "seq", scatter_dimension=0, tiled=True)
    full_term, attended_grad = lax.optimization_barrier((full_term, attended_grad))
    grad_blk = attended_grad.reshape(local_blocks, BLOCK, HEADS, HEAD_DIM)
    fine_dot = jnp.einsum(
        "nqhe,nkhe->nhqk", grad_blk, value_win, preferred_element_type=jnp.float32
    )
    coarse_dot = jnp.einsum(
        "nqhe,che->nhqc", grad_blk, coarse_vh, preferred_element_type=jnp.float32
    )
    delta_rows = jnp.einsum(
        "nqhe,nqhe->nhq", grad_blk, attended, preferred_element_type=jnp.float32
    )[..., None]
    fine_ds = (fine_w * (fine_dot - delta_rows)).astype(jnp.bfloat16)
    coarse_ds = (coarse_w * (coarse_dot - delta_rows)).astype(jnp.bfloat16)
    query_grad = (
        jnp.einsum("nhqk,nkhe->nqhe", fine_ds, key_win, preferred_element_type=jnp.float32)
        + jnp.einsum("nhqc,che->nqhe", coarse_ds, coarse_kh, preferred_element_type=jnp.float32)
    ) * score_scale
    query_grad = query_grad.astype(jnp.bfloat16).reshape(1, tokens, model_width)
    key_win_grad = (
        jnp.einsum("nhqk,nqhe->nkhe", fine_ds, query_blk, preferred_element_type=jnp.float32)
        * score_scale
    )
    value_win_grad = jnp.einsum(
        "nhqk,nqhe->nkhe", fine_wb, grad_blk, preferred_element_type=jnp.float32
    )
    key_ext = fold_windows(key_win_grad, local_blocks).reshape(local_blocks + 2, BLOCK, model_width)
    value_ext = fold_windows(value_win_grad, local_blocks).reshape(
        local_blocks + 2, BLOCK, model_width
    )
    edge_first = jnp.stack([key_ext[0], value_ext[0]])
    edge_last = jnp.stack([key_ext[local_blocks + 1], value_ext[local_blocks + 1]])
    from_right = from_behind(edge_first, "seq", -1)
    from_left = from_behind(edge_last, "seq", 1)
    zeros_mid = jnp.zeros((2, local_blocks - 1, BLOCK, model_width), jnp.float32)
    boundary = jnp.concatenate([from_left[:, None], zeros_mid], axis=1) + jnp.concatenate(
        [zeros_mid, from_right[:, None]], axis=1
    )
    coarse_key_all = (
        jnp.einsum("nhqc,nqhe->che", coarse_ds, query_blk, preferred_element_type=jnp.float32)
        * score_scale
    )
    coarse_value_all = jnp.einsum(
        "nhqc,nqhe->che", coarse_wb, grad_blk, preferred_element_type=jnp.float32
    )
    coarse_all = jnp.concatenate(
        [
            coarse_key_all.reshape(all_blocks, model_width),
            coarse_value_all.reshape(all_blocks, model_width),
        ],
        axis=1,
    )
    owned_grads = halving_scatter(
        coarse_all.reshape(seq_devices, local_blocks, 2 * model_width), "seq"
    )
    owned_keys = owned_grads[:, :model_width] / divisor[:, None]
    owned_values = owned_grads[:, model_width:] / divisor[:, None]
    spread_keys = owned_keys[:, None, :] * pooled_mask[:, :, None]
    spread_values = owned_values[:, None, :] * pooled_mask[:, :, None]
    key_grad = (
        (key_ext[1 : local_blocks + 1] + boundary[0] + spread_keys)
        .astype(jnp.bfloat16)
        .reshape(1, tokens, model_width)
    )
    value_grad = (
        (value_ext[1 : local_blocks + 1] + boundary[1] + spread_values)
        .astype(jnp.bfloat16)
        .reshape(1, tokens, model_width)
    )
    dp_devices = lax.axis_size("dp")
    dp_rows = halving_scatter(seq_part.reshape(dp_devices, -1, model_width), "dp")
    weight_grad = doubling_gather(dp_rows, "dp").reshape(-1, model_width)
    return (query_grad, key_grad, value_grad, weight_grad)


def solution(mesh):
    placed = (
        P("dp", "seq", None),
        P("dp", "seq", None),
        P("dp", "seq", None),
        P(),
        P("dp", "seq", None),
        P("dp", "seq"),
    )
    return jax.shard_map(
        per_device,
        mesh=mesh,
        in_specs=placed,
        out_specs=(
            P("dp", "seq", None),
            P("dp", "seq", None),
            P("dp", "seq", None),
            P("seq", None),
        ),
        check_vma=False,
    )
```

```python
import math

import jax
import jax.numpy as jnp
from jax import lax
from jax.sharding import PartitionSpec as P

HEADS = 16
HEAD_DIM = 64
BLOCK = 128


def padded_2(block, sides, width):
    for axis, dim in sides:
        count = lax.axis_size(axis)
        forward = [(i, i + 1) for i in range(count - 1)]
        backward = [(target, source) for source, target in forward]
        low = lax.ppermute(
            lax.slice_in_dim(block, block.shape[dim] - width, None, axis=dim), axis, forward
        )
        high = lax.ppermute(lax.slice_in_dim(block, 0, width, axis=dim), axis, backward)
        block = jnp.concatenate([low, block, high], axis=dim)
    return block


def from_behind(value, axis, steps):
    count = lax.axis_size(axis)
    leading, last = (max(0, -steps), min(count, count - steps))
    return lax.ppermute(value, axis, [(source, source + steps) for source in range(leading, last)])


def xor_pairs(count, bit):
    return [(source, source ^ (1 << bit)) for source in range(count)]


def own_bit(axis, bit):
    return (lax.axis_index(axis) // (1 << bit)) % 2


def doubling_gather(piece, axis):
    count = lax.axis_size(axis)
    bits = count.bit_length() - 1
    held = piece
    for done, bit in enumerate(reversed(range(bits))):
        other = lax.ppermute(held, axis, xor_pairs(count, bit))
        mine_low = own_bit(axis, bit) == 0
        low = jnp.where(mine_low, held, other)
        high = jnp.where(mine_low, other, held)
        held = jnp.stack([low, high], axis=done)
    return held.reshape((count,) + piece.shape)


def halving_scatter(stack, axis):
    count = lax.axis_size(axis)
    bits = count.bit_length() - 1
    held = stack.reshape((2,) * bits + stack.shape[1:])
    for bit in range(bits):
        dim = bits - 1 - bit
        mine = own_bit(axis, bit)
        keep = lax.dynamic_index_in_dim(held, mine, dim, keepdims=False)
        send = lax.dynamic_index_in_dim(held, 1 - mine, dim, keepdims=False)
        held = keep + lax.ppermute(send, axis, xor_pairs(count, bit))
    return held


def doubling_sum(value, axis):
    count = lax.axis_size(axis)
    for bit in range(count.bit_length() - 1):
        value = value + lax.ppermute(value, axis, xor_pairs(count, bit))
    return value


def block_windows(padded, local_blocks):
    return jnp.concatenate(
        [padded[0:local_blocks], padded[1 : local_blocks + 1], padded[2 : local_blocks + 2]], axis=1
    )


def fold_windows(grads, local_blocks):
    parts = grads.reshape((local_blocks, 3, BLOCK) + grads.shape[2:])
    edge_zero = jnp.zeros((1,) + parts.shape[2:], jnp.float32)
    left_part = jnp.concatenate([parts[:, 0], edge_zero, edge_zero], axis=0)
    middle = jnp.concatenate([edge_zero, parts[:, 1], edge_zero], axis=0)
    right_part = jnp.concatenate([edge_zero, edge_zero, parts[:, 2]], axis=0)
    return left_part + middle + right_part


def per_device(queries, keys, values, out_weight, out_grad, pooled):
    query_rows = queries[0]
    key_rows = keys[0]
    value_rows = values[0]
    grad_out = out_grad[0]
    tokens, model_width = query_rows.shape
    local_blocks = tokens // BLOCK
    seq_devices = lax.axis_size("seq")
    seq_index = lax.axis_index("seq")
    all_blocks = local_blocks * seq_devices
    score_scale = 1.0 / math.sqrt(HEAD_DIM)
    pooled_mask = pooled[0].reshape(local_blocks, BLOCK).astype(jnp.float32)
    counts = jnp.sum(pooled_mask, axis=1)
    divisor = jnp.maximum(counts, 1.0)
    pooled_bf = pooled_mask.astype(jnp.bfloat16)
    key_sum = jnp.einsum(
        "nb,nbd->nd",
        pooled_bf,
        key_rows.reshape(local_blocks, BLOCK, model_width),
        preferred_element_type=jnp.float32,
    )
    value_sum = jnp.einsum(
        "nb,nbd->nd",
        pooled_bf,
        value_rows.reshape(local_blocks, BLOCK, model_width),
        preferred_element_type=jnp.float32,
    )
    coarse_keys = (key_sum / divisor[:, None]).astype(jnp.bfloat16)
    coarse_values = (value_sum / divisor[:, None]).astype(jnp.bfloat16)
    count_cols = jnp.broadcast_to(counts.astype(jnp.bfloat16)[:, None], (local_blocks, 128))
    packed = jnp.concatenate([coarse_keys, coarse_values, count_cols], axis=1)
    gathered = doubling_gather(packed, "seq").reshape(all_blocks, packed.shape[1])
    gathered_keys = gathered[:, :model_width]
    gathered_values = gathered[:, model_width : 2 * model_width]
    gathered_counts = gathered[:, 2 * model_width].astype(jnp.float32)
    paired = jnp.stack([key_rows, value_rows])
    extended = padded_2(paired, (("seq", 1),), BLOCK)
    padded_kv = extended.reshape(2, local_blocks + 2, BLOCK, HEADS, HEAD_DIM)
    key_win = block_windows(padded_kv[0], local_blocks)
    value_win = block_windows(padded_kv[1], local_blocks)
    query_blk = query_rows.reshape(local_blocks, BLOCK, HEADS, HEAD_DIM)
    coarse_kh = gathered_keys.reshape(all_blocks, HEADS, HEAD_DIM)
    coarse_vh = gathered_values.reshape(all_blocks, HEADS, HEAD_DIM)
    local_ids = seq_index * local_blocks + jnp.arange(local_blocks)
    offsets = jnp.repeat(jnp.arange(3) - 1, BLOCK)
    key_blocks = local_ids[:, None] + offsets[None, :]
    fine_ok = (key_blocks >= 0) & (key_blocks < all_blocks)
    far_ok = jnp.abs(local_ids[:, None] - jnp.arange(all_blocks)[None, :]) >= 2
    fine_s = (
        jnp.einsum("nqhe,nkhe->nhqk", query_blk, key_win, preferred_element_type=jnp.float32)
        * score_scale
    )
    coarse_s = (
        jnp.einsum("nqhe,che->nhqc", query_blk, coarse_kh, preferred_element_type=jnp.float32)
        * score_scale
    )
    fine_s = jnp.where(fine_ok[:, None, None, :], fine_s, -jnp.inf)
    coarse_s = jnp.where(far_ok[:, None, None, :], coarse_s, -jnp.inf)
    row_top = jnp.maximum(jnp.max(fine_s, axis=-1), jnp.max(coarse_s, axis=-1))[..., None]
    fine_e = jnp.exp(fine_s - row_top)
    coarse_e = gathered_counts * jnp.exp(coarse_s - row_top)
    row_total = jnp.sum(fine_e, axis=-1, keepdims=True) + jnp.sum(coarse_e, axis=-1, keepdims=True)
    fine_w = fine_e / row_total
    coarse_w = coarse_e / row_total
    fine_wb = fine_w.astype(jnp.bfloat16)
    coarse_wb = coarse_w.astype(jnp.bfloat16)
    attended = (
        jnp.einsum("nhqk,nkhe->nqhe", fine_wb, value_win, preferred_element_type=jnp.float32)
        + jnp.einsum("nhqc,che->nqhe", coarse_wb, coarse_vh, preferred_element_type=jnp.float32)
    ).astype(jnp.bfloat16)
    attended_rows = attended.reshape(tokens, model_width)
    attended_grad = jnp.dot(grad_out, out_weight, preferred_element_type=jnp.float32).astype(
        jnp.bfloat16
    )
    grad_norm = 1.0 / math.sqrt(seq_devices * tokens)
    full_term = (
        jnp.einsum("to,ti->oi", grad_out, attended_rows, preferred_element_type=jnp.float32)
        * grad_norm
    )
    seq_part = lax.psum_scatter(
        full_term.astype(jnp.bfloat16), "seq", scatter_dimension=0, tiled=True
    ).astype(jnp.float32)
    full_term, attended_grad = lax.optimization_barrier((full_term, attended_grad))
    grad_blk = attended_grad.reshape(local_blocks, BLOCK, HEADS, HEAD_DIM)
    fine_dot = jnp.einsum(
        "nqhe,nkhe->nhqk", grad_blk, value_win, preferred_element_type=jnp.float32
    )
    coarse_dot = jnp.einsum(
        "nqhe,che->nhqc", grad_blk, coarse_vh, preferred_element_type=jnp.float32
    )
    delta_rows = jnp.einsum(
        "nqhe,nqhe->nhq", grad_blk, attended, preferred_element_type=jnp.float32
    )[..., None]
    fine_ds = (fine_w * (fine_dot - delta_rows)).astype(jnp.bfloat16)
    coarse_ds = (coarse_w * (coarse_dot - delta_rows)).astype(jnp.bfloat16)
    query_grad = (
        jnp.einsum("nhqk,nkhe->nqhe", fine_ds, key_win, preferred_element_type=jnp.float32)
        + jnp.einsum("nhqc,che->nqhe", coarse_ds, coarse_kh, preferred_element_type=jnp.float32)
    ) * score_scale
    query_grad = query_grad.astype(jnp.bfloat16).reshape(1, tokens, model_width)
    key_win_grad = (
        jnp.einsum("nhqk,nqhe->nkhe", fine_ds, query_blk, preferred_element_type=jnp.float32)
        * score_scale
    )
    value_win_grad = jnp.einsum(
        "nhqk,nqhe->nkhe", fine_wb, grad_blk, preferred_element_type=jnp.float32
    )
    key_ext = fold_windows(key_win_grad, local_blocks).reshape(local_blocks + 2, BLOCK, model_width)
    value_ext = fold_windows(value_win_grad, local_blocks).reshape(
        local_blocks + 2, BLOCK, model_width
    )
    edge_first = jnp.stack([key_ext[0], value_ext[0]])
    edge_last = jnp.stack([key_ext[local_blocks + 1], value_ext[local_blocks + 1]])
    from_right = from_behind(edge_first, "seq", -1)
    from_left = from_behind(edge_last, "seq", 1)
    zeros_mid = jnp.zeros((2, local_blocks - 1, BLOCK, model_width), jnp.float32)
    boundary = jnp.concatenate([from_left[:, None], zeros_mid], axis=1) + jnp.concatenate(
        [zeros_mid, from_right[:, None]], axis=1
    )
    coarse_key_all = (
        jnp.einsum("nhqc,nqhe->che", coarse_ds, query_blk, preferred_element_type=jnp.float32)
        * score_scale
    )
    coarse_value_all = jnp.einsum(
        "nhqc,nqhe->che", coarse_wb, grad_blk, preferred_element_type=jnp.float32
    )
    coarse_all = jnp.concatenate(
        [
            coarse_key_all.reshape(all_blocks, model_width),
            coarse_value_all.reshape(all_blocks, model_width),
        ],
        axis=1,
    )
    owned_grads = halving_scatter(
        coarse_all.reshape(seq_devices, local_blocks, 2 * model_width), "seq"
    )
    owned_keys = owned_grads[:, :model_width] / divisor[:, None]
    owned_values = owned_grads[:, model_width:] / divisor[:, None]
    spread_keys = owned_keys[:, None, :] * pooled_mask[:, :, None]
    spread_values = owned_values[:, None, :] * pooled_mask[:, :, None]
    key_grad = (
        (key_ext[1 : local_blocks + 1] + boundary[0] + spread_keys)
        .astype(jnp.bfloat16)
        .reshape(1, tokens, model_width)
    )
    value_grad = (
        (value_ext[1 : local_blocks + 1] + boundary[1] + spread_values)
        .astype(jnp.bfloat16)
        .reshape(1, tokens, model_width)
    )
    dp_devices = lax.axis_size("dp")
    dp_rows = halving_scatter(seq_part.reshape(dp_devices, -1, model_width), "dp")
    weight_grad = doubling_gather(dp_rows, "dp").reshape(-1, model_width)
    return (query_grad, key_grad, value_grad, weight_grad)


def solution(mesh):
    placed = (
        P("dp", "seq", None),
        P("dp", "seq", None),
        P("dp", "seq", None),
        P(),
        P("dp", "seq", None),
        P("dp", "seq"),
    )
    return jax.shard_map(
        per_device,
        mesh=mesh,
        in_specs=placed,
        out_specs=(
            P("dp", "seq", None),
            P("dp", "seq", None),
            P("dp", "seq", None),
            P("seq", None),
        ),
        check_vma=False,
    )
```

```python
import math

import jax
import jax.numpy as jnp
from jax import lax
from jax.sharding import PartitionSpec as P

HEADS = 16
HEAD_DIM = 64
BLOCK = 128


def padded_2(block, sides, width):
    for axis, dim in sides:
        count = lax.axis_size(axis)
        forward = [(i, i + 1) for i in range(count - 1)]
        backward = [(target, source) for source, target in forward]
        low = lax.ppermute(
            lax.slice_in_dim(block, block.shape[dim] - width, None, axis=dim), axis, forward
        )
        high = lax.ppermute(lax.slice_in_dim(block, 0, width, axis=dim), axis, backward)
        block = jnp.concatenate([low, block, high], axis=dim)
    return block


def from_behind(value, axis, steps):
    count = lax.axis_size(axis)
    leading, last = (max(0, -steps), min(count, count - steps))
    return lax.ppermute(value, axis, [(source, source + steps) for source in range(leading, last)])


def xor_pairs(count, bit):
    return [(source, source ^ (1 << bit)) for source in range(count)]


def own_bit(axis, bit):
    return (lax.axis_index(axis) // (1 << bit)) % 2


def doubling_gather(piece, axis):
    count = lax.axis_size(axis)
    bits = count.bit_length() - 1
    held = piece
    for done, bit in enumerate(reversed(range(bits))):
        other = lax.ppermute(held, axis, xor_pairs(count, bit))
        mine_low = own_bit(axis, bit) == 0
        low = jnp.where(mine_low, held, other)
        high = jnp.where(mine_low, other, held)
        held = jnp.stack([low, high], axis=done)
    return held.reshape((count,) + piece.shape)


def halving_scatter(stack, axis):
    count = lax.axis_size(axis)
    bits = count.bit_length() - 1
    held = stack.reshape((2,) * bits + stack.shape[1:])
    for bit in range(bits):
        dim = bits - 1 - bit
        mine = own_bit(axis, bit)
        keep = lax.dynamic_index_in_dim(held, mine, dim, keepdims=False)
        send = lax.dynamic_index_in_dim(held, 1 - mine, dim, keepdims=False)
        held = keep + lax.ppermute(send, axis, xor_pairs(count, bit))
    return held


def doubling_sum(value, axis):
    count = lax.axis_size(axis)
    for bit in range(count.bit_length() - 1):
        value = value + lax.ppermute(value, axis, xor_pairs(count, bit))
    return value


def block_windows(padded, local_blocks):
    return jnp.concatenate(
        [padded[0:local_blocks], padded[1 : local_blocks + 1], padded[2 : local_blocks + 2]], axis=1
    )


def fold_windows(grads, local_blocks):
    parts = grads.reshape((local_blocks, 3, BLOCK) + grads.shape[2:])
    edge_zero = jnp.zeros((1,) + parts.shape[2:], jnp.float32)
    left_part = jnp.concatenate([parts[:, 0], edge_zero, edge_zero], axis=0)
    middle = jnp.concatenate([edge_zero, parts[:, 1], edge_zero], axis=0)
    right_part = jnp.concatenate([edge_zero, edge_zero, parts[:, 2]], axis=0)
    return left_part + middle + right_part


def per_device(queries, keys, values, out_weight, out_grad, pooled):
    query_rows = queries[0]
    key_rows = keys[0]
    value_rows = values[0]
    grad_out = out_grad[0]
    tokens, model_width = query_rows.shape
    local_blocks = tokens // BLOCK
    seq_devices = lax.axis_size("seq")
    seq_index = lax.axis_index("seq")
    all_blocks = local_blocks * seq_devices
    score_scale = 1.0 / math.sqrt(HEAD_DIM)
    pooled_mask = pooled[0].reshape(local_blocks, BLOCK).astype(jnp.float32)
    counts = jnp.sum(pooled_mask, axis=1)
    divisor = jnp.maximum(counts, 1.0)
    pooled_bf = pooled_mask.astype(jnp.bfloat16)
    key_sum = jnp.einsum(
        "nb,nbd->nd",
        pooled_bf,
        key_rows.reshape(local_blocks, BLOCK, model_width),
        preferred_element_type=jnp.float32,
    )
    value_sum = jnp.einsum(
        "nb,nbd->nd",
        pooled_bf,
        value_rows.reshape(local_blocks, BLOCK, model_width),
        preferred_element_type=jnp.float32,
    )
    coarse_keys = (key_sum / divisor[:, None]).astype(jnp.bfloat16)
    coarse_values = (value_sum / divisor[:, None]).astype(jnp.bfloat16)
    count_cols = jnp.broadcast_to(counts.astype(jnp.bfloat16)[:, None], (local_blocks, 128))
    packed = jnp.concatenate([coarse_keys, coarse_values, count_cols], axis=1)
    gathered = doubling_gather(packed, "seq").reshape(all_blocks, packed.shape[1])
    gathered_keys = gathered[:, :model_width]
    gathered_values = gathered[:, model_width : 2 * model_width]
    gathered_counts = gathered[:, 2 * model_width].astype(jnp.float32)
    paired = jnp.stack([key_rows, value_rows])
    extended = padded_2(paired, (("seq", 1),), BLOCK)
    padded_kv = extended.reshape(2, local_blocks + 2, BLOCK, HEADS, HEAD_DIM)
    key_win = block_windows(padded_kv[0], local_blocks)
    value_win = block_windows(padded_kv[1], local_blocks)
    query_blk = query_rows.reshape(local_blocks, BLOCK, HEADS, HEAD_DIM)
    coarse_kh = gathered_keys.reshape(all_blocks, HEADS, HEAD_DIM)
    coarse_vh = gathered_values.reshape(all_blocks, HEADS, HEAD_DIM)
    local_ids = seq_index * local_blocks + jnp.arange(local_blocks)
    offsets = jnp.repeat(jnp.arange(3) - 1, BLOCK)
    key_blocks = local_ids[:, None] + offsets[None, :]
    fine_ok = (key_blocks >= 0) & (key_blocks < all_blocks)
    far_ok = jnp.abs(local_ids[:, None] - jnp.arange(all_blocks)[None, :]) >= 2
    fine_s = (
        jnp.einsum("nqhe,nkhe->nhqk", query_blk, key_win, preferred_element_type=jnp.float32)
        * score_scale
    )
    coarse_s = (
        jnp.einsum("nqhe,che->nhqc", query_blk, coarse_kh, preferred_element_type=jnp.float32)
        * score_scale
    )
    fine_s = jnp.where(fine_ok[:, None, None, :], fine_s, -jnp.inf)
    coarse_s = jnp.where(far_ok[:, None, None, :], coarse_s, -jnp.inf)
    row_top = jnp.maximum(jnp.max(fine_s, axis=-1), jnp.max(coarse_s, axis=-1))[..., None]
    fine_e = jnp.exp(fine_s - row_top)
    coarse_e = gathered_counts * jnp.exp(coarse_s - row_top)
    row_total = jnp.sum(fine_e, axis=-1, keepdims=True) + jnp.sum(coarse_e, axis=-1, keepdims=True)
    fine_w = fine_e / row_total
    coarse_w = coarse_e / row_total
    fine_wb = fine_w.astype(jnp.bfloat16)
    coarse_wb = coarse_w.astype(jnp.bfloat16)
    attended = (
        jnp.einsum("nhqk,nkhe->nqhe", fine_wb, value_win, preferred_element_type=jnp.float32)
        + jnp.einsum("nhqc,che->nqhe", coarse_wb, coarse_vh, preferred_element_type=jnp.float32)
    ).astype(jnp.bfloat16)
    attended_rows = attended.reshape(tokens, model_width)
    attended_grad = jnp.dot(grad_out, out_weight, preferred_element_type=jnp.float32).astype(
        jnp.bfloat16
    )
    grad_norm = 1.0 / math.sqrt(seq_devices * tokens)
    full_term = (
        jnp.einsum("to,ti->oi", grad_out, attended_rows, preferred_element_type=jnp.float32)
        * grad_norm
    )
    seq_part = lax.psum_scatter(full_term, "seq", scatter_dimension=0, tiled=True)
    full_term, attended_grad = lax.optimization_barrier((full_term, attended_grad))
    grad_blk = attended_grad.reshape(local_blocks, BLOCK, HEADS, HEAD_DIM)
    fine_dot = jnp.einsum(
        "nqhe,nkhe->nhqk", grad_blk, value_win, preferred_element_type=jnp.float32
    )
    coarse_dot = jnp.einsum(
        "nqhe,che->nhqc", grad_blk, coarse_vh, preferred_element_type=jnp.float32
    )
    delta_rows = jnp.einsum(
        "nqhe,nqhe->nhq", grad_blk, attended, preferred_element_type=jnp.float32
    )[..., None]
    fine_ds = (fine_w * (fine_dot - delta_rows)).astype(jnp.bfloat16)
    coarse_ds = (coarse_w * (coarse_dot - delta_rows)).astype(jnp.bfloat16)
    query_grad = (
        jnp.einsum("nhqk,nkhe->nqhe", fine_ds, key_win, preferred_element_type=jnp.float32)
        + jnp.einsum("nhqc,che->nqhe", coarse_ds, coarse_kh, preferred_element_type=jnp.float32)
    ) * score_scale
    query_grad = query_grad.astype(jnp.bfloat16).reshape(1, tokens, model_width)
    key_win_grad = (
        jnp.einsum("nhqk,nqhe->nkhe", fine_ds, query_blk, preferred_element_type=jnp.float32)
        * score_scale
    )
    value_win_grad = jnp.einsum(
        "nhqk,nqhe->nkhe", fine_wb, grad_blk, preferred_element_type=jnp.float32
    )
    key_ext = fold_windows(key_win_grad, local_blocks).reshape(local_blocks + 2, BLOCK, model_width)
    value_ext = fold_windows(value_win_grad, local_blocks).reshape(
        local_blocks + 2, BLOCK, model_width
    )
    edge_first = jnp.stack([key_ext[0], value_ext[0]])
    edge_last = jnp.stack([key_ext[local_blocks + 1], value_ext[local_blocks + 1]])
    from_right = from_behind(edge_first, "seq", -1)
    from_left = from_behind(edge_last, "seq", 1)
    zeros_mid = jnp.zeros((2, local_blocks - 1, BLOCK, model_width), jnp.float32)
    boundary = jnp.concatenate([from_left[:, None], zeros_mid], axis=1) + jnp.concatenate(
        [zeros_mid, from_right[:, None]], axis=1
    )
    coarse_key_all = (
        jnp.einsum("nhqc,nqhe->che", coarse_ds, query_blk, preferred_element_type=jnp.float32)
        * score_scale
    )
    coarse_value_all = jnp.einsum(
        "nhqc,nqhe->che", coarse_wb, grad_blk, preferred_element_type=jnp.float32
    )
    coarse_all = jnp.concatenate(
        [
            coarse_key_all.reshape(all_blocks, model_width),
            coarse_value_all.reshape(all_blocks, model_width),
        ],
        axis=1,
    )
    owned_grads = halving_scatter(
        coarse_all.reshape(seq_devices, local_blocks, 2 * model_width), "seq"
    )
    owned_keys = owned_grads[:, :model_width] / divisor[:, None]
    owned_values = owned_grads[:, model_width:] / divisor[:, None]
    spread_keys = owned_keys[:, None, :] * pooled_mask[:, :, None]
    spread_values = owned_values[:, None, :] * pooled_mask[:, :, None]
    key_grad = (
        (key_ext[1 : local_blocks + 1] + boundary[0] + spread_keys)
        .astype(jnp.bfloat16)
        .reshape(1, tokens, model_width)
    )
    value_grad = (
        (value_ext[1 : local_blocks + 1] + boundary[1] + spread_values)
        .astype(jnp.bfloat16)
        .reshape(1, tokens, model_width)
    )
    seq_part, query_grad, key_grad, value_grad = lax.optimization_barrier(
        (seq_part, query_grad, key_grad, value_grad)
    )
    dp_devices = lax.axis_size("dp")
    dp_rows = halving_scatter(seq_part.reshape(dp_devices, -1, model_width), "dp")
    weight_grad = doubling_gather(dp_rows, "dp").reshape(-1, model_width)
    return (query_grad, key_grad, value_grad, weight_grad)


def solution(mesh):
    placed = (
        P("dp", "seq", None),
        P("dp", "seq", None),
        P("dp", "seq", None),
        P(),
        P("dp", "seq", None),
        P("dp", "seq"),
    )
    return jax.shard_map(
        per_device,
        mesh=mesh,
        in_specs=placed,
        out_specs=(
            P("dp", "seq", None),
            P("dp", "seq", None),
            P("dp", "seq", None),
            P("seq", None),
        ),
        check_vma=False,
    )
```

```python
import math

import jax
import jax.numpy as jnp
from jax import lax
from jax.sharding import PartitionSpec as P

HEADS = 16
HEAD_DIM = 64
BLOCK = 128


def padded_2(block, sides, width):
    for axis, dim in sides:
        count = lax.axis_size(axis)
        forward = [(i, i + 1) for i in range(count - 1)]
        backward = [(target, source) for source, target in forward]
        low = lax.ppermute(
            lax.slice_in_dim(block, block.shape[dim] - width, None, axis=dim), axis, forward
        )
        high = lax.ppermute(lax.slice_in_dim(block, 0, width, axis=dim), axis, backward)
        block = jnp.concatenate([low, block, high], axis=dim)
    return block


def from_behind(value, axis, steps):
    count = lax.axis_size(axis)
    leading, last = (max(0, -steps), min(count, count - steps))
    return lax.ppermute(value, axis, [(source, source + steps) for source in range(leading, last)])


def xor_pairs(count, bit):
    return [(source, source ^ (1 << bit)) for source in range(count)]


def own_bit(axis, bit):
    return (lax.axis_index(axis) // (1 << bit)) % 2


def doubling_gather(piece, axis):
    count = lax.axis_size(axis)
    bits = count.bit_length() - 1
    held = piece
    for done, bit in enumerate(reversed(range(bits))):
        other = lax.ppermute(held, axis, xor_pairs(count, bit))
        mine_low = own_bit(axis, bit) == 0
        low = jnp.where(mine_low, held, other)
        high = jnp.where(mine_low, other, held)
        held = jnp.stack([low, high], axis=done)
    return held.reshape((count,) + piece.shape)


def halving_scatter(stack, axis):
    count = lax.axis_size(axis)
    bits = count.bit_length() - 1
    held = stack.reshape((2,) * bits + stack.shape[1:])
    for bit in range(bits):
        dim = bits - 1 - bit
        mine = own_bit(axis, bit)
        keep = lax.dynamic_index_in_dim(held, mine, dim, keepdims=False)
        send = lax.dynamic_index_in_dim(held, 1 - mine, dim, keepdims=False)
        held = keep + lax.ppermute(send, axis, xor_pairs(count, bit))
    return held


def doubling_sum(value, axis):
    count = lax.axis_size(axis)
    for bit in range(count.bit_length() - 1):
        value = value + lax.ppermute(value, axis, xor_pairs(count, bit))
    return value


def block_windows(padded, local_blocks):
    return jnp.concatenate(
        [padded[0:local_blocks], padded[1 : local_blocks + 1], padded[2 : local_blocks + 2]], axis=1
    )


def fold_windows(grads, local_blocks):
    parts = grads.reshape((local_blocks, 3, BLOCK) + grads.shape[2:])
    edge_zero = jnp.zeros((1,) + parts.shape[2:], jnp.float32)
    left_part = jnp.concatenate([parts[:, 0], edge_zero, edge_zero], axis=0)
    middle = jnp.concatenate([edge_zero, parts[:, 1], edge_zero], axis=0)
    right_part = jnp.concatenate([edge_zero, edge_zero, parts[:, 2]], axis=0)
    return left_part + middle + right_part


def per_device(queries, keys, values, out_weight, out_grad, pooled):
    query_rows = queries[0]
    key_rows = keys[0]
    value_rows = values[0]
    grad_out = out_grad[0]
    tokens, model_width = query_rows.shape
    local_blocks = tokens // BLOCK
    seq_devices = lax.axis_size("seq")
    seq_index = lax.axis_index("seq")
    all_blocks = local_blocks * seq_devices
    score_scale = 1.0 / math.sqrt(HEAD_DIM)
    pooled_mask = pooled[0].reshape(local_blocks, BLOCK).astype(jnp.float32)
    counts = jnp.sum(pooled_mask, axis=1)
    divisor = jnp.maximum(counts, 1.0)
    pooled_bf = pooled_mask.astype(jnp.bfloat16)
    key_sum = jnp.einsum(
        "nb,nbd->nd",
        pooled_bf,
        key_rows.reshape(local_blocks, BLOCK, model_width),
        preferred_element_type=jnp.float32,
    )
    value_sum = jnp.einsum(
        "nb,nbd->nd",
        pooled_bf,
        value_rows.reshape(local_blocks, BLOCK, model_width),
        preferred_element_type=jnp.float32,
    )
    coarse_keys = (key_sum / divisor[:, None]).astype(jnp.bfloat16)
    coarse_values = (value_sum / divisor[:, None]).astype(jnp.bfloat16)
    count_cols = jnp.broadcast_to(counts.astype(jnp.bfloat16)[:, None], (local_blocks, 128))
    packed = jnp.concatenate([coarse_keys, coarse_values, count_cols], axis=1)
    gathered = doubling_gather(packed, "seq").reshape(all_blocks, packed.shape[1])
    gathered_keys = gathered[:, :model_width]
    gathered_values = gathered[:, model_width : 2 * model_width]
    gathered_counts = gathered[:, 2 * model_width].astype(jnp.float32)
    paired = jnp.stack([key_rows, value_rows])
    extended = padded_2(paired, (("seq", 1),), BLOCK)
    padded_kv = extended.reshape(2, local_blocks + 2, BLOCK, HEADS, HEAD_DIM)
    key_win = block_windows(padded_kv[0], local_blocks)
    value_win = block_windows(padded_kv[1], local_blocks)
    query_blk = query_rows.reshape(local_blocks, BLOCK, HEADS, HEAD_DIM)
    coarse_kh = gathered_keys.reshape(all_blocks, HEADS, HEAD_DIM)
    coarse_vh = gathered_values.reshape(all_blocks, HEADS, HEAD_DIM)
    local_ids = seq_index * local_blocks + jnp.arange(local_blocks)
    offsets = jnp.repeat(jnp.arange(3) - 1, BLOCK)
    key_blocks = local_ids[:, None] + offsets[None, :]
    fine_ok = (key_blocks >= 0) & (key_blocks < all_blocks)
    far_ok = jnp.abs(local_ids[:, None] - jnp.arange(all_blocks)[None, :]) >= 2
    fine_s = (
        jnp.einsum("nqhe,nkhe->nhqk", query_blk, key_win, preferred_element_type=jnp.float32)
        * score_scale
    )
    coarse_s = (
        jnp.einsum("nqhe,che->nhqc", query_blk, coarse_kh, preferred_element_type=jnp.float32)
        * score_scale
    )
    fine_s = jnp.where(fine_ok[:, None, None, :], fine_s, -jnp.inf)
    coarse_s = jnp.where(far_ok[:, None, None, :], coarse_s, -jnp.inf)
    row_top = jnp.maximum(jnp.max(fine_s, axis=-1), jnp.max(coarse_s, axis=-1))[..., None]
    fine_e = jnp.exp(fine_s - row_top)
    coarse_e = gathered_counts * jnp.exp(coarse_s - row_top)
    row_total = jnp.sum(fine_e, axis=-1, keepdims=True) + jnp.sum(coarse_e, axis=-1, keepdims=True)
    fine_w = fine_e / row_total
    coarse_w = coarse_e / row_total
    fine_wb = fine_w.astype(jnp.bfloat16)
    coarse_wb = coarse_w.astype(jnp.bfloat16)
    attended = (
        jnp.einsum("nhqk,nkhe->nqhe", fine_wb, value_win, preferred_element_type=jnp.float32)
        + jnp.einsum("nhqc,che->nqhe", coarse_wb, coarse_vh, preferred_element_type=jnp.float32)
    ).astype(jnp.bfloat16)
    attended_rows = attended.reshape(tokens, model_width)
    attended_grad = jnp.dot(grad_out, out_weight, preferred_element_type=jnp.float32).astype(
        jnp.bfloat16
    )
    grad_norm = 1.0 / math.sqrt(seq_devices * tokens)
    full_term = (
        jnp.einsum("to,ti->oi", grad_out, attended_rows, preferred_element_type=jnp.float32)
        * grad_norm
    )
    seq_part = lax.psum_scatter(
        jnp.pad(full_term, ((0, 0), (0, 1024))), "seq", scatter_dimension=0, tiled=True
    )[:, :model_width]
    full_term, attended_grad = lax.optimization_barrier((full_term, attended_grad))
    grad_blk = attended_grad.reshape(local_blocks, BLOCK, HEADS, HEAD_DIM)
    fine_dot = jnp.einsum(
        "nqhe,nkhe->nhqk", grad_blk, value_win, preferred_element_type=jnp.float32
    )
    coarse_dot = jnp.einsum(
        "nqhe,che->nhqc", grad_blk, coarse_vh, preferred_element_type=jnp.float32
    )
    delta_rows = jnp.einsum(
        "nqhe,nqhe->nhq", grad_blk, attended, preferred_element_type=jnp.float32
    )[..., None]
    fine_ds = (fine_w * (fine_dot - delta_rows)).astype(jnp.bfloat16)
    coarse_ds = (coarse_w * (coarse_dot - delta_rows)).astype(jnp.bfloat16)
    query_grad = (
        jnp.einsum("nhqk,nkhe->nqhe", fine_ds, key_win, preferred_element_type=jnp.float32)
        + jnp.einsum("nhqc,che->nqhe", coarse_ds, coarse_kh, preferred_element_type=jnp.float32)
    ) * score_scale
    query_grad = query_grad.astype(jnp.bfloat16).reshape(1, tokens, model_width)
    key_win_grad = (
        jnp.einsum("nhqk,nqhe->nkhe", fine_ds, query_blk, preferred_element_type=jnp.float32)
        * score_scale
    )
    value_win_grad = jnp.einsum(
        "nhqk,nqhe->nkhe", fine_wb, grad_blk, preferred_element_type=jnp.float32
    )
    key_ext = fold_windows(key_win_grad, local_blocks).reshape(local_blocks + 2, BLOCK, model_width)
    value_ext = fold_windows(value_win_grad, local_blocks).reshape(
        local_blocks + 2, BLOCK, model_width
    )
    edge_first = jnp.stack([key_ext[0], value_ext[0]])
    edge_last = jnp.stack([key_ext[local_blocks + 1], value_ext[local_blocks + 1]])
    from_right = from_behind(edge_first, "seq", -1)
    from_left = from_behind(edge_last, "seq", 1)
    zeros_mid = jnp.zeros((2, local_blocks - 1, BLOCK, model_width), jnp.float32)
    boundary = jnp.concatenate([from_left[:, None], zeros_mid], axis=1) + jnp.concatenate(
        [zeros_mid, from_right[:, None]], axis=1
    )
    coarse_key_all = (
        jnp.einsum("nhqc,nqhe->che", coarse_ds, query_blk, preferred_element_type=jnp.float32)
        * score_scale
    )
    coarse_value_all = jnp.einsum(
        "nhqc,nqhe->che", coarse_wb, grad_blk, preferred_element_type=jnp.float32
    )
    coarse_all = jnp.concatenate(
        [
            coarse_key_all.reshape(all_blocks, model_width),
            coarse_value_all.reshape(all_blocks, model_width),
        ],
        axis=1,
    )
    owned_grads = halving_scatter(
        coarse_all.reshape(seq_devices, local_blocks, 2 * model_width), "seq"
    )
    owned_keys = owned_grads[:, :model_width] / divisor[:, None]
    owned_values = owned_grads[:, model_width:] / divisor[:, None]
    spread_keys = owned_keys[:, None, :] * pooled_mask[:, :, None]
    spread_values = owned_values[:, None, :] * pooled_mask[:, :, None]
    key_grad = (
        (key_ext[1 : local_blocks + 1] + boundary[0] + spread_keys)
        .astype(jnp.bfloat16)
        .reshape(1, tokens, model_width)
    )
    value_grad = (
        (value_ext[1 : local_blocks + 1] + boundary[1] + spread_values)
        .astype(jnp.bfloat16)
        .reshape(1, tokens, model_width)
    )
    seq_part, query_grad, key_grad, value_grad = lax.optimization_barrier(
        (seq_part, query_grad, key_grad, value_grad)
    )
    dp_devices = lax.axis_size("dp")
    dp_rows = halving_scatter(seq_part.reshape(dp_devices, -1, model_width), "dp")
    weight_grad = doubling_gather(dp_rows, "dp").reshape(-1, model_width)
    return (query_grad, key_grad, value_grad, weight_grad)


def solution(mesh):
    placed = (
        P("dp", "seq", None),
        P("dp", "seq", None),
        P("dp", "seq", None),
        P(),
        P("dp", "seq", None),
        P("dp", "seq"),
    )
    return jax.shard_map(
        per_device,
        mesh=mesh,
        in_specs=placed,
        out_specs=(
            P("dp", "seq", None),
            P("dp", "seq", None),
            P("dp", "seq", None),
            P("seq", None),
        ),
        check_vma=False,
    )
```

```python
import math

import jax
import jax.numpy as jnp
from jax import lax
from jax.experimental import pallas as pl
from jax.experimental.pallas import tpu as pltpu
from jax.sharding import PartitionSpec as P

HEADS = 16
HEAD_DIM = 64
BLOCK = 128


def padded_2(block, sides, width):
    for axis, dim in sides:
        count = lax.axis_size(axis)
        forward = [(i, i + 1) for i in range(count - 1)]
        backward = [(target, source) for source, target in forward]
        low = lax.ppermute(
            lax.slice_in_dim(block, block.shape[dim] - width, None, axis=dim), axis, forward
        )
        high = lax.ppermute(lax.slice_in_dim(block, 0, width, axis=dim), axis, backward)
        block = jnp.concatenate([low, block, high], axis=dim)
    return block


def from_behind(value, axis, steps):
    count = lax.axis_size(axis)
    leading, last = (max(0, -steps), min(count, count - steps))
    return lax.ppermute(value, axis, [(source, source + steps) for source in range(leading, last)])


def xor_pairs(count, bit):
    return [(source, source ^ (1 << bit)) for source in range(count)]


def own_bit(axis, bit):
    return (lax.axis_index(axis) // (1 << bit)) % 2


def doubling_gather(piece, axis):
    count = lax.axis_size(axis)
    bits = count.bit_length() - 1
    held = piece
    for done, bit in enumerate(reversed(range(bits))):
        other = lax.ppermute(held, axis, xor_pairs(count, bit))
        mine_low = own_bit(axis, bit) == 0
        low = jnp.where(mine_low, held, other)
        high = jnp.where(mine_low, other, held)
        held = jnp.stack([low, high], axis=done)
    return held.reshape((count,) + piece.shape)


def halving_scatter(stack, axis):
    count = lax.axis_size(axis)
    bits = count.bit_length() - 1
    held = stack.reshape((2,) * bits + stack.shape[1:])
    for bit in range(bits):
        dim = bits - 1 - bit
        mine = own_bit(axis, bit)
        keep = lax.dynamic_index_in_dim(held, mine, dim, keepdims=False)
        send = lax.dynamic_index_in_dim(held, 1 - mine, dim, keepdims=False)
        held = keep + lax.ppermute(send, axis, xor_pairs(count, bit))
    return held


def doubling_sum(value, axis):
    count = lax.axis_size(axis)
    for bit in range(count.bit_length() - 1):
        value = value + lax.ppermute(value, axis, xor_pairs(count, bit))
    return value


def forward_kernel(q_ref, k_ref, v_ref, ck_ref, cv_ref, counts_ref, fine_ref, far_ref,
                   att_ref, top_ref, total_ref):
    score_scale = 1.0 / math.sqrt(HEAD_DIM)
    lanes = q_ref.shape[1]
    low_lanes = lax.broadcasted_iota(jnp.int32, (BLOCK, lanes), 1) < HEAD_DIM
    coarse_k = ck_ref[...]
    coarse_v = cv_ref[...]
    counts = counts_ref[...]
    contract_last = (((1,), (1,)), ((), ()))
    for block in range(q_ref.shape[0] // BLOCK):
        query = q_ref[pl.ds(block * BLOCK, BLOCK), :]
        key_win = k_ref[pl.ds(block * BLOCK, 3 * BLOCK), :]
        value_win = v_ref[pl.ds(block * BLOCK, 3 * BLOCK), :]
        fine_ok = fine_ref[pl.ds(block, 1), :] > 0
        far_ok = far_ref[pl.ds(block, 1), :] > 0
        halves = []
        for half in range(2):
            own = low_lanes if half == 0 else jnp.logical_not(low_lanes)
            query_h = jnp.where(own, query, jnp.zeros_like(query))
            fine_s = lax.dot_general(query_h, key_win, contract_last,
                                     preferred_element_type=jnp.float32) * score_scale
            coarse_s = lax.dot_general(query_h, coarse_k, contract_last,
                                       preferred_element_type=jnp.float32) * score_scale
            fine_s = jnp.where(fine_ok, fine_s, -jnp.inf)
            coarse_s = jnp.where(far_ok, coarse_s, -jnp.inf)
            top = jnp.maximum(jnp.max(fine_s, axis=1, keepdims=True),
                              jnp.max(coarse_s, axis=1, keepdims=True))
            fine_e = jnp.exp(fine_s - top)
            coarse_e = counts * jnp.exp(coarse_s - top)
            total = (jnp.sum(fine_e, axis=1, keepdims=True)
                     + jnp.sum(coarse_e, axis=1, keepdims=True))
            fine_w = (fine_e / total).astype(jnp.bfloat16)
            coarse_w = (coarse_e / total).astype(jnp.bfloat16)
            att = (jnp.dot(fine_w, value_win, preferred_element_type=jnp.float32)
                   + jnp.dot(coarse_w, coarse_v, preferred_element_type=jnp.float32))
            halves.append((att, top, total))
        rows = pl.ds(block * BLOCK, BLOCK)
        att_ref[rows, :] = jnp.where(low_lanes, halves[0][0], halves[1][0]).astype(att_ref.dtype)
        top_ref[rows, :] = jnp.where(low_lanes, halves[0][1], halves[1][1])
        total_ref[rows, :] = jnp.where(low_lanes, halves[0][2], halves[1][2])


def attention_forward(query_rows, padded_k, padded_v, coarse_k, coarse_v, counts, fine_ok, far_ok):
    tokens, width = query_rows.shape
    lanes = 2 * HEAD_DIM
    by_pair = lambda rows: pl.BlockSpec((rows, lanes), lambda pair: (0, pair))
    whole = lambda shape: pl.BlockSpec(shape, lambda pair: (0, 0))
    stat = jax.ShapeDtypeStruct((tokens, width), jnp.float32)
    return pl.pallas_call(
        forward_kernel,
        grid=(width // lanes,),
        in_specs=[
            by_pair(tokens),
            by_pair(padded_k.shape[0]),
            by_pair(padded_v.shape[0]),
            by_pair(coarse_k.shape[0]),
            by_pair(coarse_v.shape[0]),
            whole(counts.shape),
            whole(fine_ok.shape),
            whole(far_ok.shape),
        ],
        out_specs=[by_pair(tokens), by_pair(tokens), by_pair(tokens)],
        out_shape=[jax.ShapeDtypeStruct((tokens, width), jnp.bfloat16), stat, stat],
    )(query_rows, padded_k, padded_v, coarse_k, coarse_v, counts, fine_ok, far_ok)


def block_windows(padded, local_blocks):
    return jnp.concatenate(
        [padded[0:local_blocks], padded[1 : local_blocks + 1], padded[2 : local_blocks + 2]], axis=1
    )


def fold_windows(grads, local_blocks):
    parts = grads.reshape((local_blocks, 3, BLOCK) + grads.shape[2:])
    edge_zero = jnp.zeros((1,) + parts.shape[2:], jnp.float32)
    left_part = jnp.concatenate([parts[:, 0], edge_zero, edge_zero], axis=0)
    middle = jnp.concatenate([edge_zero, parts[:, 1], edge_zero], axis=0)
    right_part = jnp.concatenate([edge_zero, edge_zero, parts[:, 2]], axis=0)
    return left_part + middle + right_part


def per_device(queries, keys, values, out_weight, out_grad, pooled):
    query_rows = queries[0]
    key_rows = keys[0]
    value_rows = values[0]
    grad_out = out_grad[0]
    tokens, model_width = query_rows.shape
    local_blocks = tokens // BLOCK
    seq_devices = lax.axis_size("seq")
    seq_index = lax.axis_index("seq")
    all_blocks = local_blocks * seq_devices
    score_scale = 1.0 / math.sqrt(HEAD_DIM)
    pooled_mask = pooled[0].reshape(local_blocks, BLOCK).astype(jnp.float32)
    counts = jnp.sum(pooled_mask, axis=1)
    divisor = jnp.maximum(counts, 1.0)
    pooled_bf = pooled_mask.astype(jnp.bfloat16)
    key_sum = jnp.einsum(
        "nb,nbd->nd",
        pooled_bf,
        key_rows.reshape(local_blocks, BLOCK, model_width),
        preferred_element_type=jnp.float32,
    )
    value_sum = jnp.einsum(
        "nb,nbd->nd",
        pooled_bf,
        value_rows.reshape(local_blocks, BLOCK, model_width),
        preferred_element_type=jnp.float32,
    )
    coarse_keys = (key_sum / divisor[:, None]).astype(jnp.bfloat16)
    coarse_values = (value_sum / divisor[:, None]).astype(jnp.bfloat16)
    count_cols = jnp.broadcast_to(counts.astype(jnp.bfloat16)[:, None], (local_blocks, 128))
    packed = jnp.concatenate([coarse_keys, coarse_values, count_cols], axis=1)
    gathered = doubling_gather(packed, "seq").reshape(all_blocks, packed.shape[1])
    gathered_keys = gathered[:, :model_width]
    gathered_values = gathered[:, model_width : 2 * model_width]
    gathered_counts = gathered[:, 2 * model_width].astype(jnp.float32)
    paired = jnp.stack([key_rows, value_rows])
    extended = padded_2(paired, (("seq", 1),), BLOCK)
    padded_kv = extended.reshape(2, local_blocks + 2, BLOCK, HEADS, HEAD_DIM)
    key_win = block_windows(padded_kv[0], local_blocks)
    value_win = block_windows(padded_kv[1], local_blocks)
    query_blk = query_rows.reshape(local_blocks, BLOCK, HEADS, HEAD_DIM)
    coarse_kh = gathered_keys.reshape(all_blocks, HEADS, HEAD_DIM)
    coarse_vh = gathered_values.reshape(all_blocks, HEADS, HEAD_DIM)
    local_ids = seq_index * local_blocks + jnp.arange(local_blocks)
    offsets = jnp.repeat(jnp.arange(3) - 1, BLOCK)
    key_blocks = local_ids[:, None] + offsets[None, :]
    fine_ok = (key_blocks >= 0) & (key_blocks < all_blocks)
    far_ok = jnp.abs(local_ids[:, None] - jnp.arange(all_blocks)[None, :]) >= 2
    fine_s = (
        jnp.einsum("nqhe,nkhe->nhqk", query_blk, key_win, preferred_element_type=jnp.float32)
        * score_scale
    )
    coarse_s = (
        jnp.einsum("nqhe,che->nhqc", query_blk, coarse_kh, preferred_element_type=jnp.float32)
        * score_scale
    )
    fine_s = jnp.where(fine_ok[:, None, None, :], fine_s, -jnp.inf)
    coarse_s = jnp.where(far_ok[:, None, None, :], coarse_s, -jnp.inf)
    padded_rows = extended.reshape(2, (local_blocks + 2) * BLOCK, model_width)
    attended_rows, top_rows, total_rows = attention_forward(
        query_rows,
        padded_rows[0],
        padded_rows[1],
        gathered_keys,
        gathered_values,
        gathered_counts[None, :],
        fine_ok.astype(jnp.float32),
        far_ok.astype(jnp.float32),
    )
    attended = attended_rows.reshape(local_blocks, BLOCK, HEADS, HEAD_DIM)
    head_stat = lambda rows: rows.reshape(local_blocks, BLOCK, HEADS, HEAD_DIM)[..., 0].transpose(0, 2, 1)[..., None]
    row_top = head_stat(top_rows)
    row_total = head_stat(total_rows)
    fine_w = jnp.exp(fine_s - row_top) / row_total
    coarse_w = gathered_counts * jnp.exp(coarse_s - row_top) / row_total
    fine_wb = fine_w.astype(jnp.bfloat16)
    coarse_wb = coarse_w.astype(jnp.bfloat16)
    attended_grad = jnp.dot(grad_out, out_weight, preferred_element_type=jnp.float32).astype(
        jnp.bfloat16
    )
    grad_norm = 1.0 / math.sqrt(seq_devices * tokens)
    full_term = (
        jnp.einsum("to,ti->oi", grad_out, attended_rows, preferred_element_type=jnp.float32)
        * grad_norm
    )
    seq_part = lax.psum_scatter(
        jnp.pad(full_term, ((0, 0), (0, model_width))), "seq", scatter_dimension=0, tiled=True
    )[:, :model_width]
    full_term, attended_grad = lax.optimization_barrier((full_term, attended_grad))
    grad_blk = attended_grad.reshape(local_blocks, BLOCK, HEADS, HEAD_DIM)
    fine_dot = jnp.einsum(
        "nqhe,nkhe->nhqk", grad_blk, value_win, preferred_element_type=jnp.float32
    )
    coarse_dot = jnp.einsum(
        "nqhe,che->nhqc", grad_blk, coarse_vh, preferred_element_type=jnp.float32
    )
    delta_rows = jnp.einsum(
        "nqhe,nqhe->nhq", grad_blk, attended, preferred_element_type=jnp.float32
    )[..., None]
    fine_ds = (fine_w * (fine_dot - delta_rows)).astype(jnp.bfloat16)
    coarse_ds = (coarse_w * (coarse_dot - delta_rows)).astype(jnp.bfloat16)
    query_grad = (
        jnp.einsum("nhqk,nkhe->nqhe", fine_ds, key_win, preferred_element_type=jnp.float32)
        + jnp.einsum("nhqc,che->nqhe", coarse_ds, coarse_kh, preferred_element_type=jnp.float32)
    ) * score_scale
    query_grad = query_grad.astype(jnp.bfloat16).reshape(1, tokens, model_width)
    key_win_grad = (
        jnp.einsum("nhqk,nqhe->nkhe", fine_ds, query_blk, preferred_element_type=jnp.float32)
        * score_scale
    )
    value_win_grad = jnp.einsum(
        "nhqk,nqhe->nkhe", fine_wb, grad_blk, preferred_element_type=jnp.float32
    )
    key_ext = fold_windows(key_win_grad, local_blocks).reshape(local_blocks + 2, BLOCK, model_width)
    value_ext = fold_windows(value_win_grad, local_blocks).reshape(
        local_blocks + 2, BLOCK, model_width
    )
    edge_first = jnp.stack([key_ext[0], value_ext[0]])
    edge_last = jnp.stack([key_ext[local_blocks + 1], value_ext[local_blocks + 1]])
    from_right = from_behind(edge_first, "seq", -1)
    from_left = from_behind(edge_last, "seq", 1)
    zeros_mid = jnp.zeros((2, local_blocks - 1, BLOCK, model_width), jnp.float32)
    boundary = jnp.concatenate([from_left[:, None], zeros_mid], axis=1) + jnp.concatenate(
        [zeros_mid, from_right[:, None]], axis=1
    )
    coarse_key_all = (
        jnp.einsum("nhqc,nqhe->che", coarse_ds, query_blk, preferred_element_type=jnp.float32)
        * score_scale
    )
    coarse_value_all = jnp.einsum(
        "nhqc,nqhe->che", coarse_wb, grad_blk, preferred_element_type=jnp.float32
    )
    coarse_all = jnp.concatenate(
        [
            coarse_key_all.reshape(all_blocks, model_width),
            coarse_value_all.reshape(all_blocks, model_width),
        ],
        axis=1,
    )
    owned_grads = halving_scatter(
        coarse_all.reshape(seq_devices, local_blocks, 2 * model_width), "seq"
    )
    owned_keys = owned_grads[:, :model_width] / divisor[:, None]
    owned_values = owned_grads[:, model_width:] / divisor[:, None]
    spread_keys = owned_keys[:, None, :] * pooled_mask[:, :, None]
    spread_values = owned_values[:, None, :] * pooled_mask[:, :, None]
    key_grad = (
        (key_ext[1 : local_blocks + 1] + boundary[0] + spread_keys)
        .astype(jnp.bfloat16)
        .reshape(1, tokens, model_width)
    )
    value_grad = (
        (value_ext[1 : local_blocks + 1] + boundary[1] + spread_values)
        .astype(jnp.bfloat16)
        .reshape(1, tokens, model_width)
    )
    seq_part, query_grad, key_grad, value_grad = lax.optimization_barrier(
        (seq_part, query_grad, key_grad, value_grad)
    )
    dp_devices = lax.axis_size("dp")
    dp_rows = halving_scatter(seq_part.reshape(dp_devices, -1, model_width), "dp")
    weight_grad = doubling_gather(dp_rows, "dp").reshape(-1, model_width)
    return (query_grad, key_grad, value_grad, weight_grad)


def solution(mesh):
    placed = (
        P("dp", "seq", None),
        P("dp", "seq", None),
        P("dp", "seq", None),
        P(),
        P("dp", "seq", None),
        P("dp", "seq"),
    )
    return jax.shard_map(
        per_device,
        mesh=mesh,
        in_specs=placed,
        out_specs=(
            P("dp", "seq", None),
            P("dp", "seq", None),
            P("dp", "seq", None),
            P("seq", None),
        ),
        check_vma=False,
    )
```

```python
import math

import jax
import jax.numpy as jnp
from jax import lax
from jax.experimental import pallas as pl
from jax.experimental.pallas import tpu as pltpu
from jax.sharding import PartitionSpec as P

HEADS = 16
HEAD_DIM = 64
BLOCK = 128


def padded_2(block, sides, width):
    for axis, dim in sides:
        count = lax.axis_size(axis)
        forward = [(i, i + 1) for i in range(count - 1)]
        backward = [(target, source) for source, target in forward]
        low = lax.ppermute(
            lax.slice_in_dim(block, block.shape[dim] - width, None, axis=dim), axis, forward
        )
        high = lax.ppermute(lax.slice_in_dim(block, 0, width, axis=dim), axis, backward)
        block = jnp.concatenate([low, block, high], axis=dim)
    return block


def from_behind(value, axis, steps):
    count = lax.axis_size(axis)
    leading, last = (max(0, -steps), min(count, count - steps))
    return lax.ppermute(value, axis, [(source, source + steps) for source in range(leading, last)])


def xor_pairs(count, bit):
    return [(source, source ^ (1 << bit)) for source in range(count)]


def own_bit(axis, bit):
    return (lax.axis_index(axis) // (1 << bit)) % 2


def doubling_gather(piece, axis):
    count = lax.axis_size(axis)
    bits = count.bit_length() - 1
    held = piece
    for done, bit in enumerate(reversed(range(bits))):
        other = lax.ppermute(held, axis, xor_pairs(count, bit))
        mine_low = own_bit(axis, bit) == 0
        low = jnp.where(mine_low, held, other)
        high = jnp.where(mine_low, other, held)
        held = jnp.stack([low, high], axis=done)
    return held.reshape((count,) + piece.shape)


def halving_scatter(stack, axis):
    count = lax.axis_size(axis)
    bits = count.bit_length() - 1
    held = stack.reshape((2,) * bits + stack.shape[1:])
    for bit in range(bits):
        dim = bits - 1 - bit
        mine = own_bit(axis, bit)
        keep = lax.dynamic_index_in_dim(held, mine, dim, keepdims=False)
        send = lax.dynamic_index_in_dim(held, 1 - mine, dim, keepdims=False)
        held = keep + lax.ppermute(send, axis, xor_pairs(count, bit))
    return held


def doubling_sum(value, axis):
    count = lax.axis_size(axis)
    for bit in range(count.bit_length() - 1):
        value = value + lax.ppermute(value, axis, xor_pairs(count, bit))
    return value


def forward_kernel(q_ref, k_ref, v_ref, ck_ref, cv_ref, counts_ref, fine_ref, far_ref,
                   att_ref, top_ref, total_ref):
    score_scale = 1.0 / math.sqrt(HEAD_DIM)
    lanes = q_ref.shape[1]
    low_lanes = lax.broadcasted_iota(jnp.int32, (BLOCK, lanes), 1) < HEAD_DIM
    coarse_k = ck_ref[...]
    coarse_v = cv_ref[...]
    counts = counts_ref[...]
    contract_last = (((1,), (1,)), ((), ()))
    for block in range(q_ref.shape[0] // BLOCK):
        query = q_ref[pl.ds(block * BLOCK, BLOCK), :]
        key_win = k_ref[pl.ds(block * BLOCK, 3 * BLOCK), :]
        value_win = v_ref[pl.ds(block * BLOCK, 3 * BLOCK), :]
        fine_ok = fine_ref[pl.ds(block, 1), :] > 0
        far_ok = far_ref[pl.ds(block, 1), :] > 0
        halves = []
        for half in range(2):
            own = low_lanes if half == 0 else jnp.logical_not(low_lanes)
            query_h = jnp.where(own, query, jnp.zeros_like(query))
            fine_s = lax.dot_general(query_h, key_win, contract_last,
                                     preferred_element_type=jnp.float32) * score_scale
            coarse_s = lax.dot_general(query_h, coarse_k, contract_last,
                                       preferred_element_type=jnp.float32) * score_scale
            fine_s = jnp.where(fine_ok, fine_s, -jnp.inf)
            coarse_s = jnp.where(far_ok, coarse_s, -jnp.inf)
            top = jnp.maximum(jnp.max(fine_s, axis=1, keepdims=True),
                              jnp.max(coarse_s, axis=1, keepdims=True))
            fine_e = jnp.exp(fine_s - top)
            coarse_e = counts * jnp.exp(coarse_s - top)
            total = (jnp.sum(fine_e, axis=1, keepdims=True)
                     + jnp.sum(coarse_e, axis=1, keepdims=True))
            fine_w = (fine_e / total).astype(jnp.bfloat16)
            coarse_w = (coarse_e / total).astype(jnp.bfloat16)
            att = (jnp.dot(fine_w, value_win, preferred_element_type=jnp.float32)
                   + jnp.dot(coarse_w, coarse_v, preferred_element_type=jnp.float32))
            halves.append((att, top, total))
        rows = pl.ds(block * BLOCK, BLOCK)
        att_ref[rows, :] = jnp.where(low_lanes, halves[0][0], halves[1][0]).astype(att_ref.dtype)
        top_ref[rows, :] = jnp.where(low_lanes, halves[0][1], halves[1][1])
        total_ref[rows, :] = jnp.where(low_lanes, halves[0][2], halves[1][2])


def attention_forward(query_rows, padded_k, padded_v, coarse_k, coarse_v, counts, fine_ok, far_ok):
    tokens, width = query_rows.shape
    lanes = 2 * HEAD_DIM
    by_pair = lambda rows: pl.BlockSpec((rows, lanes), lambda pair: (0, pair))
    whole = lambda shape: pl.BlockSpec(shape, lambda pair: (0, 0))
    stat = jax.ShapeDtypeStruct((tokens, width), jnp.float32)
    return pl.pallas_call(
        forward_kernel,
        grid=(width // lanes,),
        in_specs=[
            by_pair(tokens),
            by_pair(padded_k.shape[0]),
            by_pair(padded_v.shape[0]),
            by_pair(coarse_k.shape[0]),
            by_pair(coarse_v.shape[0]),
            whole(counts.shape),
            whole(fine_ok.shape),
            whole(far_ok.shape),
        ],
        out_specs=[by_pair(tokens), by_pair(tokens), by_pair(tokens)],
        out_shape=[jax.ShapeDtypeStruct((tokens, width), jnp.bfloat16), stat, stat],
    )(query_rows, padded_k, padded_v, coarse_k, coarse_v, counts, fine_ok, far_ok)


def backward_kernel(q_ref, k_ref, v_ref, ck_ref, cv_ref, counts_ref, fine_ref, far_ref,
                    g_ref, att_ref, qg_ref, kg_ref, vg_ref, ckg_ref, cvg_ref):
    score_scale = 1.0 / math.sqrt(HEAD_DIM)
    lanes = q_ref.shape[1]
    low_lanes = lax.broadcasted_iota(jnp.int32, (BLOCK, lanes), 1) < HEAD_DIM
    coarse_k = ck_ref[...]
    coarse_v = cv_ref[...]
    counts = counts_ref[...]
    contract_last = (((1,), (1,)), ((), ()))
    kg_ref[...] = jnp.zeros_like(kg_ref)
    vg_ref[...] = jnp.zeros_like(vg_ref)
    coarse_kg = jnp.zeros(ckg_ref.shape, jnp.float32)
    coarse_vg = jnp.zeros(cvg_ref.shape, jnp.float32)
    for block in range(q_ref.shape[0] // BLOCK):
        rows = pl.ds(block * BLOCK, BLOCK)
        window = pl.ds(block * BLOCK, 3 * BLOCK)
        query = q_ref[rows, :]
        grad = g_ref[rows, :]
        att = att_ref[rows, :].astype(jnp.float32)
        key_win = k_ref[window, :]
        value_win = v_ref[window, :]
        fine_ok = fine_ref[pl.ds(block, 1), :] > 0
        far_ok = far_ref[pl.ds(block, 1), :] > 0
        query_grads = []
        key_grad = jnp.zeros((3 * BLOCK, lanes), jnp.float32)
        value_grad = jnp.zeros((3 * BLOCK, lanes), jnp.float32)
        for half in range(2):
            own = low_lanes if half == 0 else jnp.logical_not(low_lanes)
            query_h = jnp.where(own, query, jnp.zeros_like(query))
            grad_h = jnp.where(own, grad, jnp.zeros_like(grad))
            fine_s = lax.dot_general(query_h, key_win, contract_last,
                                     preferred_element_type=jnp.float32) * score_scale
            coarse_s = lax.dot_general(query_h, coarse_k, contract_last,
                                       preferred_element_type=jnp.float32) * score_scale
            fine_s = jnp.where(fine_ok, fine_s, -jnp.inf)
            coarse_s = jnp.where(far_ok, coarse_s, -jnp.inf)
            top = jnp.maximum(jnp.max(fine_s, axis=1, keepdims=True),
                              jnp.max(coarse_s, axis=1, keepdims=True))
            fine_e = jnp.exp(fine_s - top)
            coarse_e = counts * jnp.exp(coarse_s - top)
            total = (jnp.sum(fine_e, axis=1, keepdims=True)
                     + jnp.sum(coarse_e, axis=1, keepdims=True))
            fine_w = fine_e / total
            coarse_w = coarse_e / total
            fine_dot = lax.dot_general(grad_h, value_win, contract_last,
                                       preferred_element_type=jnp.float32)
            coarse_dot = lax.dot_general(grad_h, coarse_v, contract_last,
                                         preferred_element_type=jnp.float32)
            delta = jnp.sum(jnp.where(own, grad.astype(jnp.float32) * att, 0.0),
                            axis=1, keepdims=True)
            fine_ds = fine_w * (fine_dot - delta)
            coarse_ds = coarse_w * (coarse_dot - delta)
            fine_ds_b = fine_ds.astype(jnp.bfloat16)
            coarse_ds_b = coarse_ds.astype(jnp.bfloat16)
            query_grads.append(
                (jnp.dot(fine_ds_b, key_win, preferred_element_type=jnp.float32)
                 + jnp.dot(coarse_ds_b, coarse_k, preferred_element_type=jnp.float32))
                * score_scale)
            fine_ds_t = fine_ds.T.astype(jnp.bfloat16)
            coarse_ds_t = coarse_ds.T.astype(jnp.bfloat16)
            fine_w_t = fine_w.T.astype(jnp.bfloat16)
            coarse_w_t = coarse_w.T.astype(jnp.bfloat16)
            key_grad = key_grad + jnp.dot(fine_ds_t, query_h,
                                          preferred_element_type=jnp.float32) * score_scale
            value_grad = value_grad + jnp.dot(fine_w_t, grad_h,
                                              preferred_element_type=jnp.float32)
            coarse_kg = coarse_kg + jnp.dot(coarse_ds_t, query_h,
                                            preferred_element_type=jnp.float32) * score_scale
            coarse_vg = coarse_vg + jnp.dot(coarse_w_t, grad_h,
                                            preferred_element_type=jnp.float32)
        qg_ref[rows, :] = jnp.where(low_lanes, query_grads[0], query_grads[1]).astype(qg_ref.dtype)
        kg_ref[window, :] += key_grad
        vg_ref[window, :] += value_grad
    ckg_ref[...] = coarse_kg
    cvg_ref[...] = coarse_vg


def attention_backward(query_rows, padded_k, padded_v, coarse_k, coarse_v, counts, fine_ok,
                       far_ok, grad_rows, attended_rows):
    tokens, width = query_rows.shape
    lanes = 2 * HEAD_DIM
    by_pair = lambda rows: pl.BlockSpec((rows, lanes), lambda pair: (0, pair))
    whole = lambda shape: pl.BlockSpec(shape, lambda pair: (0, 0))
    wide = lambda rows: jax.ShapeDtypeStruct((rows, width), jnp.float32)
    return pl.pallas_call(
        backward_kernel,
        grid=(width // lanes,),
        in_specs=[
            by_pair(tokens),
            by_pair(padded_k.shape[0]),
            by_pair(padded_v.shape[0]),
            by_pair(coarse_k.shape[0]),
            by_pair(coarse_v.shape[0]),
            whole(counts.shape),
            whole(fine_ok.shape),
            whole(far_ok.shape),
            by_pair(tokens),
            by_pair(tokens),
        ],
        out_specs=[
            by_pair(tokens),
            by_pair(padded_k.shape[0]),
            by_pair(padded_v.shape[0]),
            by_pair(coarse_k.shape[0]),
            by_pair(coarse_v.shape[0]),
        ],
        out_shape=[
            jax.ShapeDtypeStruct((tokens, width), jnp.bfloat16),
            wide(padded_k.shape[0]),
            wide(padded_v.shape[0]),
            wide(coarse_k.shape[0]),
            wide(coarse_v.shape[0]),
        ],
    )(query_rows, padded_k, padded_v, coarse_k, coarse_v, counts, fine_ok, far_ok, grad_rows,
      attended_rows)


def block_windows(padded, local_blocks):
    return jnp.concatenate(
        [padded[0:local_blocks], padded[1 : local_blocks + 1], padded[2 : local_blocks + 2]], axis=1
    )


def fold_windows(grads, local_blocks):
    parts = grads.reshape((local_blocks, 3, BLOCK) + grads.shape[2:])
    edge_zero = jnp.zeros((1,) + parts.shape[2:], jnp.float32)
    left_part = jnp.concatenate([parts[:, 0], edge_zero, edge_zero], axis=0)
    middle = jnp.concatenate([edge_zero, parts[:, 1], edge_zero], axis=0)
    right_part = jnp.concatenate([edge_zero, edge_zero, parts[:, 2]], axis=0)
    return left_part + middle + right_part


def per_device(queries, keys, values, out_weight, out_grad, pooled):
    query_rows = queries[0]
    key_rows = keys[0]
    value_rows = values[0]
    grad_out = out_grad[0]
    tokens, model_width = query_rows.shape
    local_blocks = tokens // BLOCK
    seq_devices = lax.axis_size("seq")
    seq_index = lax.axis_index("seq")
    all_blocks = local_blocks * seq_devices
    score_scale = 1.0 / math.sqrt(HEAD_DIM)
    pooled_mask = pooled[0].reshape(local_blocks, BLOCK).astype(jnp.float32)
    counts = jnp.sum(pooled_mask, axis=1)
    divisor = jnp.maximum(counts, 1.0)
    pooled_bf = pooled_mask.astype(jnp.bfloat16)
    key_sum = jnp.einsum(
        "nb,nbd->nd",
        pooled_bf,
        key_rows.reshape(local_blocks, BLOCK, model_width),
        preferred_element_type=jnp.float32,
    )
    value_sum = jnp.einsum(
        "nb,nbd->nd",
        pooled_bf,
        value_rows.reshape(local_blocks, BLOCK, model_width),
        preferred_element_type=jnp.float32,
    )
    coarse_keys = (key_sum / divisor[:, None]).astype(jnp.bfloat16)
    coarse_values = (value_sum / divisor[:, None]).astype(jnp.bfloat16)
    count_cols = jnp.broadcast_to(counts.astype(jnp.bfloat16)[:, None], (local_blocks, 128))
    packed = jnp.concatenate([coarse_keys, coarse_values, count_cols], axis=1)
    gathered = doubling_gather(packed, "seq").reshape(all_blocks, packed.shape[1])
    gathered_keys = gathered[:, :model_width]
    gathered_values = gathered[:, model_width : 2 * model_width]
    gathered_counts = gathered[:, 2 * model_width].astype(jnp.float32)
    paired = jnp.stack([key_rows, value_rows])
    extended = padded_2(paired, (("seq", 1),), BLOCK)
    padded_kv = extended.reshape(2, local_blocks + 2, BLOCK, HEADS, HEAD_DIM)
    key_win = block_windows(padded_kv[0], local_blocks)
    value_win = block_windows(padded_kv[1], local_blocks)
    query_blk = query_rows.reshape(local_blocks, BLOCK, HEADS, HEAD_DIM)
    coarse_kh = gathered_keys.reshape(all_blocks, HEADS, HEAD_DIM)
    coarse_vh = gathered_values.reshape(all_blocks, HEADS, HEAD_DIM)
    local_ids = seq_index * local_blocks + jnp.arange(local_blocks)
    offsets = jnp.repeat(jnp.arange(3) - 1, BLOCK)
    key_blocks = local_ids[:, None] + offsets[None, :]
    fine_ok = (key_blocks >= 0) & (key_blocks < all_blocks)
    far_ok = jnp.abs(local_ids[:, None] - jnp.arange(all_blocks)[None, :]) >= 2
    fine_s = (
        jnp.einsum("nqhe,nkhe->nhqk", query_blk, key_win, preferred_element_type=jnp.float32)
        * score_scale
    )
    coarse_s = (
        jnp.einsum("nqhe,che->nhqc", query_blk, coarse_kh, preferred_element_type=jnp.float32)
        * score_scale
    )
    fine_s = jnp.where(fine_ok[:, None, None, :], fine_s, -jnp.inf)
    coarse_s = jnp.where(far_ok[:, None, None, :], coarse_s, -jnp.inf)
    padded_rows = extended.reshape(2, (local_blocks + 2) * BLOCK, model_width)
    attended_rows, top_rows, total_rows = attention_forward(
        query_rows,
        padded_rows[0],
        padded_rows[1],
        gathered_keys,
        gathered_values,
        gathered_counts[None, :],
        fine_ok.astype(jnp.float32),
        far_ok.astype(jnp.float32),
    )
    attended = attended_rows.reshape(local_blocks, BLOCK, HEADS, HEAD_DIM)
    head_stat = lambda rows: rows.reshape(local_blocks, BLOCK, HEADS, HEAD_DIM)[..., 0].transpose(0, 2, 1)[..., None]
    row_top = head_stat(top_rows)
    row_total = head_stat(total_rows)
    fine_w = jnp.exp(fine_s - row_top) / row_total
    coarse_w = gathered_counts * jnp.exp(coarse_s - row_top) / row_total
    fine_wb = fine_w.astype(jnp.bfloat16)
    coarse_wb = coarse_w.astype(jnp.bfloat16)
    attended_grad = jnp.dot(grad_out, out_weight, preferred_element_type=jnp.float32).astype(
        jnp.bfloat16
    )
    grad_norm = 1.0 / math.sqrt(seq_devices * tokens)
    full_term = (
        jnp.einsum("to,ti->oi", grad_out, attended_rows, preferred_element_type=jnp.float32)
        * grad_norm
    )
    seq_part = lax.psum_scatter(
        jnp.pad(full_term, ((0, 0), (0, model_width))), "seq", scatter_dimension=0, tiled=True
    )[:, :model_width]
    full_term, attended_grad = lax.optimization_barrier((full_term, attended_grad))
    query_grad, key_pad, value_pad, coarse_key_all, coarse_value_all = attention_backward(
        query_rows,
        padded_rows[0],
        padded_rows[1],
        gathered_keys,
        gathered_values,
        gathered_counts[None, :],
        fine_ok.astype(jnp.float32),
        far_ok.astype(jnp.float32),
        attended_grad,
        attended_rows,
    )
    query_grad = query_grad.reshape(1, tokens, model_width)
    key_ext = key_pad.reshape(local_blocks + 2, BLOCK, model_width)
    value_ext = value_pad.reshape(local_blocks + 2, BLOCK, model_width)
    edge_first = jnp.stack([key_ext[0], value_ext[0]])
    edge_last = jnp.stack([key_ext[local_blocks + 1], value_ext[local_blocks + 1]])
    from_right = from_behind(edge_first, "seq", -1)
    from_left = from_behind(edge_last, "seq", 1)
    zeros_mid = jnp.zeros((2, local_blocks - 1, BLOCK, model_width), jnp.float32)
    boundary = jnp.concatenate([from_left[:, None], zeros_mid], axis=1) + jnp.concatenate(
        [zeros_mid, from_right[:, None]], axis=1
    )
    coarse_all = jnp.concatenate(
        [
            coarse_key_all.reshape(all_blocks, model_width),
            coarse_value_all.reshape(all_blocks, model_width),
        ],
        axis=1,
    )
    owned_grads = halving_scatter(
        coarse_all.reshape(seq_devices, local_blocks, 2 * model_width), "seq"
    )
    owned_keys = owned_grads[:, :model_width] / divisor[:, None]
    owned_values = owned_grads[:, model_width:] / divisor[:, None]
    spread_keys = owned_keys[:, None, :] * pooled_mask[:, :, None]
    spread_values = owned_values[:, None, :] * pooled_mask[:, :, None]
    key_grad = (
        (key_ext[1 : local_blocks + 1] + boundary[0] + spread_keys)
        .astype(jnp.bfloat16)
        .reshape(1, tokens, model_width)
    )
    value_grad = (
        (value_ext[1 : local_blocks + 1] + boundary[1] + spread_values)
        .astype(jnp.bfloat16)
        .reshape(1, tokens, model_width)
    )
    seq_part, query_grad, key_grad, value_grad = lax.optimization_barrier(
        (seq_part, query_grad, key_grad, value_grad)
    )
    dp_devices = lax.axis_size("dp")
    dp_rows = halving_scatter(seq_part.reshape(dp_devices, -1, model_width), "dp")
    weight_grad = doubling_gather(dp_rows, "dp").reshape(-1, model_width)
    return (query_grad, key_grad, value_grad, weight_grad)


def solution(mesh):
    placed = (
        P("dp", "seq", None),
        P("dp", "seq", None),
        P("dp", "seq", None),
        P(),
        P("dp", "seq", None),
        P("dp", "seq"),
    )
    return jax.shard_map(
        per_device,
        mesh=mesh,
        in_specs=placed,
        out_specs=(
            P("dp", "seq", None),
            P("dp", "seq", None),
            P("dp", "seq", None),
            P("seq", None),
        ),
        check_vma=False,
    )
```

```python
import functools
import math

import jax
import jax.numpy as jnp
from jax import lax
from jax.experimental import pallas as pl
from jax.experimental.pallas import tpu as pltpu
from jax.sharding import PartitionSpec as P

HEADS = 16
HEAD_DIM = 64
BLOCK = 128


def padded_2(block, sides, width):
    for axis, dim in sides:
        count = lax.axis_size(axis)
        forward = [(i, i + 1) for i in range(count - 1)]
        backward = [(target, source) for source, target in forward]
        low = lax.ppermute(
            lax.slice_in_dim(block, block.shape[dim] - width, None, axis=dim), axis, forward
        )
        high = lax.ppermute(lax.slice_in_dim(block, 0, width, axis=dim), axis, backward)
        block = jnp.concatenate([low, block, high], axis=dim)
    return block


def from_behind(value, axis, steps):
    count = lax.axis_size(axis)
    leading, last = (max(0, -steps), min(count, count - steps))
    return lax.ppermute(value, axis, [(source, source + steps) for source in range(leading, last)])


def xor_pairs(count, bit):
    return [(source, source ^ (1 << bit)) for source in range(count)]


def own_bit(axis, bit):
    return (lax.axis_index(axis) // (1 << bit)) % 2


def doubling_gather(piece, axis):
    count = lax.axis_size(axis)
    bits = count.bit_length() - 1
    held = piece
    for done, bit in enumerate(reversed(range(bits))):
        other = lax.ppermute(held, axis, xor_pairs(count, bit))
        mine_low = own_bit(axis, bit) == 0
        low = jnp.where(mine_low, held, other)
        high = jnp.where(mine_low, other, held)
        held = jnp.stack([low, high], axis=done)
    return held.reshape((count,) + piece.shape)


def halving_scatter(stack, axis):
    count = lax.axis_size(axis)
    bits = count.bit_length() - 1
    held = stack.reshape((2,) * bits + stack.shape[1:])
    for bit in range(bits):
        dim = bits - 1 - bit
        mine = own_bit(axis, bit)
        keep = lax.dynamic_index_in_dim(held, mine, dim, keepdims=False)
        send = lax.dynamic_index_in_dim(held, 1 - mine, dim, keepdims=False)
        held = keep + lax.ppermute(send, axis, xor_pairs(count, bit))
    return held


def doubling_sum(value, axis):
    count = lax.axis_size(axis)
    for bit in range(count.bit_length() - 1):
        value = value + lax.ppermute(value, axis, xor_pairs(count, bit))
    return value


def forward_kernel(term_scale, q_ref, k_ref, v_ref, ck_ref, cv_ref, counts_ref, fine_ref, far_ref,
                   grad_t_ref, att_ref, term_ref):
    score_scale = 1.0 / math.sqrt(HEAD_DIM)
    lanes = q_ref.shape[1]
    low_lanes = lax.broadcasted_iota(jnp.int32, (BLOCK, lanes), 1) < HEAD_DIM
    coarse_k = ck_ref[...]
    coarse_v = cv_ref[...]
    counts = counts_ref[...]
    contract_last = (((1,), (1,)), ((), ()))
    for block in range(q_ref.shape[0] // BLOCK):
        query = q_ref[pl.ds(block * BLOCK, BLOCK), :]
        key_win = k_ref[pl.ds(block * BLOCK, 3 * BLOCK), :]
        value_win = v_ref[pl.ds(block * BLOCK, 3 * BLOCK), :]
        fine_ok = fine_ref[pl.ds(block, 1), :] > 0
        far_ok = far_ref[pl.ds(block, 1), :] > 0
        halves = []
        for half in range(2):
            own = low_lanes if half == 0 else jnp.logical_not(low_lanes)
            query_h = jnp.where(own, query, jnp.zeros_like(query))
            fine_s = lax.dot_general(query_h, key_win, contract_last,
                                     preferred_element_type=jnp.float32) * score_scale
            coarse_s = lax.dot_general(query_h, coarse_k, contract_last,
                                       preferred_element_type=jnp.float32) * score_scale
            fine_s = jnp.where(fine_ok, fine_s, -jnp.inf)
            coarse_s = jnp.where(far_ok, coarse_s, -jnp.inf)
            top = jnp.maximum(jnp.max(fine_s, axis=1, keepdims=True),
                              jnp.max(coarse_s, axis=1, keepdims=True))
            fine_e = jnp.exp(fine_s - top)
            coarse_e = counts * jnp.exp(coarse_s - top)
            total = (jnp.sum(fine_e, axis=1, keepdims=True)
                     + jnp.sum(coarse_e, axis=1, keepdims=True))
            fine_w = (fine_e / total).astype(jnp.bfloat16)
            coarse_w = (coarse_e / total).astype(jnp.bfloat16)
            att = (jnp.dot(fine_w, value_win, preferred_element_type=jnp.float32)
                   + jnp.dot(coarse_w, coarse_v, preferred_element_type=jnp.float32))
            halves.append((att, top, total))
        rows = pl.ds(block * BLOCK, BLOCK)
        att_ref[rows, :] = jnp.where(low_lanes, halves[0][0], halves[1][0]).astype(att_ref.dtype)
    term_ref[...] = jnp.dot(grad_t_ref[...], att_ref[...],
                            preferred_element_type=jnp.float32) * term_scale


def attention_forward(query_rows, padded_k, padded_v, coarse_k, coarse_v, counts, fine_ok, far_ok,
                      grad_t, term_scale):
    tokens, width = query_rows.shape
    lanes = 2 * HEAD_DIM
    by_pair = lambda rows: pl.BlockSpec((rows, lanes), lambda pair: (0, pair))
    whole = lambda shape: pl.BlockSpec(shape, lambda pair: (0, 0))
    return pl.pallas_call(
        functools.partial(forward_kernel, term_scale),
        grid=(width // lanes,),
        in_specs=[
            by_pair(tokens),
            by_pair(padded_k.shape[0]),
            by_pair(padded_v.shape[0]),
            by_pair(coarse_k.shape[0]),
            by_pair(coarse_v.shape[0]),
            whole(counts.shape),
            whole(fine_ok.shape),
            whole(far_ok.shape),
            whole(grad_t.shape),
        ],
        out_specs=[by_pair(tokens), by_pair(grad_t.shape[0])],
        out_shape=[
            jax.ShapeDtypeStruct((tokens, width), jnp.bfloat16),
            jax.ShapeDtypeStruct((grad_t.shape[0], width), jnp.float32),
        ],
    )(query_rows, padded_k, padded_v, coarse_k, coarse_v, counts, fine_ok, far_ok, grad_t)


def backward_kernel(q_ref, k_ref, v_ref, ck_ref, cv_ref, counts_ref, fine_ref, far_ref,
                    g_ref, att_ref, qg_ref, kg_ref, vg_ref, ckg_ref, cvg_ref):
    score_scale = 1.0 / math.sqrt(HEAD_DIM)
    lanes = q_ref.shape[1]
    low_lanes = lax.broadcasted_iota(jnp.int32, (BLOCK, lanes), 1) < HEAD_DIM
    coarse_k = ck_ref[...]
    coarse_v = cv_ref[...]
    counts = counts_ref[...]
    contract_last = (((1,), (1,)), ((), ()))
    kg_ref[...] = jnp.zeros_like(kg_ref)
    vg_ref[...] = jnp.zeros_like(vg_ref)
    coarse_kg = jnp.zeros(ckg_ref.shape, jnp.float32)
    coarse_vg = jnp.zeros(cvg_ref.shape, jnp.float32)
    for block in range(q_ref.shape[0] // BLOCK):
        rows = pl.ds(block * BLOCK, BLOCK)
        window = pl.ds(block * BLOCK, 3 * BLOCK)
        query = q_ref[rows, :]
        grad = g_ref[rows, :]
        att = att_ref[rows, :].astype(jnp.float32)
        key_win = k_ref[window, :]
        value_win = v_ref[window, :]
        fine_ok = fine_ref[pl.ds(block, 1), :] > 0
        far_ok = far_ref[pl.ds(block, 1), :] > 0
        query_grads = []
        key_grad = jnp.zeros((3 * BLOCK, lanes), jnp.float32)
        value_grad = jnp.zeros((3 * BLOCK, lanes), jnp.float32)
        for half in range(2):
            own = low_lanes if half == 0 else jnp.logical_not(low_lanes)
            query_h = jnp.where(own, query, jnp.zeros_like(query))
            grad_h = jnp.where(own, grad, jnp.zeros_like(grad))
            fine_s = lax.dot_general(query_h, key_win, contract_last,
                                     preferred_element_type=jnp.float32) * score_scale
            coarse_s = lax.dot_general(query_h, coarse_k, contract_last,
                                       preferred_element_type=jnp.float32) * score_scale
            fine_s = jnp.where(fine_ok, fine_s, -jnp.inf)
            coarse_s = jnp.where(far_ok, coarse_s, -jnp.inf)
            top = jnp.maximum(jnp.max(fine_s, axis=1, keepdims=True),
                              jnp.max(coarse_s, axis=1, keepdims=True))
            fine_e = jnp.exp(fine_s - top)
            coarse_e = counts * jnp.exp(coarse_s - top)
            total = (jnp.sum(fine_e, axis=1, keepdims=True)
                     + jnp.sum(coarse_e, axis=1, keepdims=True))
            fine_w = fine_e / total
            coarse_w = coarse_e / total
            fine_dot = lax.dot_general(grad_h, value_win, contract_last,
                                       preferred_element_type=jnp.float32)
            coarse_dot = lax.dot_general(grad_h, coarse_v, contract_last,
                                         preferred_element_type=jnp.float32)
            delta = jnp.sum(jnp.where(own, grad.astype(jnp.float32) * att, 0.0),
                            axis=1, keepdims=True)
            fine_ds = fine_w * (fine_dot - delta)
            coarse_ds = coarse_w * (coarse_dot - delta)
            fine_ds_b = fine_ds.astype(jnp.bfloat16)
            coarse_ds_b = coarse_ds.astype(jnp.bfloat16)
            query_grads.append(
                (jnp.dot(fine_ds_b, key_win, preferred_element_type=jnp.float32)
                 + jnp.dot(coarse_ds_b, coarse_k, preferred_element_type=jnp.float32))
                * score_scale)
            fine_ds_t = fine_ds.T.astype(jnp.bfloat16)
            coarse_ds_t = coarse_ds.T.astype(jnp.bfloat16)
            fine_w_t = fine_w.T.astype(jnp.bfloat16)
            coarse_w_t = coarse_w.T.astype(jnp.bfloat16)
            key_grad = key_grad + jnp.dot(fine_ds_t, query_h,
                                          preferred_element_type=jnp.float32) * score_scale
            value_grad = value_grad + jnp.dot(fine_w_t, grad_h,
                                              preferred_element_type=jnp.float32)
            coarse_kg = coarse_kg + jnp.dot(coarse_ds_t, query_h,
                                            preferred_element_type=jnp.float32) * score_scale
            coarse_vg = coarse_vg + jnp.dot(coarse_w_t, grad_h,
                                            preferred_element_type=jnp.float32)
        qg_ref[rows, :] = jnp.where(low_lanes, query_grads[0], query_grads[1]).astype(qg_ref.dtype)
        kg_ref[window, :] += key_grad
        vg_ref[window, :] += value_grad
    ckg_ref[...] = coarse_kg
    cvg_ref[...] = coarse_vg


def attention_backward(query_rows, padded_k, padded_v, coarse_k, coarse_v, counts, fine_ok,
                       far_ok, grad_rows, attended_rows):
    tokens, width = query_rows.shape
    lanes = 2 * HEAD_DIM
    by_pair = lambda rows: pl.BlockSpec((rows, lanes), lambda pair: (0, pair))
    whole = lambda shape: pl.BlockSpec(shape, lambda pair: (0, 0))
    wide = lambda rows: jax.ShapeDtypeStruct((rows, width), jnp.float32)
    return pl.pallas_call(
        backward_kernel,
        grid=(width // lanes,),
        in_specs=[
            by_pair(tokens),
            by_pair(padded_k.shape[0]),
            by_pair(padded_v.shape[0]),
            by_pair(coarse_k.shape[0]),
            by_pair(coarse_v.shape[0]),
            whole(counts.shape),
            whole(fine_ok.shape),
            whole(far_ok.shape),
            by_pair(tokens),
            by_pair(tokens),
        ],
        out_specs=[
            by_pair(tokens),
            by_pair(padded_k.shape[0]),
            by_pair(padded_v.shape[0]),
            by_pair(coarse_k.shape[0]),
            by_pair(coarse_v.shape[0]),
        ],
        out_shape=[
            jax.ShapeDtypeStruct((tokens, width), jnp.bfloat16),
            wide(padded_k.shape[0]),
            wide(padded_v.shape[0]),
            wide(coarse_k.shape[0]),
            wide(coarse_v.shape[0]),
        ],
    )(query_rows, padded_k, padded_v, coarse_k, coarse_v, counts, fine_ok, far_ok, grad_rows,
      attended_rows)


def block_windows(padded, local_blocks):
    return jnp.concatenate(
        [padded[0:local_blocks], padded[1 : local_blocks + 1], padded[2 : local_blocks + 2]], axis=1
    )


def fold_windows(grads, local_blocks):
    parts = grads.reshape((local_blocks, 3, BLOCK) + grads.shape[2:])
    edge_zero = jnp.zeros((1,) + parts.shape[2:], jnp.float32)
    left_part = jnp.concatenate([parts[:, 0], edge_zero, edge_zero], axis=0)
    middle = jnp.concatenate([edge_zero, parts[:, 1], edge_zero], axis=0)
    right_part = jnp.concatenate([edge_zero, edge_zero, parts[:, 2]], axis=0)
    return left_part + middle + right_part


def per_device(queries, keys, values, out_weight, out_grad, pooled):
    query_rows = queries[0]
    key_rows = keys[0]
    value_rows = values[0]
    grad_out = out_grad[0]
    tokens, model_width = query_rows.shape
    local_blocks = tokens // BLOCK
    seq_devices = lax.axis_size("seq")
    seq_index = lax.axis_index("seq")
    all_blocks = local_blocks * seq_devices
    score_scale = 1.0 / math.sqrt(HEAD_DIM)
    pooled_mask = pooled[0].reshape(local_blocks, BLOCK).astype(jnp.float32)
    counts = jnp.sum(pooled_mask, axis=1)
    divisor = jnp.maximum(counts, 1.0)
    pooled_bf = pooled_mask.astype(jnp.bfloat16)
    key_sum = jnp.einsum(
        "nb,nbd->nd",
        pooled_bf,
        key_rows.reshape(local_blocks, BLOCK, model_width),
        preferred_element_type=jnp.float32,
    )
    value_sum = jnp.einsum(
        "nb,nbd->nd",
        pooled_bf,
        value_rows.reshape(local_blocks, BLOCK, model_width),
        preferred_element_type=jnp.float32,
    )
    coarse_keys = (key_sum / divisor[:, None]).astype(jnp.bfloat16)
    coarse_values = (value_sum / divisor[:, None]).astype(jnp.bfloat16)
    count_cols = jnp.broadcast_to(counts.astype(jnp.bfloat16)[:, None], (local_blocks, 128))
    packed = jnp.concatenate([coarse_keys, coarse_values, count_cols], axis=1)
    gathered = doubling_gather(packed, "seq").reshape(all_blocks, packed.shape[1])
    gathered_keys = gathered[:, :model_width]
    gathered_values = gathered[:, model_width : 2 * model_width]
    gathered_counts = gathered[:, 2 * model_width].astype(jnp.float32)
    paired = jnp.stack([key_rows, value_rows])
    extended = padded_2(paired, (("seq", 1),), BLOCK)
    padded_kv = extended.reshape(2, local_blocks + 2, BLOCK, HEADS, HEAD_DIM)
    local_ids = seq_index * local_blocks + jnp.arange(local_blocks)
    offsets = jnp.repeat(jnp.arange(3) - 1, BLOCK)
    key_blocks = local_ids[:, None] + offsets[None, :]
    fine_ok = (key_blocks >= 0) & (key_blocks < all_blocks)
    far_ok = jnp.abs(local_ids[:, None] - jnp.arange(all_blocks)[None, :]) >= 2
    padded_rows = extended.reshape(2, (local_blocks + 2) * BLOCK, model_width)
    grad_norm = 1.0 / math.sqrt(seq_devices * tokens)
    attended_rows, full_term = attention_forward(
        query_rows,
        padded_rows[0],
        padded_rows[1],
        gathered_keys,
        gathered_values,
        gathered_counts[None, :],
        fine_ok.astype(jnp.float32),
        far_ok.astype(jnp.float32),
        grad_out.T,
        grad_norm,
    )
    attended_grad = jnp.dot(grad_out, out_weight, preferred_element_type=jnp.float32).astype(
        jnp.bfloat16
    )
    seq_part = lax.psum_scatter(full_term, "seq", scatter_dimension=0, tiled=True)
    full_term, attended_grad = lax.optimization_barrier((full_term, attended_grad))
    query_grad, key_pad, value_pad, coarse_key_all, coarse_value_all = attention_backward(
        query_rows,
        padded_rows[0],
        padded_rows[1],
        gathered_keys,
        gathered_values,
        gathered_counts[None, :],
        fine_ok.astype(jnp.float32),
        far_ok.astype(jnp.float32),
        attended_grad,
        attended_rows,
    )
    query_grad = query_grad.reshape(1, tokens, model_width)
    key_ext = key_pad.reshape(local_blocks + 2, BLOCK, model_width)
    value_ext = value_pad.reshape(local_blocks + 2, BLOCK, model_width)
    edge_first = jnp.stack([key_ext[0], value_ext[0]])
    edge_last = jnp.stack([key_ext[local_blocks + 1], value_ext[local_blocks + 1]])
    from_right = from_behind(edge_first, "seq", -1)
    from_left = from_behind(edge_last, "seq", 1)
    zeros_mid = jnp.zeros((2, local_blocks - 1, BLOCK, model_width), jnp.float32)
    boundary = jnp.concatenate([from_left[:, None], zeros_mid], axis=1) + jnp.concatenate(
        [zeros_mid, from_right[:, None]], axis=1
    )
    coarse_all = jnp.concatenate(
        [
            coarse_key_all.reshape(all_blocks, model_width),
            coarse_value_all.reshape(all_blocks, model_width),
        ],
        axis=1,
    )
    owned_grads = halving_scatter(
        coarse_all.reshape(seq_devices, local_blocks, 2 * model_width), "seq"
    )
    owned_keys = owned_grads[:, :model_width] / divisor[:, None]
    owned_values = owned_grads[:, model_width:] / divisor[:, None]
    spread_keys = owned_keys[:, None, :] * pooled_mask[:, :, None]
    spread_values = owned_values[:, None, :] * pooled_mask[:, :, None]
    key_grad = (
        (key_ext[1 : local_blocks + 1] + boundary[0] + spread_keys)
        .astype(jnp.bfloat16)
        .reshape(1, tokens, model_width)
    )
    value_grad = (
        (value_ext[1 : local_blocks + 1] + boundary[1] + spread_values)
        .astype(jnp.bfloat16)
        .reshape(1, tokens, model_width)
    )
    seq_part, query_grad, key_grad, value_grad = lax.optimization_barrier(
        (seq_part, query_grad, key_grad, value_grad)
    )
    dp_devices = lax.axis_size("dp")
    dp_rows = halving_scatter(seq_part.reshape(dp_devices, -1, model_width), "dp")
    weight_grad = doubling_gather(dp_rows, "dp").reshape(-1, model_width)
    return (query_grad, key_grad, value_grad, weight_grad)


def solution(mesh):
    placed = (
        P("dp", "seq", None),
        P("dp", "seq", None),
        P("dp", "seq", None),
        P(),
        P("dp", "seq", None),
        P("dp", "seq"),
    )
    return jax.shard_map(
        per_device,
        mesh=mesh,
        in_specs=placed,
        out_specs=(
            P("dp", "seq", None),
            P("dp", "seq", None),
            P("dp", "seq", None),
            P("seq", None),
        ),
        check_vma=False,
    )
```

```python
import functools
import math

import jax
import jax.numpy as jnp
from jax import lax
from jax.experimental import pallas as pl
from jax.experimental.pallas import tpu as pltpu
from jax.sharding import PartitionSpec as P

HEADS = 16
HEAD_DIM = 64
BLOCK = 128


def padded_2(block, sides, width):
    for axis, dim in sides:
        count = lax.axis_size(axis)
        forward = [(i, i + 1) for i in range(count - 1)]
        backward = [(target, source) for source, target in forward]
        low = lax.ppermute(
            lax.slice_in_dim(block, block.shape[dim] - width, None, axis=dim), axis, forward
        )
        high = lax.ppermute(lax.slice_in_dim(block, 0, width, axis=dim), axis, backward)
        block = jnp.concatenate([low, block, high], axis=dim)
    return block


def from_behind(value, axis, steps):
    count = lax.axis_size(axis)
    leading, last = (max(0, -steps), min(count, count - steps))
    return lax.ppermute(value, axis, [(source, source + steps) for source in range(leading, last)])


def xor_pairs(count, bit):
    return [(source, source ^ (1 << bit)) for source in range(count)]


def own_bit(axis, bit):
    return (lax.axis_index(axis) // (1 << bit)) % 2


def doubling_gather(piece, axis):
    count = lax.axis_size(axis)
    bits = count.bit_length() - 1
    held = piece
    for done, bit in enumerate(reversed(range(bits))):
        other = lax.ppermute(held, axis, xor_pairs(count, bit))
        mine_low = own_bit(axis, bit) == 0
        low = jnp.where(mine_low, held, other)
        high = jnp.where(mine_low, other, held)
        held = jnp.stack([low, high], axis=done)
    return held.reshape((count,) + piece.shape)


def halving_scatter(stack, axis):
    count = lax.axis_size(axis)
    bits = count.bit_length() - 1
    held = stack.reshape((2,) * bits + stack.shape[1:])
    for bit in range(bits):
        dim = bits - 1 - bit
        mine = own_bit(axis, bit)
        keep = lax.dynamic_index_in_dim(held, mine, dim, keepdims=False)
        send = lax.dynamic_index_in_dim(held, 1 - mine, dim, keepdims=False)
        held = keep + lax.ppermute(send, axis, xor_pairs(count, bit))
    return held


def doubling_sum(value, axis):
    count = lax.axis_size(axis)
    for bit in range(count.bit_length() - 1):
        value = value + lax.ppermute(value, axis, xor_pairs(count, bit))
    return value


def forward_kernel(term_scale, q_ref, k_ref, v_ref, ck_ref, cv_ref, counts_ref, fine_ref, far_ref,
                   grad_t_ref, att_ref, term_ref):
    score_scale = 1.0 / math.sqrt(HEAD_DIM)
    lanes = q_ref.shape[1]
    low_lanes = lax.broadcasted_iota(jnp.int32, (BLOCK, lanes), 1) < HEAD_DIM
    coarse_k = ck_ref[...]
    coarse_v = cv_ref[...]
    counts = counts_ref[...]
    contract_last = (((1,), (1,)), ((), ()))
    for block in range(q_ref.shape[0] // BLOCK):
        query = q_ref[pl.ds(block * BLOCK, BLOCK), :]
        key_win = k_ref[pl.ds(block * BLOCK, 3 * BLOCK), :]
        value_win = v_ref[pl.ds(block * BLOCK, 3 * BLOCK), :]
        fine_ok = fine_ref[pl.ds(block, 1), :] > 0
        far_ok = far_ref[pl.ds(block, 1), :] > 0
        halves = []
        for half in range(2):
            own = low_lanes if half == 0 else jnp.logical_not(low_lanes)
            query_h = jnp.where(own, query, jnp.zeros_like(query))
            fine_s = lax.dot_general(query_h, key_win, contract_last,
                                     preferred_element_type=jnp.float32) * score_scale
            coarse_s = lax.dot_general(query_h, coarse_k, contract_last,
                                       preferred_element_type=jnp.float32) * score_scale
            fine_s = jnp.where(fine_ok, fine_s, -jnp.inf)
            coarse_s = jnp.where(far_ok, coarse_s, -jnp.inf)
            top = jnp.maximum(jnp.max(fine_s, axis=1, keepdims=True),
                              jnp.max(coarse_s, axis=1, keepdims=True))
            fine_e = jnp.exp(fine_s - top)
            coarse_e = counts * jnp.exp(coarse_s - top)
            total = (jnp.sum(fine_e, axis=1, keepdims=True)
                     + jnp.sum(coarse_e, axis=1, keepdims=True))
            inverse = 1.0 / total
            fine_w = (fine_e * inverse).astype(jnp.bfloat16)
            coarse_w = (coarse_e * inverse).astype(jnp.bfloat16)
            att = (jnp.dot(fine_w, value_win, preferred_element_type=jnp.float32)
                   + jnp.dot(coarse_w, coarse_v, preferred_element_type=jnp.float32))
            halves.append((att, top, total))
        rows = pl.ds(block * BLOCK, BLOCK)
        att_ref[rows, :] = jnp.where(low_lanes, halves[0][0], halves[1][0]).astype(att_ref.dtype)
    term_ref[...] = jnp.dot(grad_t_ref[...], att_ref[...],
                            preferred_element_type=jnp.float32) * term_scale


def attention_forward(query_rows, padded_k, padded_v, coarse_k, coarse_v, counts, fine_ok, far_ok,
                      grad_t, term_scale):
    tokens, width = query_rows.shape
    lanes = 2 * HEAD_DIM
    by_pair = lambda rows: pl.BlockSpec((rows, lanes), lambda pair: (0, pair))
    whole = lambda shape: pl.BlockSpec(shape, lambda pair: (0, 0))
    return pl.pallas_call(
        functools.partial(forward_kernel, term_scale),
        grid=(width // lanes,),
        in_specs=[
            by_pair(tokens),
            by_pair(padded_k.shape[0]),
            by_pair(padded_v.shape[0]),
            by_pair(coarse_k.shape[0]),
            by_pair(coarse_v.shape[0]),
            whole(counts.shape),
            whole(fine_ok.shape),
            whole(far_ok.shape),
            whole(grad_t.shape),
        ],
        out_specs=[by_pair(tokens), by_pair(grad_t.shape[0])],
        out_shape=[
            jax.ShapeDtypeStruct((tokens, width), jnp.bfloat16),
            jax.ShapeDtypeStruct((grad_t.shape[0], width), jnp.float32),
        ],
    )(query_rows, padded_k, padded_v, coarse_k, coarse_v, counts, fine_ok, far_ok, grad_t)


def backward_kernel(q_ref, k_ref, v_ref, ck_ref, cv_ref, counts_ref, fine_ref, far_ref,
                    g_ref, att_ref, qg_ref, kg_ref, vg_ref, ckg_ref, cvg_ref):
    score_scale = 1.0 / math.sqrt(HEAD_DIM)
    lanes = q_ref.shape[1]
    low_lanes = lax.broadcasted_iota(jnp.int32, (BLOCK, lanes), 1) < HEAD_DIM
    coarse_k = ck_ref[...]
    coarse_v = cv_ref[...]
    counts = counts_ref[...]
    contract_last = (((1,), (1,)), ((), ()))
    kg_ref[...] = jnp.zeros_like(kg_ref)
    vg_ref[...] = jnp.zeros_like(vg_ref)
    coarse_kg = jnp.zeros(ckg_ref.shape, jnp.float32)
    coarse_vg = jnp.zeros(cvg_ref.shape, jnp.float32)
    for block in range(q_ref.shape[0] // BLOCK):
        rows = pl.ds(block * BLOCK, BLOCK)
        window = pl.ds(block * BLOCK, 3 * BLOCK)
        query = q_ref[rows, :]
        grad = g_ref[rows, :]
        att = att_ref[rows, :].astype(jnp.float32)
        key_win = k_ref[window, :]
        value_win = v_ref[window, :]
        fine_ok = fine_ref[pl.ds(block, 1), :] > 0
        far_ok = far_ref[pl.ds(block, 1), :] > 0
        query_grads = []
        key_grad = jnp.zeros((3 * BLOCK, lanes), jnp.float32)
        value_grad = jnp.zeros((3 * BLOCK, lanes), jnp.float32)
        for half in range(2):
            own = low_lanes if half == 0 else jnp.logical_not(low_lanes)
            query_h = jnp.where(own, query, jnp.zeros_like(query))
            grad_h = jnp.where(own, grad, jnp.zeros_like(grad))
            fine_s = lax.dot_general(query_h, key_win, contract_last,
                                     preferred_element_type=jnp.float32) * score_scale
            coarse_s = lax.dot_general(query_h, coarse_k, contract_last,
                                       preferred_element_type=jnp.float32) * score_scale
            fine_s = jnp.where(fine_ok, fine_s, -jnp.inf)
            coarse_s = jnp.where(far_ok, coarse_s, -jnp.inf)
            top = jnp.maximum(jnp.max(fine_s, axis=1, keepdims=True),
                              jnp.max(coarse_s, axis=1, keepdims=True))
            fine_e = jnp.exp(fine_s - top)
            coarse_e = counts * jnp.exp(coarse_s - top)
            total = (jnp.sum(fine_e, axis=1, keepdims=True)
                     + jnp.sum(coarse_e, axis=1, keepdims=True))
            inverse = 1.0 / total
            fine_w = fine_e * inverse
            coarse_w = coarse_e * inverse
            fine_dot = lax.dot_general(grad_h, value_win, contract_last,
                                       preferred_element_type=jnp.float32)
            coarse_dot = lax.dot_general(grad_h, coarse_v, contract_last,
                                         preferred_element_type=jnp.float32)
            delta = jnp.sum(jnp.where(own, grad.astype(jnp.float32) * att, 0.0),
                            axis=1, keepdims=True)
            fine_ds = fine_w * (fine_dot - delta)
            coarse_ds = coarse_w * (coarse_dot - delta)
            fine_ds_b = fine_ds.astype(jnp.bfloat16)
            coarse_ds_b = coarse_ds.astype(jnp.bfloat16)
            query_grads.append(
                (jnp.dot(fine_ds_b, key_win, preferred_element_type=jnp.float32)
                 + jnp.dot(coarse_ds_b, coarse_k, preferred_element_type=jnp.float32))
                * score_scale)
            fine_ds_t = fine_ds.T.astype(jnp.bfloat16)
            coarse_ds_t = coarse_ds.T.astype(jnp.bfloat16)
            fine_w_t = fine_w.T.astype(jnp.bfloat16)
            coarse_w_t = coarse_w.T.astype(jnp.bfloat16)
            key_grad = key_grad + jnp.dot(fine_ds_t, query_h,
                                          preferred_element_type=jnp.float32) * score_scale
            value_grad = value_grad + jnp.dot(fine_w_t, grad_h,
                                              preferred_element_type=jnp.float32)
            coarse_kg = coarse_kg + jnp.dot(coarse_ds_t, query_h,
                                            preferred_element_type=jnp.float32) * score_scale
            coarse_vg = coarse_vg + jnp.dot(coarse_w_t, grad_h,
                                            preferred_element_type=jnp.float32)
        qg_ref[rows, :] = jnp.where(low_lanes, query_grads[0], query_grads[1]).astype(qg_ref.dtype)
        kg_ref[window, :] += key_grad
        vg_ref[window, :] += value_grad
    ckg_ref[...] = coarse_kg
    cvg_ref[...] = coarse_vg


def attention_backward(query_rows, padded_k, padded_v, coarse_k, coarse_v, counts, fine_ok,
                       far_ok, grad_rows, attended_rows):
    tokens, width = query_rows.shape
    lanes = 2 * HEAD_DIM
    by_pair = lambda rows: pl.BlockSpec((rows, lanes), lambda pair: (0, pair))
    whole = lambda shape: pl.BlockSpec(shape, lambda pair: (0, 0))
    wide = lambda rows: jax.ShapeDtypeStruct((rows, width), jnp.float32)
    return pl.pallas_call(
        backward_kernel,
        grid=(width // lanes,),
        in_specs=[
            by_pair(tokens),
            by_pair(padded_k.shape[0]),
            by_pair(padded_v.shape[0]),
            by_pair(coarse_k.shape[0]),
            by_pair(coarse_v.shape[0]),
            whole(counts.shape),
            whole(fine_ok.shape),
            whole(far_ok.shape),
            by_pair(tokens),
            by_pair(tokens),
        ],
        out_specs=[
            by_pair(tokens),
            by_pair(padded_k.shape[0]),
            by_pair(padded_v.shape[0]),
            by_pair(coarse_k.shape[0]),
            by_pair(coarse_v.shape[0]),
        ],
        out_shape=[
            jax.ShapeDtypeStruct((tokens, width), jnp.bfloat16),
            wide(padded_k.shape[0]),
            wide(padded_v.shape[0]),
            wide(coarse_k.shape[0]),
            wide(coarse_v.shape[0]),
        ],
    )(query_rows, padded_k, padded_v, coarse_k, coarse_v, counts, fine_ok, far_ok, grad_rows,
      attended_rows)


def block_windows(padded, local_blocks):
    return jnp.concatenate(
        [padded[0:local_blocks], padded[1 : local_blocks + 1], padded[2 : local_blocks + 2]], axis=1
    )


def fold_windows(grads, local_blocks):
    parts = grads.reshape((local_blocks, 3, BLOCK) + grads.shape[2:])
    edge_zero = jnp.zeros((1,) + parts.shape[2:], jnp.float32)
    left_part = jnp.concatenate([parts[:, 0], edge_zero, edge_zero], axis=0)
    middle = jnp.concatenate([edge_zero, parts[:, 1], edge_zero], axis=0)
    right_part = jnp.concatenate([edge_zero, edge_zero, parts[:, 2]], axis=0)
    return left_part + middle + right_part


def per_device(queries, keys, values, out_weight, out_grad, pooled):
    query_rows = queries[0]
    key_rows = keys[0]
    value_rows = values[0]
    grad_out = out_grad[0]
    tokens, model_width = query_rows.shape
    local_blocks = tokens // BLOCK
    seq_devices = lax.axis_size("seq")
    seq_index = lax.axis_index("seq")
    all_blocks = local_blocks * seq_devices
    score_scale = 1.0 / math.sqrt(HEAD_DIM)
    pooled_mask = pooled[0].reshape(local_blocks, BLOCK).astype(jnp.float32)
    counts = jnp.sum(pooled_mask, axis=1)
    divisor = jnp.maximum(counts, 1.0)
    pooled_bf = pooled_mask.astype(jnp.bfloat16)
    key_sum = jnp.einsum(
        "nb,nbd->nd",
        pooled_bf,
        key_rows.reshape(local_blocks, BLOCK, model_width),
        preferred_element_type=jnp.float32,
    )
    value_sum = jnp.einsum(
        "nb,nbd->nd",
        pooled_bf,
        value_rows.reshape(local_blocks, BLOCK, model_width),
        preferred_element_type=jnp.float32,
    )
    coarse_keys = (key_sum / divisor[:, None]).astype(jnp.bfloat16)
    coarse_values = (value_sum / divisor[:, None]).astype(jnp.bfloat16)
    count_cols = jnp.broadcast_to(counts.astype(jnp.bfloat16)[:, None], (local_blocks, 128))
    packed = jnp.concatenate([coarse_keys, coarse_values, count_cols], axis=1)
    gathered = doubling_gather(packed, "seq").reshape(all_blocks, packed.shape[1])
    gathered_keys = gathered[:, :model_width]
    gathered_values = gathered[:, model_width : 2 * model_width]
    gathered_counts = gathered[:, 2 * model_width].astype(jnp.float32)
    paired = jnp.stack([key_rows, value_rows])
    extended = padded_2(paired, (("seq", 1),), BLOCK)
    padded_kv = extended.reshape(2, local_blocks + 2, BLOCK, HEADS, HEAD_DIM)
    local_ids = seq_index * local_blocks + jnp.arange(local_blocks)
    offsets = jnp.repeat(jnp.arange(3) - 1, BLOCK)
    key_blocks = local_ids[:, None] + offsets[None, :]
    fine_ok = (key_blocks >= 0) & (key_blocks < all_blocks)
    far_ok = jnp.abs(local_ids[:, None] - jnp.arange(all_blocks)[None, :]) >= 2
    padded_rows = extended.reshape(2, (local_blocks + 2) * BLOCK, model_width)
    grad_norm = 1.0 / math.sqrt(seq_devices * tokens)
    attended_rows, full_term = attention_forward(
        query_rows,
        padded_rows[0],
        padded_rows[1],
        gathered_keys,
        gathered_values,
        gathered_counts[None, :],
        fine_ok.astype(jnp.float32),
        far_ok.astype(jnp.float32),
        grad_out.T,
        grad_norm,
    )
    attended_grad = jnp.dot(grad_out, out_weight, preferred_element_type=jnp.float32).astype(
        jnp.bfloat16
    )
    seq_part = lax.psum_scatter(full_term, "seq", scatter_dimension=0, tiled=True)
    full_term, attended_grad = lax.optimization_barrier((full_term, attended_grad))
    query_grad, key_pad, value_pad, coarse_key_all, coarse_value_all = attention_backward(
        query_rows,
        padded_rows[0],
        padded_rows[1],
        gathered_keys,
        gathered_values,
        gathered_counts[None, :],
        fine_ok.astype(jnp.float32),
        far_ok.astype(jnp.float32),
        attended_grad,
        attended_rows,
    )
    query_grad = query_grad.reshape(1, tokens, model_width)
    key_ext = key_pad.reshape(local_blocks + 2, BLOCK, model_width)
    value_ext = value_pad.reshape(local_blocks + 2, BLOCK, model_width)
    edge_first = jnp.stack([key_ext[0], value_ext[0]])
    edge_last = jnp.stack([key_ext[local_blocks + 1], value_ext[local_blocks + 1]])
    from_right = from_behind(edge_first, "seq", -1)
    from_left = from_behind(edge_last, "seq", 1)
    zeros_mid = jnp.zeros((2, local_blocks - 1, BLOCK, model_width), jnp.float32)
    boundary = jnp.concatenate([from_left[:, None], zeros_mid], axis=1) + jnp.concatenate(
        [zeros_mid, from_right[:, None]], axis=1
    )
    coarse_all = jnp.concatenate(
        [
            coarse_key_all.reshape(all_blocks, model_width),
            coarse_value_all.reshape(all_blocks, model_width),
        ],
        axis=1,
    )
    owned_grads = halving_scatter(
        coarse_all.reshape(seq_devices, local_blocks, 2 * model_width), "seq"
    )
    owned_keys = owned_grads[:, :model_width] / divisor[:, None]
    owned_values = owned_grads[:, model_width:] / divisor[:, None]
    spread_keys = owned_keys[:, None, :] * pooled_mask[:, :, None]
    spread_values = owned_values[:, None, :] * pooled_mask[:, :, None]
    key_grad = (
        (key_ext[1 : local_blocks + 1] + boundary[0] + spread_keys)
        .astype(jnp.bfloat16)
        .reshape(1, tokens, model_width)
    )
    value_grad = (
        (value_ext[1 : local_blocks + 1] + boundary[1] + spread_values)
        .astype(jnp.bfloat16)
        .reshape(1, tokens, model_width)
    )
    seq_part, query_grad, key_grad, value_grad = lax.optimization_barrier(
        (seq_part, query_grad, key_grad, value_grad)
    )
    dp_devices = lax.axis_size("dp")
    dp_rows = halving_scatter(seq_part.reshape(dp_devices, -1, model_width), "dp")
    weight_grad = doubling_gather(dp_rows, "dp").reshape(-1, model_width)
    return (query_grad, key_grad, value_grad, weight_grad)


def solution(mesh):
    placed = (
        P("dp", "seq", None),
        P("dp", "seq", None),
        P("dp", "seq", None),
        P(),
        P("dp", "seq", None),
        P("dp", "seq"),
    )
    return jax.shard_map(
        per_device,
        mesh=mesh,
        in_specs=placed,
        out_specs=(
            P("dp", "seq", None),
            P("dp", "seq", None),
            P("dp", "seq", None),
            P("seq", None),
        ),
        check_vma=False,
    )
```

```python
import functools
import math

import jax
import jax.numpy as jnp
from jax import lax
from jax.experimental import pallas as pl
from jax.experimental.pallas import tpu as pltpu
from jax.sharding import PartitionSpec as P

HEADS = 16
HEAD_DIM = 64
BLOCK = 128


def padded_2(block, sides, width):
    for axis, dim in sides:
        count = lax.axis_size(axis)
        forward = [(i, i + 1) for i in range(count - 1)]
        backward = [(target, source) for source, target in forward]
        low = lax.ppermute(
            lax.slice_in_dim(block, block.shape[dim] - width, None, axis=dim), axis, forward
        )
        high = lax.ppermute(lax.slice_in_dim(block, 0, width, axis=dim), axis, backward)
        block = jnp.concatenate([low, block, high], axis=dim)
    return block


def from_behind(value, axis, steps):
    count = lax.axis_size(axis)
    leading, last = (max(0, -steps), min(count, count - steps))
    return lax.ppermute(value, axis, [(source, source + steps) for source in range(leading, last)])


def xor_pairs(count, bit, mask=1):
    return [(source, source ^ (mask << bit)) for source in range(count)]


def own_bit(axis, bit):
    return (lax.axis_index(axis) // (1 << bit)) % 2


def doubling_gather(piece, axis):
    count = lax.axis_size(axis)
    bits = count.bit_length() - 1
    held = piece
    for done, bit in enumerate(reversed(range(bits))):
        other = lax.ppermute(held, axis, xor_pairs(count, bit))
        mine_low = own_bit(axis, bit) == 0
        low = jnp.where(mine_low, held, other)
        high = jnp.where(mine_low, other, held)
        held = jnp.stack([low, high], axis=done)
    return held.reshape((count,) + piece.shape)


def halving_scatter(stack, axis):
    count = lax.axis_size(axis)
    bits = count.bit_length() - 1
    held = stack.reshape((2,) * bits + stack.shape[1:])
    for bit in range(bits):
        dim = bits - 1 - bit
        mine = own_bit(axis, bit)
        keep = lax.dynamic_index_in_dim(held, mine, dim, keepdims=False)
        send = lax.dynamic_index_in_dim(held, 1 - mine, dim, keepdims=False)
        held = keep + lax.ppermute(send, axis, xor_pairs(count, bit))
    return held


def doubling_sum(value, axis):
    count = lax.axis_size(axis)
    for bit in range(count.bit_length() - 1):
        value = value + lax.ppermute(value, axis, xor_pairs(count, bit))
    return value


def forward_kernel(term_scale, q_ref, k_ref, v_ref, ck_ref, cv_ref, counts_ref, fine_ref, far_ref,
                   grad_t_ref, att_ref, term_ref):
    score_scale = 1.0 / math.sqrt(HEAD_DIM)
    lanes = q_ref.shape[1]
    low_lanes = lax.broadcasted_iota(jnp.int32, (BLOCK, lanes), 1) < HEAD_DIM
    coarse_k = ck_ref[...]
    coarse_v = cv_ref[...]
    counts = counts_ref[...]
    contract_last = (((1,), (1,)), ((), ()))
    for block in range(q_ref.shape[0] // BLOCK):
        query = q_ref[pl.ds(block * BLOCK, BLOCK), :]
        key_win = k_ref[pl.ds(block * BLOCK, 3 * BLOCK), :]
        value_win = v_ref[pl.ds(block * BLOCK, 3 * BLOCK), :]
        fine_ok = fine_ref[pl.ds(block, 1), :] > 0
        far_ok = far_ref[pl.ds(block, 1), :] > 0
        halves = []
        for half in range(2):
            own = low_lanes if half == 0 else jnp.logical_not(low_lanes)
            query_h = jnp.where(own, query, jnp.zeros_like(query))
            fine_s = lax.dot_general(query_h, key_win, contract_last,
                                     preferred_element_type=jnp.float32) * score_scale
            coarse_s = lax.dot_general(query_h, coarse_k, contract_last,
                                       preferred_element_type=jnp.float32) * score_scale
            fine_s = jnp.where(fine_ok, fine_s, -jnp.inf)
            coarse_s = jnp.where(far_ok, coarse_s, -jnp.inf)
            top = jnp.maximum(jnp.max(fine_s, axis=1, keepdims=True),
                              jnp.max(coarse_s, axis=1, keepdims=True))
            fine_e = jnp.exp(fine_s - top)
            coarse_e = counts * jnp.exp(coarse_s - top)
            total = (jnp.sum(fine_e, axis=1, keepdims=True)
                     + jnp.sum(coarse_e, axis=1, keepdims=True))
            fine_w = (fine_e / total).astype(jnp.bfloat16)
            coarse_w = (coarse_e / total).astype(jnp.bfloat16)
            att = (jnp.dot(fine_w, value_win, preferred_element_type=jnp.float32)
                   + jnp.dot(coarse_w, coarse_v, preferred_element_type=jnp.float32))
            halves.append((att, top, total))
        rows = pl.ds(block * BLOCK, BLOCK)
        att_ref[rows, :] = jnp.where(low_lanes, halves[0][0], halves[1][0]).astype(att_ref.dtype)
    term_ref[...] = jnp.dot(grad_t_ref[...], att_ref[...],
                            preferred_element_type=jnp.float32) * term_scale


def attention_forward(query_rows, padded_k, padded_v, coarse_k, coarse_v, counts, fine_ok, far_ok,
                      grad_t, term_scale):
    tokens, width = query_rows.shape
    lanes = 2 * HEAD_DIM
    by_pair = lambda rows: pl.BlockSpec((rows, lanes), lambda pair: (0, pair))
    whole = lambda shape: pl.BlockSpec(shape, lambda pair: (0, 0))
    return pl.pallas_call(
        functools.partial(forward_kernel, term_scale),
        grid=(width // lanes,),
        in_specs=[
            by_pair(tokens),
            by_pair(padded_k.shape[0]),
            by_pair(padded_v.shape[0]),
            by_pair(coarse_k.shape[0]),
            by_pair(coarse_v.shape[0]),
            whole(counts.shape),
            whole(fine_ok.shape),
            whole(far_ok.shape),
            whole(grad_t.shape),
        ],
        out_specs=[by_pair(tokens), by_pair(grad_t.shape[0])],
        out_shape=[
            jax.ShapeDtypeStruct((tokens, width), jnp.bfloat16),
            jax.ShapeDtypeStruct((grad_t.shape[0], width), jnp.float32),
        ],
    )(query_rows, padded_k, padded_v, coarse_k, coarse_v, counts, fine_ok, far_ok, grad_t)


def backward_kernel(q_ref, k_ref, v_ref, ck_ref, cv_ref, counts_ref, fine_ref, far_ref,
                    g_ref, att_ref, qg_ref, kg_ref, vg_ref, ckg_ref, cvg_ref):
    score_scale = 1.0 / math.sqrt(HEAD_DIM)
    lanes = q_ref.shape[1]
    low_lanes = lax.broadcasted_iota(jnp.int32, (BLOCK, lanes), 1) < HEAD_DIM
    coarse_k = ck_ref[...]
    coarse_v = cv_ref[...]
    counts = counts_ref[...]
    contract_last = (((1,), (1,)), ((), ()))
    kg_ref[...] = jnp.zeros_like(kg_ref)
    vg_ref[...] = jnp.zeros_like(vg_ref)
    coarse_kg = jnp.zeros(ckg_ref.shape, jnp.float32)
    coarse_vg = jnp.zeros(cvg_ref.shape, jnp.float32)
    for block in range(q_ref.shape[0] // BLOCK):
        rows = pl.ds(block * BLOCK, BLOCK)
        window = pl.ds(block * BLOCK, 3 * BLOCK)
        query = q_ref[rows, :]
        grad = g_ref[rows, :]
        att = att_ref[rows, :].astype(jnp.float32)
        key_win = k_ref[window, :]
        value_win = v_ref[window, :]
        fine_ok = fine_ref[pl.ds(block, 1), :] > 0
        far_ok = far_ref[pl.ds(block, 1), :] > 0
        query_grads = []
        key_grad = jnp.zeros((3 * BLOCK, lanes), jnp.float32)
        value_grad = jnp.zeros((3 * BLOCK, lanes), jnp.float32)
        for half in range(2):
            own = low_lanes if half == 0 else jnp.logical_not(low_lanes)
            query_h = jnp.where(own, query, jnp.zeros_like(query))
            grad_h = jnp.where(own, grad, jnp.zeros_like(grad))
            fine_s = lax.dot_general(query_h, key_win, contract_last,
                                     preferred_element_type=jnp.float32) * score_scale
            coarse_s = lax.dot_general(query_h, coarse_k, contract_last,
                                       preferred_element_type=jnp.float32) * score_scale
            fine_s = jnp.where(fine_ok, fine_s, -jnp.inf)
            coarse_s = jnp.where(far_ok, coarse_s, -jnp.inf)
            top = jnp.maximum(jnp.max(fine_s, axis=1, keepdims=True),
                              jnp.max(coarse_s, axis=1, keepdims=True))
            fine_e = jnp.exp(fine_s - top)
            coarse_e = counts * jnp.exp(coarse_s - top)
            total = (jnp.sum(fine_e, axis=1, keepdims=True)
                     + jnp.sum(coarse_e, axis=1, keepdims=True))
            fine_w = fine_e / total
            coarse_w = coarse_e / total
            fine_dot = lax.dot_general(grad_h, value_win, contract_last,
                                       preferred_element_type=jnp.float32)
            coarse_dot = lax.dot_general(grad_h, coarse_v, contract_last,
                                         preferred_element_type=jnp.float32)
            delta = jnp.sum(jnp.where(own, grad.astype(jnp.float32) * att, 0.0),
                            axis=1, keepdims=True)
            fine_ds = fine_w * (fine_dot - delta)
            coarse_ds = coarse_w * (coarse_dot - delta)
            fine_ds_b = fine_ds.astype(jnp.bfloat16)
            coarse_ds_b = coarse_ds.astype(jnp.bfloat16)
            query_grads.append(
                (jnp.dot(fine_ds_b, key_win, preferred_element_type=jnp.float32)
                 + jnp.dot(coarse_ds_b, coarse_k, preferred_element_type=jnp.float32))
                * score_scale)
            fine_ds_t = fine_ds.T.astype(jnp.bfloat16)
            coarse_ds_t = coarse_ds.T.astype(jnp.bfloat16)
            fine_w_t = fine_w.T.astype(jnp.bfloat16)
            coarse_w_t = coarse_w.T.astype(jnp.bfloat16)
            key_grad = key_grad + jnp.dot(fine_ds_t, query_h,
                                          preferred_element_type=jnp.float32) * score_scale
            value_grad = value_grad + jnp.dot(fine_w_t, grad_h,
                                              preferred_element_type=jnp.float32)
            coarse_kg = coarse_kg + jnp.dot(coarse_ds_t, query_h,
                                            preferred_element_type=jnp.float32) * score_scale
            coarse_vg = coarse_vg + jnp.dot(coarse_w_t, grad_h,
                                            preferred_element_type=jnp.float32)
        qg_ref[rows, :] = jnp.where(low_lanes, query_grads[0], query_grads[1]).astype(qg_ref.dtype)
        kg_ref[window, :] += key_grad
        vg_ref[window, :] += value_grad
    ckg_ref[...] = coarse_kg
    cvg_ref[...] = coarse_vg


def attention_backward(query_rows, padded_k, padded_v, coarse_k, coarse_v, counts, fine_ok,
                       far_ok, grad_rows, attended_rows):
    tokens, width = query_rows.shape
    lanes = 2 * HEAD_DIM
    by_pair = lambda rows: pl.BlockSpec((rows, lanes), lambda pair: (0, pair))
    whole = lambda shape: pl.BlockSpec(shape, lambda pair: (0, 0))
    wide = lambda rows: jax.ShapeDtypeStruct((rows, width), jnp.float32)
    return pl.pallas_call(
        backward_kernel,
        grid=(width // lanes,),
        in_specs=[
            by_pair(tokens),
            by_pair(padded_k.shape[0]),
            by_pair(padded_v.shape[0]),
            by_pair(coarse_k.shape[0]),
            by_pair(coarse_v.shape[0]),
            whole(counts.shape),
            whole(fine_ok.shape),
            whole(far_ok.shape),
            by_pair(tokens),
            by_pair(tokens),
        ],
        out_specs=[
            by_pair(tokens),
            by_pair(padded_k.shape[0]),
            by_pair(padded_v.shape[0]),
            by_pair(coarse_k.shape[0]),
            by_pair(coarse_v.shape[0]),
        ],
        out_shape=[
            jax.ShapeDtypeStruct((tokens, width), jnp.bfloat16),
            wide(padded_k.shape[0]),
            wide(padded_v.shape[0]),
            wide(coarse_k.shape[0]),
            wide(coarse_v.shape[0]),
        ],
    )(query_rows, padded_k, padded_v, coarse_k, coarse_v, counts, fine_ok, far_ok, grad_rows,
      attended_rows)


def grouped_gather(piece, axis):
    count = lax.axis_size(axis)
    bits = count.bit_length() - 1
    me = lax.axis_index(axis)
    groups = [(low, min(2, bits - low)) for low in range(0, bits, 2)][::-1]
    held = piece
    for done, (low, width) in enumerate(groups):
        size = 1 << width
        arrived = [held] + [
            lax.ppermute(held, axis, xor_pairs(count, low, mask)) for mask in range(1, size)
        ]
        mine = (me // (1 << low)) % size
        stacked = jnp.stack(arrived, axis=done)
        held = jnp.take(stacked, jnp.arange(size) ^ mine, axis=done)
    return held.reshape((count,) + piece.shape)


def block_windows(padded, local_blocks):
    return jnp.concatenate(
        [padded[0:local_blocks], padded[1 : local_blocks + 1], padded[2 : local_blocks + 2]], axis=1
    )


def fold_windows(grads, local_blocks):
    parts = grads.reshape((local_blocks, 3, BLOCK) + grads.shape[2:])
    edge_zero = jnp.zeros((1,) + parts.shape[2:], jnp.float32)
    left_part = jnp.concatenate([parts[:, 0], edge_zero, edge_zero], axis=0)
    middle = jnp.concatenate([edge_zero, parts[:, 1], edge_zero], axis=0)
    right_part = jnp.concatenate([edge_zero, edge_zero, parts[:, 2]], axis=0)
    return left_part + middle + right_part


def per_device(queries, keys, values, out_weight, out_grad, pooled):
    query_rows = queries[0]
    key_rows = keys[0]
    value_rows = values[0]
    grad_out = out_grad[0]
    tokens, model_width = query_rows.shape
    local_blocks = tokens // BLOCK
    seq_devices = lax.axis_size("seq")
    seq_index = lax.axis_index("seq")
    all_blocks = local_blocks * seq_devices
    score_scale = 1.0 / math.sqrt(HEAD_DIM)
    pooled_mask = pooled[0].reshape(local_blocks, BLOCK).astype(jnp.float32)
    counts = jnp.sum(pooled_mask, axis=1)
    divisor = jnp.maximum(counts, 1.0)
    pooled_bf = pooled_mask.astype(jnp.bfloat16)
    key_sum = jnp.einsum(
        "nb,nbd->nd",
        pooled_bf,
        key_rows.reshape(local_blocks, BLOCK, model_width),
        preferred_element_type=jnp.float32,
    )
    value_sum = jnp.einsum(
        "nb,nbd->nd",
        pooled_bf,
        value_rows.reshape(local_blocks, BLOCK, model_width),
        preferred_element_type=jnp.float32,
    )
    coarse_keys = (key_sum / divisor[:, None]).astype(jnp.bfloat16)
    coarse_values = (value_sum / divisor[:, None]).astype(jnp.bfloat16)
    count_cols = jnp.broadcast_to(counts.astype(jnp.bfloat16)[:, None], (local_blocks, 128))
    packed = jnp.concatenate([coarse_keys, coarse_values, count_cols], axis=1)
    gathered = grouped_gather(packed, "seq").reshape(all_blocks, packed.shape[1])
    gathered_keys = gathered[:, :model_width]
    gathered_values = gathered[:, model_width : 2 * model_width]
    gathered_counts = gathered[:, 2 * model_width].astype(jnp.float32)
    paired = jnp.stack([key_rows, value_rows])
    extended = padded_2(paired, (("seq", 1),), BLOCK)
    padded_kv = extended.reshape(2, local_blocks + 2, BLOCK, HEADS, HEAD_DIM)
    local_ids = seq_index * local_blocks + jnp.arange(local_blocks)
    offsets = jnp.repeat(jnp.arange(3) - 1, BLOCK)
    key_blocks = local_ids[:, None] + offsets[None, :]
    fine_ok = (key_blocks >= 0) & (key_blocks < all_blocks)
    far_ok = jnp.abs(local_ids[:, None] - jnp.arange(all_blocks)[None, :]) >= 2
    padded_rows = extended.reshape(2, (local_blocks + 2) * BLOCK, model_width)
    grad_norm = 1.0 / math.sqrt(seq_devices * tokens)
    attended_rows, full_term = attention_forward(
        query_rows,
        padded_rows[0],
        padded_rows[1],
        gathered_keys,
        gathered_values,
        gathered_counts[None, :],
        fine_ok.astype(jnp.float32),
        far_ok.astype(jnp.float32),
        grad_out.T,
        grad_norm,
    )
    attended_grad = jnp.dot(grad_out, out_weight, preferred_element_type=jnp.float32).astype(
        jnp.bfloat16
    )
    seq_part = lax.psum_scatter(full_term, "seq", scatter_dimension=0, tiled=True)
    full_term, attended_grad = lax.optimization_barrier((full_term, attended_grad))
    query_grad, key_pad, value_pad, coarse_key_all, coarse_value_all = attention_backward(
        query_rows,
        padded_rows[0],
        padded_rows[1],
        gathered_keys,
        gathered_values,
        gathered_counts[None, :],
        fine_ok.astype(jnp.float32),
        far_ok.astype(jnp.float32),
        attended_grad,
        attended_rows,
    )
    query_grad = query_grad.reshape(1, tokens, model_width)
    key_ext = key_pad.reshape(local_blocks + 2, BLOCK, model_width)
    value_ext = value_pad.reshape(local_blocks + 2, BLOCK, model_width)
    edge_first = jnp.stack([key_ext[0], value_ext[0]])
    edge_last = jnp.stack([key_ext[local_blocks + 1], value_ext[local_blocks + 1]])
    from_right = from_behind(edge_first, "seq", -1)
    from_left = from_behind(edge_last, "seq", 1)
    zeros_mid = jnp.zeros((2, local_blocks - 1, BLOCK, model_width), jnp.float32)
    boundary = jnp.concatenate([from_left[:, None], zeros_mid], axis=1) + jnp.concatenate(
        [zeros_mid, from_right[:, None]], axis=1
    )
    coarse_all = jnp.concatenate(
        [
            coarse_key_all.reshape(all_blocks, model_width),
            coarse_value_all.reshape(all_blocks, model_width),
        ],
        axis=1,
    )
    owned_grads = halving_scatter(
        coarse_all.reshape(seq_devices, local_blocks, 2 * model_width), "seq"
    )
    owned_keys = owned_grads[:, :model_width] / divisor[:, None]
    owned_values = owned_grads[:, model_width:] / divisor[:, None]
    spread_keys = owned_keys[:, None, :] * pooled_mask[:, :, None]
    spread_values = owned_values[:, None, :] * pooled_mask[:, :, None]
    key_grad = (
        (key_ext[1 : local_blocks + 1] + boundary[0] + spread_keys)
        .astype(jnp.bfloat16)
        .reshape(1, tokens, model_width)
    )
    value_grad = (
        (value_ext[1 : local_blocks + 1] + boundary[1] + spread_values)
        .astype(jnp.bfloat16)
        .reshape(1, tokens, model_width)
    )
    seq_part, query_grad, key_grad, value_grad = lax.optimization_barrier(
        (seq_part, query_grad, key_grad, value_grad)
    )
    dp_devices = lax.axis_size("dp")
    dp_rows = halving_scatter(seq_part.reshape(dp_devices, -1, model_width), "dp")
    weight_grad = doubling_gather(dp_rows, "dp").reshape(-1, model_width)
    return (query_grad, key_grad, value_grad, weight_grad)


def solution(mesh):
    placed = (
        P("dp", "seq", None),
        P("dp", "seq", None),
        P("dp", "seq", None),
        P(),
        P("dp", "seq", None),
        P("dp", "seq"),
    )
    return jax.shard_map(
        per_device,
        mesh=mesh,
        in_specs=placed,
        out_specs=(
            P("dp", "seq", None),
            P("dp", "seq", None),
            P("dp", "seq", None),
            P("seq", None),
        ),
        check_vma=False,
    )
```

```python
import functools
import math

import jax
import jax.numpy as jnp
from jax import lax
from jax.experimental import pallas as pl
from jax.experimental.pallas import tpu as pltpu
from jax.sharding import PartitionSpec as P

HEADS = 16
HEAD_DIM = 64
BLOCK = 128


def padded_2(block, sides, width):
    for axis, dim in sides:
        count = lax.axis_size(axis)
        forward = [(i, i + 1) for i in range(count - 1)]
        backward = [(target, source) for source, target in forward]
        low = lax.ppermute(
            lax.slice_in_dim(block, block.shape[dim] - width, None, axis=dim), axis, forward
        )
        high = lax.ppermute(lax.slice_in_dim(block, 0, width, axis=dim), axis, backward)
        block = jnp.concatenate([low, block, high], axis=dim)
    return block


def from_behind(value, axis, steps):
    count = lax.axis_size(axis)
    leading, last = (max(0, -steps), min(count, count - steps))
    return lax.ppermute(value, axis, [(source, source + steps) for source in range(leading, last)])


def xor_pairs(count, bit):
    return [(source, source ^ (1 << bit)) for source in range(count)]


def own_bit(axis, bit):
    return (lax.axis_index(axis) // (1 << bit)) % 2


def doubling_gather(piece, axis):
    count = lax.axis_size(axis)
    bits = count.bit_length() - 1
    held = piece
    for done, bit in enumerate(reversed(range(bits))):
        other = lax.ppermute(held, axis, xor_pairs(count, bit))
        held = jnp.stack([held, other], axis=done)
    held = held.reshape((count,) + piece.shape)
    return jnp.take(held, jnp.arange(count) ^ lax.axis_index(axis), axis=0)


def halving_scatter(stack, axis):
    count = lax.axis_size(axis)
    bits = count.bit_length() - 1
    held = stack.reshape((2,) * bits + stack.shape[1:])
    for bit in range(bits):
        dim = bits - 1 - bit
        mine = own_bit(axis, bit)
        keep = lax.dynamic_index_in_dim(held, mine, dim, keepdims=False)
        send = lax.dynamic_index_in_dim(held, 1 - mine, dim, keepdims=False)
        held = keep + lax.ppermute(send, axis, xor_pairs(count, bit))
    return held


def doubling_sum(value, axis):
    count = lax.axis_size(axis)
    for bit in range(count.bit_length() - 1):
        value = value + lax.ppermute(value, axis, xor_pairs(count, bit))
    return value


def forward_kernel(term_scale, q_ref, k_ref, v_ref, ck_ref, cv_ref, counts_ref, fine_ref, far_ref,
                   grad_t_ref, att_ref, term_ref):
    score_scale = 1.0 / math.sqrt(HEAD_DIM)
    lanes = q_ref.shape[1]
    low_lanes = lax.broadcasted_iota(jnp.int32, (BLOCK, lanes), 1) < HEAD_DIM
    coarse_k = ck_ref[...]
    coarse_v = cv_ref[...]
    counts = counts_ref[...]
    contract_last = (((1,), (1,)), ((), ()))
    for block in range(q_ref.shape[0] // BLOCK):
        query = q_ref[pl.ds(block * BLOCK, BLOCK), :]
        key_win = k_ref[pl.ds(block * BLOCK, 3 * BLOCK), :]
        value_win = v_ref[pl.ds(block * BLOCK, 3 * BLOCK), :]
        fine_ok = fine_ref[pl.ds(block, 1), :] > 0
        far_ok = far_ref[pl.ds(block, 1), :] > 0
        halves = []
        for half in range(2):
            own = low_lanes if half == 0 else jnp.logical_not(low_lanes)
            query_h = jnp.where(own, query, jnp.zeros_like(query))
            fine_s = lax.dot_general(query_h, key_win, contract_last,
                                     preferred_element_type=jnp.float32) * score_scale
            coarse_s = lax.dot_general(query_h, coarse_k, contract_last,
                                       preferred_element_type=jnp.float32) * score_scale
            fine_s = jnp.where(fine_ok, fine_s, -jnp.inf)
            coarse_s = jnp.where(far_ok, coarse_s, -jnp.inf)
            top = jnp.maximum(jnp.max(fine_s, axis=1, keepdims=True),
                              jnp.max(coarse_s, axis=1, keepdims=True))
            fine_e = jnp.exp(fine_s - top)
            coarse_e = counts * jnp.exp(coarse_s - top)
            total = (jnp.sum(fine_e, axis=1, keepdims=True)
                     + jnp.sum(coarse_e, axis=1, keepdims=True))
            fine_w = (fine_e / total).astype(jnp.bfloat16)
            coarse_w = (coarse_e / total).astype(jnp.bfloat16)
            att = (jnp.dot(fine_w, value_win, preferred_element_type=jnp.float32)
                   + jnp.dot(coarse_w, coarse_v, preferred_element_type=jnp.float32))
            halves.append((att, top, total))
        rows = pl.ds(block * BLOCK, BLOCK)
        att_ref[rows, :] = jnp.where(low_lanes, halves[0][0], halves[1][0]).astype(att_ref.dtype)
    term_ref[...] = jnp.dot(grad_t_ref[...], att_ref[...],
                            preferred_element_type=jnp.float32) * term_scale


def attention_forward(query_rows, padded_k, padded_v, coarse_k, coarse_v, counts, fine_ok, far_ok,
                      grad_t, term_scale):
    tokens, width = query_rows.shape
    lanes = 2 * HEAD_DIM
    by_pair = lambda rows: pl.BlockSpec((rows, lanes), lambda pair: (0, pair))
    whole = lambda shape: pl.BlockSpec(shape, lambda pair: (0, 0))
    return pl.pallas_call(
        functools.partial(forward_kernel, term_scale),
        grid=(width // lanes,),
        in_specs=[
            by_pair(tokens),
            by_pair(padded_k.shape[0]),
            by_pair(padded_v.shape[0]),
            by_pair(coarse_k.shape[0]),
            by_pair(coarse_v.shape[0]),
            whole(counts.shape),
            whole(fine_ok.shape),
            whole(far_ok.shape),
            whole(grad_t.shape),
        ],
        out_specs=[by_pair(tokens), by_pair(grad_t.shape[0])],
        out_shape=[
            jax.ShapeDtypeStruct((tokens, width), jnp.bfloat16),
            jax.ShapeDtypeStruct((grad_t.shape[0], width), jnp.float32),
        ],
    )(query_rows, padded_k, padded_v, coarse_k, coarse_v, counts, fine_ok, far_ok, grad_t)


def backward_kernel(q_ref, k_ref, v_ref, ck_ref, cv_ref, counts_ref, fine_ref, far_ref,
                    g_ref, att_ref, qg_ref, kg_ref, vg_ref, ckg_ref, cvg_ref):
    score_scale = 1.0 / math.sqrt(HEAD_DIM)
    lanes = q_ref.shape[1]
    low_lanes = lax.broadcasted_iota(jnp.int32, (BLOCK, lanes), 1) < HEAD_DIM
    coarse_k = ck_ref[...]
    coarse_v = cv_ref[...]
    counts = counts_ref[...]
    contract_last = (((1,), (1,)), ((), ()))
    kg_ref[...] = jnp.zeros_like(kg_ref)
    vg_ref[...] = jnp.zeros_like(vg_ref)
    coarse_kg = jnp.zeros(ckg_ref.shape, jnp.float32)
    coarse_vg = jnp.zeros(cvg_ref.shape, jnp.float32)
    for block in range(q_ref.shape[0] // BLOCK):
        rows = pl.ds(block * BLOCK, BLOCK)
        window = pl.ds(block * BLOCK, 3 * BLOCK)
        query = q_ref[rows, :]
        grad = g_ref[rows, :]
        att = att_ref[rows, :].astype(jnp.float32)
        key_win = k_ref[window, :]
        value_win = v_ref[window, :]
        fine_ok = fine_ref[pl.ds(block, 1), :] > 0
        far_ok = far_ref[pl.ds(block, 1), :] > 0
        query_grads = []
        key_grad = jnp.zeros((3 * BLOCK, lanes), jnp.float32)
        value_grad = jnp.zeros((3 * BLOCK, lanes), jnp.float32)
        for half in range(2):
            own = low_lanes if half == 0 else jnp.logical_not(low_lanes)
            query_h = jnp.where(own, query, jnp.zeros_like(query))
            grad_h = jnp.where(own, grad, jnp.zeros_like(grad))
            fine_s = lax.dot_general(query_h, key_win, contract_last,
                                     preferred_element_type=jnp.float32) * score_scale
            coarse_s = lax.dot_general(query_h, coarse_k, contract_last,
                                       preferred_element_type=jnp.float32) * score_scale
            fine_s = jnp.where(fine_ok, fine_s, -jnp.inf)
            coarse_s = jnp.where(far_ok, coarse_s, -jnp.inf)
            top = jnp.maximum(jnp.max(fine_s, axis=1, keepdims=True),
                              jnp.max(coarse_s, axis=1, keepdims=True))
            fine_e = jnp.exp(fine_s - top)
            coarse_e = counts * jnp.exp(coarse_s - top)
            total = (jnp.sum(fine_e, axis=1, keepdims=True)
                     + jnp.sum(coarse_e, axis=1, keepdims=True))
            fine_w = fine_e / total
            coarse_w = coarse_e / total
            fine_dot = lax.dot_general(grad_h, value_win, contract_last,
                                       preferred_element_type=jnp.float32)
            coarse_dot = lax.dot_general(grad_h, coarse_v, contract_last,
                                         preferred_element_type=jnp.float32)
            delta = jnp.sum(jnp.where(own, grad.astype(jnp.float32) * att, 0.0),
                            axis=1, keepdims=True)
            fine_ds = fine_w * (fine_dot - delta)
            coarse_ds = coarse_w * (coarse_dot - delta)
            fine_ds_b = fine_ds.astype(jnp.bfloat16)
            coarse_ds_b = coarse_ds.astype(jnp.bfloat16)
            query_grads.append(
                (jnp.dot(fine_ds_b, key_win, preferred_element_type=jnp.float32)
                 + jnp.dot(coarse_ds_b, coarse_k, preferred_element_type=jnp.float32))
                * score_scale)
            fine_ds_t = fine_ds.T.astype(jnp.bfloat16)
            coarse_ds_t = coarse_ds.T.astype(jnp.bfloat16)
            fine_w_t = fine_w.T.astype(jnp.bfloat16)
            coarse_w_t = coarse_w.T.astype(jnp.bfloat16)
            key_grad = key_grad + jnp.dot(fine_ds_t, query_h,
                                          preferred_element_type=jnp.float32) * score_scale
            value_grad = value_grad + jnp.dot(fine_w_t, grad_h,
                                              preferred_element_type=jnp.float32)
            coarse_kg = coarse_kg + jnp.dot(coarse_ds_t, query_h,
                                            preferred_element_type=jnp.float32) * score_scale
            coarse_vg = coarse_vg + jnp.dot(coarse_w_t, grad_h,
                                            preferred_element_type=jnp.float32)
        qg_ref[rows, :] = jnp.where(low_lanes, query_grads[0], query_grads[1]).astype(qg_ref.dtype)
        kg_ref[window, :] += key_grad
        vg_ref[window, :] += value_grad
    ckg_ref[...] = coarse_kg
    cvg_ref[...] = coarse_vg


def attention_backward(query_rows, padded_k, padded_v, coarse_k, coarse_v, counts, fine_ok,
                       far_ok, grad_rows, attended_rows):
    tokens, width = query_rows.shape
    lanes = 2 * HEAD_DIM
    by_pair = lambda rows: pl.BlockSpec((rows, lanes), lambda pair: (0, pair))
    whole = lambda shape: pl.BlockSpec(shape, lambda pair: (0, 0))
    wide = lambda rows: jax.ShapeDtypeStruct((rows, width), jnp.float32)
    return pl.pallas_call(
        backward_kernel,
        grid=(width // lanes,),
        in_specs=[
            by_pair(tokens),
            by_pair(padded_k.shape[0]),
            by_pair(padded_v.shape[0]),
            by_pair(coarse_k.shape[0]),
            by_pair(coarse_v.shape[0]),
            whole(counts.shape),
            whole(fine_ok.shape),
            whole(far_ok.shape),
            by_pair(tokens),
            by_pair(tokens),
        ],
        out_specs=[
            by_pair(tokens),
            by_pair(padded_k.shape[0]),
            by_pair(padded_v.shape[0]),
            by_pair(coarse_k.shape[0]),
            by_pair(coarse_v.shape[0]),
        ],
        out_shape=[
            jax.ShapeDtypeStruct((tokens, width), jnp.bfloat16),
            wide(padded_k.shape[0]),
            wide(padded_v.shape[0]),
            wide(coarse_k.shape[0]),
            wide(coarse_v.shape[0]),
        ],
    )(query_rows, padded_k, padded_v, coarse_k, coarse_v, counts, fine_ok, far_ok, grad_rows,
      attended_rows)


def block_windows(padded, local_blocks):
    return jnp.concatenate(
        [padded[0:local_blocks], padded[1 : local_blocks + 1], padded[2 : local_blocks + 2]], axis=1
    )


def fold_windows(grads, local_blocks):
    parts = grads.reshape((local_blocks, 3, BLOCK) + grads.shape[2:])
    edge_zero = jnp.zeros((1,) + parts.shape[2:], jnp.float32)
    left_part = jnp.concatenate([parts[:, 0], edge_zero, edge_zero], axis=0)
    middle = jnp.concatenate([edge_zero, parts[:, 1], edge_zero], axis=0)
    right_part = jnp.concatenate([edge_zero, edge_zero, parts[:, 2]], axis=0)
    return left_part + middle + right_part


def per_device(queries, keys, values, out_weight, out_grad, pooled):
    query_rows = queries[0]
    key_rows = keys[0]
    value_rows = values[0]
    grad_out = out_grad[0]
    tokens, model_width = query_rows.shape
    local_blocks = tokens // BLOCK
    seq_devices = lax.axis_size("seq")
    seq_index = lax.axis_index("seq")
    all_blocks = local_blocks * seq_devices
    score_scale = 1.0 / math.sqrt(HEAD_DIM)
    pooled_mask = pooled[0].reshape(local_blocks, BLOCK).astype(jnp.float32)
    counts = jnp.sum(pooled_mask, axis=1)
    divisor = jnp.maximum(counts, 1.0)
    pooled_bf = pooled_mask.astype(jnp.bfloat16)
    key_sum = jnp.einsum(
        "nb,nbd->nd",
        pooled_bf,
        key_rows.reshape(local_blocks, BLOCK, model_width),
        preferred_element_type=jnp.float32,
    )
    value_sum = jnp.einsum(
        "nb,nbd->nd",
        pooled_bf,
        value_rows.reshape(local_blocks, BLOCK, model_width),
        preferred_element_type=jnp.float32,
    )
    coarse_keys = (key_sum / divisor[:, None]).astype(jnp.bfloat16)
    coarse_values = (value_sum / divisor[:, None]).astype(jnp.bfloat16)
    count_cols = jnp.broadcast_to(counts.astype(jnp.bfloat16)[:, None], (local_blocks, 128))
    packed = jnp.concatenate([coarse_keys, coarse_values, count_cols], axis=1)
    gathered = doubling_gather(packed, "seq").reshape(all_blocks, packed.shape[1])
    gathered_keys = gathered[:, :model_width]
    gathered_values = gathered[:, model_width : 2 * model_width]
    gathered_counts = gathered[:, 2 * model_width].astype(jnp.float32)
    paired = jnp.stack([key_rows, value_rows])
    extended = padded_2(paired, (("seq", 1),), BLOCK)
    padded_kv = extended.reshape(2, local_blocks + 2, BLOCK, HEADS, HEAD_DIM)
    local_ids = seq_index * local_blocks + jnp.arange(local_blocks)
    offsets = jnp.repeat(jnp.arange(3) - 1, BLOCK)
    key_blocks = local_ids[:, None] + offsets[None, :]
    fine_ok = (key_blocks >= 0) & (key_blocks < all_blocks)
    far_ok = jnp.abs(local_ids[:, None] - jnp.arange(all_blocks)[None, :]) >= 2
    padded_rows = extended.reshape(2, (local_blocks + 2) * BLOCK, model_width)
    grad_norm = 1.0 / math.sqrt(seq_devices * tokens)
    attended_rows, full_term = attention_forward(
        query_rows,
        padded_rows[0],
        padded_rows[1],
        gathered_keys,
        gathered_values,
        gathered_counts[None, :],
        fine_ok.astype(jnp.float32),
        far_ok.astype(jnp.float32),
        grad_out.T,
        grad_norm,
    )
    attended_grad = jnp.dot(grad_out, out_weight, preferred_element_type=jnp.float32).astype(
        jnp.bfloat16
    )
    seq_part = lax.psum_scatter(full_term, "seq", scatter_dimension=0, tiled=True)
    full_term, attended_grad = lax.optimization_barrier((full_term, attended_grad))
    query_grad, key_pad, value_pad, coarse_key_all, coarse_value_all = attention_backward(
        query_rows,
        padded_rows[0],
        padded_rows[1],
        gathered_keys,
        gathered_values,
        gathered_counts[None, :],
        fine_ok.astype(jnp.float32),
        far_ok.astype(jnp.float32),
        attended_grad,
        attended_rows,
    )
    query_grad = query_grad.reshape(1, tokens, model_width)
    key_ext = key_pad.reshape(local_blocks + 2, BLOCK, model_width)
    value_ext = value_pad.reshape(local_blocks + 2, BLOCK, model_width)
    edge_first = jnp.stack([key_ext[0], value_ext[0]])
    edge_last = jnp.stack([key_ext[local_blocks + 1], value_ext[local_blocks + 1]])
    from_right = from_behind(edge_first, "seq", -1)
    from_left = from_behind(edge_last, "seq", 1)
    zeros_mid = jnp.zeros((2, local_blocks - 1, BLOCK, model_width), jnp.float32)
    boundary = jnp.concatenate([from_left[:, None], zeros_mid], axis=1) + jnp.concatenate(
        [zeros_mid, from_right[:, None]], axis=1
    )
    coarse_all = jnp.concatenate(
        [
            coarse_key_all.reshape(all_blocks, model_width),
            coarse_value_all.reshape(all_blocks, model_width),
        ],
        axis=1,
    )
    owned_grads = halving_scatter(
        coarse_all.reshape(seq_devices, local_blocks, 2 * model_width), "seq"
    )
    owned_keys = owned_grads[:, :model_width] / divisor[:, None]
    owned_values = owned_grads[:, model_width:] / divisor[:, None]
    spread_keys = owned_keys[:, None, :] * pooled_mask[:, :, None]
    spread_values = owned_values[:, None, :] * pooled_mask[:, :, None]
    key_grad = (
        (key_ext[1 : local_blocks + 1] + boundary[0] + spread_keys)
        .astype(jnp.bfloat16)
        .reshape(1, tokens, model_width)
    )
    value_grad = (
        (value_ext[1 : local_blocks + 1] + boundary[1] + spread_values)
        .astype(jnp.bfloat16)
        .reshape(1, tokens, model_width)
    )
    seq_part, query_grad, key_grad, value_grad = lax.optimization_barrier(
        (seq_part, query_grad, key_grad, value_grad)
    )
    dp_devices = lax.axis_size("dp")
    dp_rows = halving_scatter(seq_part.reshape(dp_devices, -1, model_width), "dp")
    weight_grad = doubling_gather(dp_rows, "dp").reshape(-1, model_width)
    return (query_grad, key_grad, value_grad, weight_grad)


def solution(mesh):
    placed = (
        P("dp", "seq", None),
        P("dp", "seq", None),
        P("dp", "seq", None),
        P(),
        P("dp", "seq", None),
        P("dp", "seq"),
    )
    return jax.shard_map(
        per_device,
        mesh=mesh,
        in_specs=placed,
        out_specs=(
            P("dp", "seq", None),
            P("dp", "seq", None),
            P("dp", "seq", None),
            P("seq", None),
        ),
        check_vma=False,
    )
```

```python
import functools
import math

import jax
import jax.numpy as jnp
from jax import lax
from jax.experimental import pallas as pl
from jax.experimental.pallas import tpu as pltpu
from jax.sharding import PartitionSpec as P

HEADS = 16
HEAD_DIM = 64
BLOCK = 128


def padded_2(block, sides, width):
    for axis, dim in sides:
        count = lax.axis_size(axis)
        forward = [(i, i + 1) for i in range(count - 1)]
        backward = [(target, source) for source, target in forward]
        low = lax.ppermute(
            lax.slice_in_dim(block, block.shape[dim] - width, None, axis=dim), axis, forward
        )
        high = lax.ppermute(lax.slice_in_dim(block, 0, width, axis=dim), axis, backward)
        block = jnp.concatenate([low, block, high], axis=dim)
    return block


def from_behind(value, axis, steps):
    count = lax.axis_size(axis)
    leading, last = (max(0, -steps), min(count, count - steps))
    return lax.ppermute(value, axis, [(source, source + steps) for source in range(leading, last)])


def xor_pairs(count, bit):
    return [(source, source ^ (1 << bit)) for source in range(count)]


def own_bit(axis, bit):
    return (lax.axis_index(axis) // (1 << bit)) % 2


def doubling_gather(piece, axis):
    count = lax.axis_size(axis)
    bits = count.bit_length() - 1
    held = piece
    for done, bit in enumerate(reversed(range(bits))):
        other = lax.ppermute(held, axis, xor_pairs(count, bit))
        mine_low = own_bit(axis, bit) == 0
        low = jnp.where(mine_low, held, other)
        high = jnp.where(mine_low, other, held)
        held = jnp.stack([low, high], axis=done)
    return held.reshape((count,) + piece.shape)


def halving_scatter(stack, axis):
    count = lax.axis_size(axis)
    bits = count.bit_length() - 1
    held = stack.reshape((2,) * bits + stack.shape[1:])
    for bit in range(bits):
        dim = bits - 1 - bit
        mine = own_bit(axis, bit)
        keep = lax.dynamic_index_in_dim(held, mine, dim, keepdims=False)
        send = lax.dynamic_index_in_dim(held, 1 - mine, dim, keepdims=False)
        held = keep + lax.ppermute(send, axis, xor_pairs(count, bit))
    return held


def doubling_sum(value, axis):
    count = lax.axis_size(axis)
    for bit in range(count.bit_length() - 1):
        value = value + lax.ppermute(value, axis, xor_pairs(count, bit))
    return value


def forward_kernel(term_scale, q_ref, k_ref, v_ref, ck_ref, cv_ref, counts_ref, fine_ref, far_ref,
                   grad_t_ref, att_ref, term_ref):
    score_scale = 1.0 / math.sqrt(HEAD_DIM)
    lanes = q_ref.shape[1]
    lane_head = lax.broadcasted_iota(jnp.int32, (BLOCK, lanes), 1) // HEAD_DIM
    coarse_k = ck_ref[...]
    coarse_v = cv_ref[...]
    counts = counts_ref[...]
    contract_last = (((1,), (1,)), ((), ()))
    for block in range(q_ref.shape[0] // BLOCK):
        query = q_ref[pl.ds(block * BLOCK, BLOCK), :]
        key_win = k_ref[pl.ds(block * BLOCK, 3 * BLOCK), :]
        value_win = v_ref[pl.ds(block * BLOCK, 3 * BLOCK), :]
        fine_ok = fine_ref[pl.ds(block, 1), :] > 0
        far_ok = far_ref[pl.ds(block, 1), :] > 0
        att_all = None
        for half in range(lanes // HEAD_DIM):
            own = lane_head == half
            query_h = jnp.where(own, query, jnp.zeros_like(query))
            fine_s = lax.dot_general(query_h, key_win, contract_last,
                                     preferred_element_type=jnp.float32) * score_scale
            coarse_s = lax.dot_general(query_h, coarse_k, contract_last,
                                       preferred_element_type=jnp.float32) * score_scale
            fine_s = jnp.where(fine_ok, fine_s, -jnp.inf)
            coarse_s = jnp.where(far_ok, coarse_s, -jnp.inf)
            top = jnp.maximum(jnp.max(fine_s, axis=1, keepdims=True),
                              jnp.max(coarse_s, axis=1, keepdims=True))
            fine_e = jnp.exp(fine_s - top)
            coarse_e = counts * jnp.exp(coarse_s - top)
            total = (jnp.sum(fine_e, axis=1, keepdims=True)
                     + jnp.sum(coarse_e, axis=1, keepdims=True))
            fine_w = (fine_e / total).astype(jnp.bfloat16)
            coarse_w = (coarse_e / total).astype(jnp.bfloat16)
            att = (jnp.dot(fine_w, value_win, preferred_element_type=jnp.float32)
                   + jnp.dot(coarse_w, coarse_v, preferred_element_type=jnp.float32))
            att_all = att if att_all is None else jnp.where(own, att, att_all)
        rows = pl.ds(block * BLOCK, BLOCK)
        att_ref[rows, :] = att_all.astype(att_ref.dtype)
    term_ref[...] = jnp.dot(grad_t_ref[...], att_ref[...],
                            preferred_element_type=jnp.float32) * term_scale


def attention_forward(query_rows, padded_k, padded_v, coarse_k, coarse_v, counts, fine_ok, far_ok,
                      grad_t, term_scale):
    tokens, width = query_rows.shape
    lanes = 4 * HEAD_DIM
    by_pair = lambda rows: pl.BlockSpec((rows, lanes), lambda pair: (0, pair))
    whole = lambda shape: pl.BlockSpec(shape, lambda pair: (0, 0))
    return pl.pallas_call(
        functools.partial(forward_kernel, term_scale),
        grid=(width // lanes,),
        in_specs=[
            by_pair(tokens),
            by_pair(padded_k.shape[0]),
            by_pair(padded_v.shape[0]),
            by_pair(coarse_k.shape[0]),
            by_pair(coarse_v.shape[0]),
            whole(counts.shape),
            whole(fine_ok.shape),
            whole(far_ok.shape),
            whole(grad_t.shape),
        ],
        out_specs=[by_pair(tokens), by_pair(grad_t.shape[0])],
        out_shape=[
            jax.ShapeDtypeStruct((tokens, width), jnp.bfloat16),
            jax.ShapeDtypeStruct((grad_t.shape[0], width), jnp.float32),
        ],
    )(query_rows, padded_k, padded_v, coarse_k, coarse_v, counts, fine_ok, far_ok, grad_t)


def backward_kernel(q_ref, k_ref, v_ref, ck_ref, cv_ref, counts_ref, fine_ref, far_ref,
                    g_ref, att_ref, qg_ref, kg_ref, vg_ref, ckg_ref, cvg_ref):
    score_scale = 1.0 / math.sqrt(HEAD_DIM)
    lanes = q_ref.shape[1]
    low_lanes = lax.broadcasted_iota(jnp.int32, (BLOCK, lanes), 1) < HEAD_DIM
    coarse_k = ck_ref[...]
    coarse_v = cv_ref[...]
    counts = counts_ref[...]
    contract_last = (((1,), (1,)), ((), ()))
    kg_ref[...] = jnp.zeros_like(kg_ref)
    vg_ref[...] = jnp.zeros_like(vg_ref)
    coarse_kg = jnp.zeros(ckg_ref.shape, jnp.float32)
    coarse_vg = jnp.zeros(cvg_ref.shape, jnp.float32)
    for block in range(q_ref.shape[0] // BLOCK):
        rows = pl.ds(block * BLOCK, BLOCK)
        window = pl.ds(block * BLOCK, 3 * BLOCK)
        query = q_ref[rows, :]
        grad = g_ref[rows, :]
        att = att_ref[rows, :].astype(jnp.float32)
        key_win = k_ref[window, :]
        value_win = v_ref[window, :]
        fine_ok = fine_ref[pl.ds(block, 1), :] > 0
        far_ok = far_ref[pl.ds(block, 1), :] > 0
        query_grads = []
        key_grad = jnp.zeros((3 * BLOCK, lanes), jnp.float32)
        value_grad = jnp.zeros((3 * BLOCK, lanes), jnp.float32)
        for half in range(2):
            own = low_lanes if half == 0 else jnp.logical_not(low_lanes)
            query_h = jnp.where(own, query, jnp.zeros_like(query))
            grad_h = jnp.where(own, grad, jnp.zeros_like(grad))
            fine_s = lax.dot_general(query_h, key_win, contract_last,
                                     preferred_element_type=jnp.float32) * score_scale
            coarse_s = lax.dot_general(query_h, coarse_k, contract_last,
                                       preferred_element_type=jnp.float32) * score_scale
            fine_s = jnp.where(fine_ok, fine_s, -jnp.inf)
            coarse_s = jnp.where(far_ok, coarse_s, -jnp.inf)
            top = jnp.maximum(jnp.max(fine_s, axis=1, keepdims=True),
                              jnp.max(coarse_s, axis=1, keepdims=True))
            fine_e = jnp.exp(fine_s - top)
            coarse_e = counts * jnp.exp(coarse_s - top)
            total = (jnp.sum(fine_e, axis=1, keepdims=True)
                     + jnp.sum(coarse_e, axis=1, keepdims=True))
            fine_w = fine_e / total
            coarse_w = coarse_e / total
            fine_dot = lax.dot_general(grad_h, value_win, contract_last,
                                       preferred_element_type=jnp.float32)
            coarse_dot = lax.dot_general(grad_h, coarse_v, contract_last,
                                         preferred_element_type=jnp.float32)
            delta = jnp.sum(jnp.where(own, grad.astype(jnp.float32) * att, 0.0),
                            axis=1, keepdims=True)
            fine_ds = fine_w * (fine_dot - delta)
            coarse_ds = coarse_w * (coarse_dot - delta)
            fine_ds_b = fine_ds.astype(jnp.bfloat16)
            coarse_ds_b = coarse_ds.astype(jnp.bfloat16)
            query_grads.append(
                (jnp.dot(fine_ds_b, key_win, preferred_element_type=jnp.float32)
                 + jnp.dot(coarse_ds_b, coarse_k, preferred_element_type=jnp.float32))
                * score_scale)
            fine_ds_t = fine_ds.T.astype(jnp.bfloat16)
            coarse_ds_t = coarse_ds.T.astype(jnp.bfloat16)
            fine_w_t = fine_w.T.astype(jnp.bfloat16)
            coarse_w_t = coarse_w.T.astype(jnp.bfloat16)
            key_grad = key_grad + jnp.dot(fine_ds_t, query_h,
                                          preferred_element_type=jnp.float32) * score_scale
            value_grad = value_grad + jnp.dot(fine_w_t, grad_h,
                                              preferred_element_type=jnp.float32)
            coarse_kg = coarse_kg + jnp.dot(coarse_ds_t, query_h,
                                            preferred_element_type=jnp.float32) * score_scale
            coarse_vg = coarse_vg + jnp.dot(coarse_w_t, grad_h,
                                            preferred_element_type=jnp.float32)
        qg_ref[rows, :] = jnp.where(low_lanes, query_grads[0], query_grads[1]).astype(qg_ref.dtype)
        kg_ref[window, :] += key_grad
        vg_ref[window, :] += value_grad
    ckg_ref[...] = coarse_kg
    cvg_ref[...] = coarse_vg


def attention_backward(query_rows, padded_k, padded_v, coarse_k, coarse_v, counts, fine_ok,
                       far_ok, grad_rows, attended_rows):
    tokens, width = query_rows.shape
    lanes = 2 * HEAD_DIM
    by_pair = lambda rows: pl.BlockSpec((rows, lanes), lambda pair: (0, pair))
    whole = lambda shape: pl.BlockSpec(shape, lambda pair: (0, 0))
    wide = lambda rows: jax.ShapeDtypeStruct((rows, width), jnp.float32)
    return pl.pallas_call(
        backward_kernel,
        grid=(width // lanes,),
        in_specs=[
            by_pair(tokens),
            by_pair(padded_k.shape[0]),
            by_pair(padded_v.shape[0]),
            by_pair(coarse_k.shape[0]),
            by_pair(coarse_v.shape[0]),
            whole(counts.shape),
            whole(fine_ok.shape),
            whole(far_ok.shape),
            by_pair(tokens),
            by_pair(tokens),
        ],
        out_specs=[
            by_pair(tokens),
            by_pair(padded_k.shape[0]),
            by_pair(padded_v.shape[0]),
            by_pair(coarse_k.shape[0]),
            by_pair(coarse_v.shape[0]),
        ],
        out_shape=[
            jax.ShapeDtypeStruct((tokens, width), jnp.bfloat16),
            wide(padded_k.shape[0]),
            wide(padded_v.shape[0]),
            wide(coarse_k.shape[0]),
            wide(coarse_v.shape[0]),
        ],
    )(query_rows, padded_k, padded_v, coarse_k, coarse_v, counts, fine_ok, far_ok, grad_rows,
      attended_rows)


def block_windows(padded, local_blocks):
    return jnp.concatenate(
        [padded[0:local_blocks], padded[1 : local_blocks + 1], padded[2 : local_blocks + 2]], axis=1
    )


def fold_windows(grads, local_blocks):
    parts = grads.reshape((local_blocks, 3, BLOCK) + grads.shape[2:])
    edge_zero = jnp.zeros((1,) + parts.shape[2:], jnp.float32)
    left_part = jnp.concatenate([parts[:, 0], edge_zero, edge_zero], axis=0)
    middle = jnp.concatenate([edge_zero, parts[:, 1], edge_zero], axis=0)
    right_part = jnp.concatenate([edge_zero, edge_zero, parts[:, 2]], axis=0)
    return left_part + middle + right_part


def per_device(queries, keys, values, out_weight, out_grad, pooled):
    query_rows = queries[0]
    key_rows = keys[0]
    value_rows = values[0]
    grad_out = out_grad[0]
    tokens, model_width = query_rows.shape
    local_blocks = tokens // BLOCK
    seq_devices = lax.axis_size("seq")
    seq_index = lax.axis_index("seq")
    all_blocks = local_blocks * seq_devices
    score_scale = 1.0 / math.sqrt(HEAD_DIM)
    pooled_mask = pooled[0].reshape(local_blocks, BLOCK).astype(jnp.float32)
    counts = jnp.sum(pooled_mask, axis=1)
    divisor = jnp.maximum(counts, 1.0)
    pooled_bf = pooled_mask.astype(jnp.bfloat16)
    key_sum = jnp.einsum(
        "nb,nbd->nd",
        pooled_bf,
        key_rows.reshape(local_blocks, BLOCK, model_width),
        preferred_element_type=jnp.float32,
    )
    value_sum = jnp.einsum(
        "nb,nbd->nd",
        pooled_bf,
        value_rows.reshape(local_blocks, BLOCK, model_width),
        preferred_element_type=jnp.float32,
    )
    coarse_keys = (key_sum / divisor[:, None]).astype(jnp.bfloat16)
    coarse_values = (value_sum / divisor[:, None]).astype(jnp.bfloat16)
    count_cols = jnp.broadcast_to(counts.astype(jnp.bfloat16)[:, None], (local_blocks, 128))
    packed = jnp.concatenate([coarse_keys, coarse_values, count_cols], axis=1)
    gathered = doubling_gather(packed, "seq").reshape(all_blocks, packed.shape[1])
    gathered_keys = gathered[:, :model_width]
    gathered_values = gathered[:, model_width : 2 * model_width]
    gathered_counts = gathered[:, 2 * model_width].astype(jnp.float32)
    paired = jnp.stack([key_rows, value_rows])
    extended = padded_2(paired, (("seq", 1),), BLOCK)
    padded_kv = extended.reshape(2, local_blocks + 2, BLOCK, HEADS, HEAD_DIM)
    local_ids = seq_index * local_blocks + jnp.arange(local_blocks)
    offsets = jnp.repeat(jnp.arange(3) - 1, BLOCK)
    key_blocks = local_ids[:, None] + offsets[None, :]
    fine_ok = (key_blocks >= 0) & (key_blocks < all_blocks)
    far_ok = jnp.abs(local_ids[:, None] - jnp.arange(all_blocks)[None, :]) >= 2
    padded_rows = extended.reshape(2, (local_blocks + 2) * BLOCK, model_width)
    grad_norm = 1.0 / math.sqrt(seq_devices * tokens)
    attended_rows, full_term = attention_forward(
        query_rows,
        padded_rows[0],
        padded_rows[1],
        gathered_keys,
        gathered_values,
        gathered_counts[None, :],
        fine_ok.astype(jnp.float32),
        far_ok.astype(jnp.float32),
        grad_out.T,
        grad_norm,
    )
    attended_grad = jnp.dot(grad_out, out_weight, preferred_element_type=jnp.float32).astype(
        jnp.bfloat16
    )
    seq_part = lax.psum_scatter(full_term, "seq", scatter_dimension=0, tiled=True)
    full_term, attended_grad = lax.optimization_barrier((full_term, attended_grad))
    query_grad, key_pad, value_pad, coarse_key_all, coarse_value_all = attention_backward(
        query_rows,
        padded_rows[0],
        padded_rows[1],
        gathered_keys,
        gathered_values,
        gathered_counts[None, :],
        fine_ok.astype(jnp.float32),
        far_ok.astype(jnp.float32),
        attended_grad,
        attended_rows,
    )
    query_grad = query_grad.reshape(1, tokens, model_width)
    key_ext = key_pad.reshape(local_blocks + 2, BLOCK, model_width)
    value_ext = value_pad.reshape(local_blocks + 2, BLOCK, model_width)
    edge_first = jnp.stack([key_ext[0], value_ext[0]])
    edge_last = jnp.stack([key_ext[local_blocks + 1], value_ext[local_blocks + 1]])
    from_right = from_behind(edge_first, "seq", -1)
    from_left = from_behind(edge_last, "seq", 1)
    zeros_mid = jnp.zeros((2, local_blocks - 1, BLOCK, model_width), jnp.float32)
    boundary = jnp.concatenate([from_left[:, None], zeros_mid], axis=1) + jnp.concatenate(
        [zeros_mid, from_right[:, None]], axis=1
    )
    coarse_all = jnp.concatenate(
        [
            coarse_key_all.reshape(all_blocks, model_width),
            coarse_value_all.reshape(all_blocks, model_width),
        ],
        axis=1,
    )
    owned_grads = halving_scatter(
        coarse_all.reshape(seq_devices, local_blocks, 2 * model_width), "seq"
    )
    owned_keys = owned_grads[:, :model_width] / divisor[:, None]
    owned_values = owned_grads[:, model_width:] / divisor[:, None]
    spread_keys = owned_keys[:, None, :] * pooled_mask[:, :, None]
    spread_values = owned_values[:, None, :] * pooled_mask[:, :, None]
    key_grad = (
        (key_ext[1 : local_blocks + 1] + boundary[0] + spread_keys)
        .astype(jnp.bfloat16)
        .reshape(1, tokens, model_width)
    )
    value_grad = (
        (value_ext[1 : local_blocks + 1] + boundary[1] + spread_values)
        .astype(jnp.bfloat16)
        .reshape(1, tokens, model_width)
    )
    seq_part, query_grad, key_grad, value_grad = lax.optimization_barrier(
        (seq_part, query_grad, key_grad, value_grad)
    )
    dp_devices = lax.axis_size("dp")
    dp_rows = halving_scatter(seq_part.reshape(dp_devices, -1, model_width), "dp")
    weight_grad = doubling_gather(dp_rows, "dp").reshape(-1, model_width)
    return (query_grad, key_grad, value_grad, weight_grad)


def solution(mesh):
    placed = (
        P("dp", "seq", None),
        P("dp", "seq", None),
        P("dp", "seq", None),
        P(),
        P("dp", "seq", None),
        P("dp", "seq"),
    )
    return jax.shard_map(
        per_device,
        mesh=mesh,
        in_specs=placed,
        out_specs=(
            P("dp", "seq", None),
            P("dp", "seq", None),
            P("dp", "seq", None),
            P("seq", None),
        ),
        check_vma=False,
    )
```

```python
import functools
import math

import jax
import jax.numpy as jnp
from jax import lax
from jax.experimental import pallas as pl
from jax.experimental.pallas import tpu as pltpu
from jax.sharding import PartitionSpec as P

HEADS = 16
HEAD_DIM = 64
BLOCK = 128


def padded_2(block, sides, width):
    for axis, dim in sides:
        count = lax.axis_size(axis)
        forward = [(i, i + 1) for i in range(count - 1)]
        backward = [(target, source) for source, target in forward]
        low = lax.ppermute(
            lax.slice_in_dim(block, block.shape[dim] - width, None, axis=dim), axis, forward
        )
        high = lax.ppermute(lax.slice_in_dim(block, 0, width, axis=dim), axis, backward)
        block = jnp.concatenate([low, block, high], axis=dim)
    return block


def from_behind(value, axis, steps):
    count = lax.axis_size(axis)
    leading, last = (max(0, -steps), min(count, count - steps))
    return lax.ppermute(value, axis, [(source, source + steps) for source in range(leading, last)])


def xor_pairs(count, bit):
    return [(source, source ^ (1 << bit)) for source in range(count)]


def own_bit(axis, bit):
    return (lax.axis_index(axis) // (1 << bit)) % 2


def doubling_gather(piece, axis):
    count = lax.axis_size(axis)
    bits = count.bit_length() - 1
    held = piece
    for done, bit in enumerate(reversed(range(bits))):
        other = lax.ppermute(held, axis, xor_pairs(count, bit))
        mine_low = own_bit(axis, bit) == 0
        low = jnp.where(mine_low, held, other)
        high = jnp.where(mine_low, other, held)
        held = jnp.stack([low, high], axis=done)
    return held.reshape((count,) + piece.shape)


def halving_scatter(stack, axis):
    count = lax.axis_size(axis)
    bits = count.bit_length() - 1
    held = stack.reshape((2,) * bits + stack.shape[1:])
    for bit in range(bits):
        dim = bits - 1 - bit
        mine = own_bit(axis, bit)
        keep = lax.dynamic_index_in_dim(held, mine, dim, keepdims=False)
        send = lax.dynamic_index_in_dim(held, 1 - mine, dim, keepdims=False)
        held = keep + lax.ppermute(send, axis, xor_pairs(count, bit))
    return held


def doubling_sum(value, axis):
    count = lax.axis_size(axis)
    for bit in range(count.bit_length() - 1):
        value = value + lax.ppermute(value, axis, xor_pairs(count, bit))
    return value


def forward_kernel(term_scale, q_ref, k_ref, v_ref, ck_ref, cv_ref, counts_ref, fine_ref, far_ref,
                   grad_t_ref, att_ref, term_ref):
    score_scale = 1.0 / math.sqrt(HEAD_DIM)
    lanes = q_ref.shape[1]
    lane_head = lax.broadcasted_iota(jnp.int32, (BLOCK, lanes), 1) // HEAD_DIM
    coarse_k = ck_ref[...]
    coarse_v = cv_ref[...]
    counts = counts_ref[...]
    contract_last = (((1,), (1,)), ((), ()))
    for block in range(q_ref.shape[0] // BLOCK):
        query = q_ref[pl.ds(block * BLOCK, BLOCK), :]
        key_win = k_ref[pl.ds(block * BLOCK, 3 * BLOCK), :]
        value_win = v_ref[pl.ds(block * BLOCK, 3 * BLOCK), :]
        fine_ok = fine_ref[pl.ds(block, 1), :] > 0
        far_ok = far_ref[pl.ds(block, 1), :] > 0
        att_all = None
        for half in range(lanes // HEAD_DIM):
            own = lane_head == half
            query_h = jnp.where(own, query, jnp.zeros_like(query))
            fine_s = lax.dot_general(query_h, key_win, contract_last,
                                     preferred_element_type=jnp.float32) * score_scale
            coarse_s = lax.dot_general(query_h, coarse_k, contract_last,
                                       preferred_element_type=jnp.float32) * score_scale
            fine_s = jnp.where(fine_ok, fine_s, -jnp.inf)
            coarse_s = jnp.where(far_ok, coarse_s, -jnp.inf)
            top = jnp.maximum(jnp.max(fine_s, axis=1, keepdims=True),
                              jnp.max(coarse_s, axis=1, keepdims=True))
            fine_e = jnp.exp(fine_s - top)
            coarse_e = counts * jnp.exp(coarse_s - top)
            total = (jnp.sum(fine_e, axis=1, keepdims=True)
                     + jnp.sum(coarse_e, axis=1, keepdims=True))
            fine_w = (fine_e / total).astype(jnp.bfloat16)
            coarse_w = (coarse_e / total).astype(jnp.bfloat16)
            att = (jnp.dot(fine_w, value_win, preferred_element_type=jnp.float32)
                   + jnp.dot(coarse_w, coarse_v, preferred_element_type=jnp.float32))
            att_all = att if att_all is None else jnp.where(own, att, att_all)
        rows = pl.ds(block * BLOCK, BLOCK)
        att_ref[rows, :] = att_all.astype(att_ref.dtype)
    term_ref[...] = jnp.dot(grad_t_ref[...], att_ref[...],
                            preferred_element_type=jnp.float32) * term_scale


def attention_forward(query_rows, padded_k, padded_v, coarse_k, coarse_v, counts, fine_ok, far_ok,
                      grad_t, term_scale):
    tokens, width = query_rows.shape
    lanes = 4 * HEAD_DIM
    by_pair = lambda rows: pl.BlockSpec((rows, lanes), lambda pair: (0, pair))
    whole = lambda shape: pl.BlockSpec(shape, lambda pair: (0, 0))
    return pl.pallas_call(
        functools.partial(forward_kernel, term_scale),
        grid=(width // lanes,),
        in_specs=[
            by_pair(tokens),
            by_pair(padded_k.shape[0]),
            by_pair(padded_v.shape[0]),
            by_pair(coarse_k.shape[0]),
            pl.BlockSpec((coarse_v.shape[0], lanes), lambda pair: (0, pair + width // lanes)),
            whole(counts.shape),
            whole(fine_ok.shape),
            whole(far_ok.shape),
            whole(grad_t.shape),
        ],
        out_specs=[by_pair(tokens), by_pair(grad_t.shape[0])],
        out_shape=[
            jax.ShapeDtypeStruct((tokens, width), jnp.bfloat16),
            jax.ShapeDtypeStruct((grad_t.shape[0], width), jnp.float32),
        ],
    )(query_rows, padded_k, padded_v, coarse_k, coarse_v, counts, fine_ok, far_ok, grad_t)


def backward_kernel(q_ref, k_ref, v_ref, ck_ref, cv_ref, counts_ref, fine_ref, far_ref,
                    g_ref, att_ref, qg_ref, kg_ref, vg_ref, ckg_ref, cvg_ref):
    score_scale = 1.0 / math.sqrt(HEAD_DIM)
    lanes = q_ref.shape[1]
    low_lanes = lax.broadcasted_iota(jnp.int32, (BLOCK, lanes), 1) < HEAD_DIM
    coarse_k = ck_ref[...]
    coarse_v = cv_ref[...]
    counts = counts_ref[...]
    contract_last = (((1,), (1,)), ((), ()))
    kg_ref[...] = jnp.zeros_like(kg_ref)
    vg_ref[...] = jnp.zeros_like(vg_ref)
    coarse_kg = jnp.zeros(ckg_ref.shape, jnp.float32)
    coarse_vg = jnp.zeros(cvg_ref.shape, jnp.float32)
    for block in range(q_ref.shape[0] // BLOCK):
        rows = pl.ds(block * BLOCK, BLOCK)
        window = pl.ds(block * BLOCK, 3 * BLOCK)
        query = q_ref[rows, :]
        grad = g_ref[rows, :]
        att = att_ref[rows, :].astype(jnp.float32)
        key_win = k_ref[window, :]
        value_win = v_ref[window, :]
        fine_ok = fine_ref[pl.ds(block, 1), :] > 0
        far_ok = far_ref[pl.ds(block, 1), :] > 0
        query_grads = []
        key_grad = jnp.zeros((3 * BLOCK, lanes), jnp.float32)
        value_grad = jnp.zeros((3 * BLOCK, lanes), jnp.float32)
        for half in range(2):
            own = low_lanes if half == 0 else jnp.logical_not(low_lanes)
            query_h = jnp.where(own, query, jnp.zeros_like(query))
            grad_h = jnp.where(own, grad, jnp.zeros_like(grad))
            fine_s = lax.dot_general(query_h, key_win, contract_last,
                                     preferred_element_type=jnp.float32) * score_scale
            coarse_s = lax.dot_general(query_h, coarse_k, contract_last,
                                       preferred_element_type=jnp.float32) * score_scale
            fine_s = jnp.where(fine_ok, fine_s, -jnp.inf)
            coarse_s = jnp.where(far_ok, coarse_s, -jnp.inf)
            top = jnp.maximum(jnp.max(fine_s, axis=1, keepdims=True),
                              jnp.max(coarse_s, axis=1, keepdims=True))
            fine_e = jnp.exp(fine_s - top)
            coarse_e = counts * jnp.exp(coarse_s - top)
            total = (jnp.sum(fine_e, axis=1, keepdims=True)
                     + jnp.sum(coarse_e, axis=1, keepdims=True))
            fine_w = fine_e / total
            coarse_w = coarse_e / total
            fine_dot = lax.dot_general(grad_h, value_win, contract_last,
                                       preferred_element_type=jnp.float32)
            coarse_dot = lax.dot_general(grad_h, coarse_v, contract_last,
                                         preferred_element_type=jnp.float32)
            delta = jnp.sum(jnp.where(own, grad.astype(jnp.float32) * att, 0.0),
                            axis=1, keepdims=True)
            fine_ds = fine_w * (fine_dot - delta)
            coarse_ds = coarse_w * (coarse_dot - delta)
            fine_ds_b = fine_ds.astype(jnp.bfloat16)
            coarse_ds_b = coarse_ds.astype(jnp.bfloat16)
            query_grads.append(
                (jnp.dot(fine_ds_b, key_win, preferred_element_type=jnp.float32)
                 + jnp.dot(coarse_ds_b, coarse_k, preferred_element_type=jnp.float32))
                * score_scale)
            fine_ds_t = fine_ds.T.astype(jnp.bfloat16)
            coarse_ds_t = coarse_ds.T.astype(jnp.bfloat16)
            fine_w_t = fine_w.T.astype(jnp.bfloat16)
            coarse_w_t = coarse_w.T.astype(jnp.bfloat16)
            key_grad = key_grad + jnp.dot(fine_ds_t, query_h,
                                          preferred_element_type=jnp.float32) * score_scale
            value_grad = value_grad + jnp.dot(fine_w_t, grad_h,
                                              preferred_element_type=jnp.float32)
            coarse_kg = coarse_kg + jnp.dot(coarse_ds_t, query_h,
                                            preferred_element_type=jnp.float32) * score_scale
            coarse_vg = coarse_vg + jnp.dot(coarse_w_t, grad_h,
                                            preferred_element_type=jnp.float32)
        qg_ref[rows, :] = jnp.where(low_lanes, query_grads[0], query_grads[1]).astype(qg_ref.dtype)
        kg_ref[window, :] += key_grad
        vg_ref[window, :] += value_grad
    ckg_ref[...] = coarse_kg
    cvg_ref[...] = coarse_vg


def attention_backward(query_rows, padded_k, padded_v, coarse_k, coarse_v, counts, fine_ok,
                       far_ok, grad_rows, attended_rows):
    tokens, width = query_rows.shape
    lanes = 2 * HEAD_DIM
    by_pair = lambda rows: pl.BlockSpec((rows, lanes), lambda pair: (0, pair))
    whole = lambda shape: pl.BlockSpec(shape, lambda pair: (0, 0))
    wide = lambda rows: jax.ShapeDtypeStruct((rows, width), jnp.float32)
    return pl.pallas_call(
        backward_kernel,
        grid=(width // lanes,),
        in_specs=[
            by_pair(tokens),
            by_pair(padded_k.shape[0]),
            by_pair(padded_v.shape[0]),
            by_pair(coarse_k.shape[0]),
            pl.BlockSpec((coarse_v.shape[0], lanes), lambda pair: (0, pair + width // lanes)),
            whole(counts.shape),
            whole(fine_ok.shape),
            whole(far_ok.shape),
            by_pair(tokens),
            by_pair(tokens),
        ],
        out_specs=[
            by_pair(tokens),
            by_pair(padded_k.shape[0]),
            by_pair(padded_v.shape[0]),
            by_pair(coarse_k.shape[0]),
            by_pair(coarse_v.shape[0]),
        ],
        out_shape=[
            jax.ShapeDtypeStruct((tokens, width), jnp.bfloat16),
            wide(padded_k.shape[0]),
            wide(padded_v.shape[0]),
            wide(coarse_k.shape[0]),
            wide(coarse_v.shape[0]),
        ],
    )(query_rows, padded_k, padded_v, coarse_k, coarse_v, counts, fine_ok, far_ok, grad_rows,
      attended_rows)


def block_windows(padded, local_blocks):
    return jnp.concatenate(
        [padded[0:local_blocks], padded[1 : local_blocks + 1], padded[2 : local_blocks + 2]], axis=1
    )


def fold_windows(grads, local_blocks):
    parts = grads.reshape((local_blocks, 3, BLOCK) + grads.shape[2:])
    edge_zero = jnp.zeros((1,) + parts.shape[2:], jnp.float32)
    left_part = jnp.concatenate([parts[:, 0], edge_zero, edge_zero], axis=0)
    middle = jnp.concatenate([edge_zero, parts[:, 1], edge_zero], axis=0)
    right_part = jnp.concatenate([edge_zero, edge_zero, parts[:, 2]], axis=0)
    return left_part + middle + right_part


def per_device(queries, keys, values, out_weight, out_grad, pooled):
    query_rows = queries[0]
    key_rows = keys[0]
    value_rows = values[0]
    grad_out = out_grad[0]
    tokens, model_width = query_rows.shape
    local_blocks = tokens // BLOCK
    seq_devices = lax.axis_size("seq")
    seq_index = lax.axis_index("seq")
    all_blocks = local_blocks * seq_devices
    score_scale = 1.0 / math.sqrt(HEAD_DIM)
    pooled_mask = pooled[0].reshape(local_blocks, BLOCK).astype(jnp.float32)
    counts = jnp.sum(pooled_mask, axis=1)
    divisor = jnp.maximum(counts, 1.0)
    pooled_bf = pooled_mask.astype(jnp.bfloat16)
    key_sum = jnp.einsum(
        "nb,nbd->nd",
        pooled_bf,
        key_rows.reshape(local_blocks, BLOCK, model_width),
        preferred_element_type=jnp.float32,
    )
    value_sum = jnp.einsum(
        "nb,nbd->nd",
        pooled_bf,
        value_rows.reshape(local_blocks, BLOCK, model_width),
        preferred_element_type=jnp.float32,
    )
    coarse_keys = (key_sum / divisor[:, None]).astype(jnp.bfloat16)
    coarse_values = (value_sum / divisor[:, None]).astype(jnp.bfloat16)
    count_cols = jnp.broadcast_to(counts.astype(jnp.bfloat16)[:, None], (local_blocks, 128))
    packed = jnp.concatenate([coarse_keys, coarse_values, count_cols], axis=1)
    gathered = doubling_gather(packed, "seq").reshape(all_blocks, packed.shape[1])
    gathered_counts = gathered[:, 2 * model_width].astype(jnp.float32)
    paired = jnp.stack([key_rows, value_rows])
    extended = padded_2(paired, (("seq", 1),), BLOCK)
    padded_kv = extended.reshape(2, local_blocks + 2, BLOCK, HEADS, HEAD_DIM)
    local_ids = seq_index * local_blocks + jnp.arange(local_blocks)
    offsets = jnp.repeat(jnp.arange(3) - 1, BLOCK)
    key_blocks = local_ids[:, None] + offsets[None, :]
    fine_ok = (key_blocks >= 0) & (key_blocks < all_blocks)
    far_ok = jnp.abs(local_ids[:, None] - jnp.arange(all_blocks)[None, :]) >= 2
    padded_rows = extended.reshape(2, (local_blocks + 2) * BLOCK, model_width)
    grad_norm = 1.0 / math.sqrt(seq_devices * tokens)
    attended_rows, full_term = attention_forward(
        query_rows,
        padded_rows[0],
        padded_rows[1],
        gathered,
        gathered,
        gathered_counts[None, :],
        fine_ok.astype(jnp.float32),
        far_ok.astype(jnp.float32),
        grad_out.T,
        grad_norm,
    )
    attended_grad = jnp.dot(grad_out, out_weight, preferred_element_type=jnp.float32).astype(
        jnp.bfloat16
    )
    seq_part = lax.psum_scatter(full_term, "seq", scatter_dimension=0, tiled=True)
    full_term, attended_grad = lax.optimization_barrier((full_term, attended_grad))
    query_grad, key_pad, value_pad, coarse_key_all, coarse_value_all = attention_backward(
        query_rows,
        padded_rows[0],
        padded_rows[1],
        gathered,
        gathered,
        gathered_counts[None, :],
        fine_ok.astype(jnp.float32),
        far_ok.astype(jnp.float32),
        attended_grad,
        attended_rows,
    )
    query_grad = query_grad.reshape(1, tokens, model_width)
    key_ext = key_pad.reshape(local_blocks + 2, BLOCK, model_width)
    value_ext = value_pad.reshape(local_blocks + 2, BLOCK, model_width)
    edge_first = jnp.stack([key_ext[0], value_ext[0]])
    edge_last = jnp.stack([key_ext[local_blocks + 1], value_ext[local_blocks + 1]])
    from_right = from_behind(edge_first, "seq", -1)
    from_left = from_behind(edge_last, "seq", 1)
    zeros_mid = jnp.zeros((2, local_blocks - 1, BLOCK, model_width), jnp.float32)
    boundary = jnp.concatenate([from_left[:, None], zeros_mid], axis=1) + jnp.concatenate(
        [zeros_mid, from_right[:, None]], axis=1
    )
    coarse_all = jnp.concatenate(
        [
            coarse_key_all.reshape(all_blocks, model_width),
            coarse_value_all.reshape(all_blocks, model_width),
        ],
        axis=1,
    )
    owned_grads = halving_scatter(
        coarse_all.reshape(seq_devices, local_blocks, 2 * model_width), "seq"
    )
    owned_keys = owned_grads[:, :model_width] / divisor[:, None]
    owned_values = owned_grads[:, model_width:] / divisor[:, None]
    spread_keys = owned_keys[:, None, :] * pooled_mask[:, :, None]
    spread_values = owned_values[:, None, :] * pooled_mask[:, :, None]
    key_grad = (
        (key_ext[1 : local_blocks + 1] + boundary[0] + spread_keys)
        .astype(jnp.bfloat16)
        .reshape(1, tokens, model_width)
    )
    value_grad = (
        (value_ext[1 : local_blocks + 1] + boundary[1] + spread_values)
        .astype(jnp.bfloat16)
        .reshape(1, tokens, model_width)
    )
    seq_part, query_grad, key_grad, value_grad = lax.optimization_barrier(
        (seq_part, query_grad, key_grad, value_grad)
    )
    dp_devices = lax.axis_size("dp")
    dp_rows = halving_scatter(seq_part.reshape(dp_devices, -1, model_width), "dp")
    weight_grad = doubling_gather(dp_rows, "dp").reshape(-1, model_width)
    return (query_grad, key_grad, value_grad, weight_grad)


def solution(mesh):
    placed = (
        P("dp", "seq", None),
        P("dp", "seq", None),
        P("dp", "seq", None),
        P(),
        P("dp", "seq", None),
        P("dp", "seq"),
    )
    return jax.shard_map(
        per_device,
        mesh=mesh,
        in_specs=placed,
        out_specs=(
            P("dp", "seq", None),
            P("dp", "seq", None),
            P("dp", "seq", None),
            P("seq", None),
        ),
        check_vma=False,
    )
```

```python
import functools
import math

import jax
import jax.numpy as jnp
from jax import lax
from jax.experimental import pallas as pl
from jax.experimental.pallas import tpu as pltpu
from jax.sharding import PartitionSpec as P

HEADS = 16
HEAD_DIM = 64
BLOCK = 128


def padded_2(block, sides, width):
    for axis, dim in sides:
        count = lax.axis_size(axis)
        forward = [(i, i + 1) for i in range(count - 1)]
        backward = [(target, source) for source, target in forward]
        low = lax.ppermute(
            lax.slice_in_dim(block, block.shape[dim] - width, None, axis=dim), axis, forward
        )
        high = lax.ppermute(lax.slice_in_dim(block, 0, width, axis=dim), axis, backward)
        block = jnp.concatenate([low, block, high], axis=dim)
    return block


def from_behind(value, axis, steps):
    count = lax.axis_size(axis)
    leading, last = (max(0, -steps), min(count, count - steps))
    return lax.ppermute(value, axis, [(source, source + steps) for source in range(leading, last)])


def xor_pairs(count, bit):
    return [(source, source ^ (1 << bit)) for source in range(count)]


def own_bit(axis, bit):
    return (lax.axis_index(axis) // (1 << bit)) % 2


def doubling_gather(piece, axis):
    count = lax.axis_size(axis)
    bits = count.bit_length() - 1
    held = piece
    for done, bit in enumerate(reversed(range(bits))):
        other = lax.ppermute(held, axis, xor_pairs(count, bit))
        mine_low = own_bit(axis, bit) == 0
        low = jnp.where(mine_low, held, other)
        high = jnp.where(mine_low, other, held)
        held = jnp.stack([low, high], axis=done)
    return held.reshape((count,) + piece.shape)


def halving_scatter(stack, axis):
    count = lax.axis_size(axis)
    bits = count.bit_length() - 1
    held = stack.reshape((2,) * bits + stack.shape[1:])
    for bit in range(bits):
        dim = bits - 1 - bit
        mine = own_bit(axis, bit)
        keep = lax.dynamic_index_in_dim(held, mine, dim, keepdims=False)
        send = lax.dynamic_index_in_dim(held, 1 - mine, dim, keepdims=False)
        held = keep + lax.ppermute(send, axis, xor_pairs(count, bit))
    return held


def doubling_sum(value, axis):
    count = lax.axis_size(axis)
    for bit in range(count.bit_length() - 1):
        value = value + lax.ppermute(value, axis, xor_pairs(count, bit))
    return value


def forward_kernel(term_scale, q_ref, k_ref, v_ref, ck_ref, cv_ref, counts_ref, fine_ref, far_ref,
                   grad_t_ref, att_ref, term_ref):
    score_scale = 1.0 / math.sqrt(HEAD_DIM)
    lanes = q_ref.shape[1]
    lane_head = lax.broadcasted_iota(jnp.int32, (BLOCK, lanes), 1) // HEAD_DIM
    coarse_k = ck_ref[...]
    coarse_v = cv_ref[...]
    counts = counts_ref[...]
    contract_last = (((1,), (1,)), ((), ()))
    for block in range(q_ref.shape[0] // BLOCK):
        query = q_ref[pl.ds(block * BLOCK, BLOCK), :]
        key_win = k_ref[pl.ds(block * BLOCK, 3 * BLOCK), :]
        value_win = v_ref[pl.ds(block * BLOCK, 3 * BLOCK), :]
        fine_ok = fine_ref[pl.ds(block, 1), :] > 0
        far_ok = far_ref[pl.ds(block, 1), :] > 0
        att_all = None
        for half in range(lanes // HEAD_DIM):
            own = lane_head == half
            query_h = jnp.where(own, query, jnp.zeros_like(query))
            fine_s = lax.dot_general(query_h, key_win, contract_last,
                                     preferred_element_type=jnp.float32) * score_scale
            coarse_s = lax.dot_general(query_h, coarse_k, contract_last,
                                       preferred_element_type=jnp.float32) * score_scale
            fine_s = jnp.where(fine_ok, fine_s, -jnp.inf)
            coarse_s = jnp.where(far_ok, coarse_s, -jnp.inf)
            top = jnp.maximum(jnp.max(fine_s, axis=1, keepdims=True),
                              jnp.max(coarse_s, axis=1, keepdims=True))
            fine_e = jnp.exp(fine_s - top)
            coarse_e = counts * jnp.exp(coarse_s - top)
            total = (jnp.sum(fine_e, axis=1, keepdims=True)
                     + jnp.sum(coarse_e, axis=1, keepdims=True))
            fine_w = (fine_e / total).astype(jnp.bfloat16)
            coarse_w = (coarse_e / total).astype(jnp.bfloat16)
            att = (jnp.dot(fine_w, value_win, preferred_element_type=jnp.float32)
                   + jnp.dot(coarse_w, coarse_v, preferred_element_type=jnp.float32))
            att_all = att if att_all is None else jnp.where(own, att, att_all)
        rows = pl.ds(block * BLOCK, BLOCK)
        att_ref[rows, :] = att_all.astype(att_ref.dtype)
    term_ref[...] = jnp.dot(grad_t_ref[...], att_ref[...],
                            preferred_element_type=jnp.float32) * term_scale


def attention_forward(query_rows, padded_k, padded_v, coarse_k, coarse_v, counts, fine_ok, far_ok,
                      grad_t, term_scale):
    tokens, width = query_rows.shape
    lanes = 8 * HEAD_DIM
    by_pair = lambda rows: pl.BlockSpec((rows, lanes), lambda pair: (0, pair))
    whole = lambda shape: pl.BlockSpec(shape, lambda pair: (0, 0))
    return pl.pallas_call(
        functools.partial(forward_kernel, term_scale),
        grid=(width // lanes,),
        in_specs=[
            by_pair(tokens),
            by_pair(padded_k.shape[0]),
            by_pair(padded_v.shape[0]),
            by_pair(coarse_k.shape[0]),
            pl.BlockSpec((coarse_v.shape[0], lanes), lambda pair: (0, pair + width // lanes)),
            whole(counts.shape),
            whole(fine_ok.shape),
            whole(far_ok.shape),
            whole(grad_t.shape),
        ],
        out_specs=[by_pair(tokens), by_pair(grad_t.shape[0])],
        out_shape=[
            jax.ShapeDtypeStruct((tokens, width), jnp.bfloat16),
            jax.ShapeDtypeStruct((grad_t.shape[0], width), jnp.float32),
        ],
    )(query_rows, padded_k, padded_v, coarse_k, coarse_v, counts, fine_ok, far_ok, grad_t)


def backward_kernel(q_ref, k_ref, v_ref, ck_ref, cv_ref, counts_ref, fine_ref, far_ref,
                    g_ref, att_ref, qg_ref, kg_ref, vg_ref, ckg_ref, cvg_ref):
    score_scale = 1.0 / math.sqrt(HEAD_DIM)
    lanes = q_ref.shape[1]
    low_lanes = lax.broadcasted_iota(jnp.int32, (BLOCK, lanes), 1) < HEAD_DIM
    coarse_k = ck_ref[...]
    coarse_v = cv_ref[...]
    counts = counts_ref[...]
    contract_last = (((1,), (1,)), ((), ()))
    kg_ref[...] = jnp.zeros_like(kg_ref)
    vg_ref[...] = jnp.zeros_like(vg_ref)
    coarse_kg = jnp.zeros(ckg_ref.shape, jnp.float32)
    coarse_vg = jnp.zeros(cvg_ref.shape, jnp.float32)
    for block in range(q_ref.shape[0] // BLOCK):
        rows = pl.ds(block * BLOCK, BLOCK)
        window = pl.ds(block * BLOCK, 3 * BLOCK)
        query = q_ref[rows, :]
        grad = g_ref[rows, :]
        att = att_ref[rows, :].astype(jnp.float32)
        key_win = k_ref[window, :]
        value_win = v_ref[window, :]
        fine_ok = fine_ref[pl.ds(block, 1), :] > 0
        far_ok = far_ref[pl.ds(block, 1), :] > 0
        query_grads = []
        key_grad = jnp.zeros((3 * BLOCK, lanes), jnp.float32)
        value_grad = jnp.zeros((3 * BLOCK, lanes), jnp.float32)
        for half in range(2):
            own = low_lanes if half == 0 else jnp.logical_not(low_lanes)
            query_h = jnp.where(own, query, jnp.zeros_like(query))
            grad_h = jnp.where(own, grad, jnp.zeros_like(grad))
            fine_s = lax.dot_general(query_h, key_win, contract_last,
                                     preferred_element_type=jnp.float32) * score_scale
            coarse_s = lax.dot_general(query_h, coarse_k, contract_last,
                                       preferred_element_type=jnp.float32) * score_scale
            fine_s = jnp.where(fine_ok, fine_s, -jnp.inf)
            coarse_s = jnp.where(far_ok, coarse_s, -jnp.inf)
            top = jnp.maximum(jnp.max(fine_s, axis=1, keepdims=True),
                              jnp.max(coarse_s, axis=1, keepdims=True))
            fine_e = jnp.exp(fine_s - top)
            coarse_e = counts * jnp.exp(coarse_s - top)
            total = (jnp.sum(fine_e, axis=1, keepdims=True)
                     + jnp.sum(coarse_e, axis=1, keepdims=True))
            fine_w = fine_e / total
            coarse_w = coarse_e / total
            fine_dot = lax.dot_general(grad_h, value_win, contract_last,
                                       preferred_element_type=jnp.float32)
            coarse_dot = lax.dot_general(grad_h, coarse_v, contract_last,
                                         preferred_element_type=jnp.float32)
            delta = jnp.sum(jnp.where(own, grad.astype(jnp.float32) * att, 0.0),
                            axis=1, keepdims=True)
            fine_ds = fine_w * (fine_dot - delta)
            coarse_ds = coarse_w * (coarse_dot - delta)
            fine_ds_b = fine_ds.astype(jnp.bfloat16)
            coarse_ds_b = coarse_ds.astype(jnp.bfloat16)
            query_grads.append(
                (jnp.dot(fine_ds_b, key_win, preferred_element_type=jnp.float32)
                 + jnp.dot(coarse_ds_b, coarse_k, preferred_element_type=jnp.float32))
                * score_scale)
            fine_ds_t = fine_ds.T.astype(jnp.bfloat16)
            coarse_ds_t = coarse_ds.T.astype(jnp.bfloat16)
            fine_w_t = fine_w.T.astype(jnp.bfloat16)
            coarse_w_t = coarse_w.T.astype(jnp.bfloat16)
            key_grad = key_grad + jnp.dot(fine_ds_t, query_h,
                                          preferred_element_type=jnp.float32) * score_scale
            value_grad = value_grad + jnp.dot(fine_w_t, grad_h,
                                              preferred_element_type=jnp.float32)
            coarse_kg = coarse_kg + jnp.dot(coarse_ds_t, query_h,
                                            preferred_element_type=jnp.float32) * score_scale
            coarse_vg = coarse_vg + jnp.dot(coarse_w_t, grad_h,
                                            preferred_element_type=jnp.float32)
        qg_ref[rows, :] = jnp.where(low_lanes, query_grads[0], query_grads[1]).astype(qg_ref.dtype)
        kg_ref[window, :] += key_grad
        vg_ref[window, :] += value_grad
    ckg_ref[...] = coarse_kg
    cvg_ref[...] = coarse_vg


def attention_backward(query_rows, padded_k, padded_v, coarse_k, coarse_v, counts, fine_ok,
                       far_ok, grad_rows, attended_rows):
    tokens, width = query_rows.shape
    lanes = 2 * HEAD_DIM
    by_pair = lambda rows: pl.BlockSpec((rows, lanes), lambda pair: (0, pair))
    whole = lambda shape: pl.BlockSpec(shape, lambda pair: (0, 0))
    wide = lambda rows: jax.ShapeDtypeStruct((rows, width), jnp.float32)
    return pl.pallas_call(
        backward_kernel,
        grid=(width // lanes,),
        in_specs=[
            by_pair(tokens),
            by_pair(padded_k.shape[0]),
            by_pair(padded_v.shape[0]),
            by_pair(coarse_k.shape[0]),
            pl.BlockSpec((coarse_v.shape[0], lanes), lambda pair: (0, pair + width // lanes)),
            whole(counts.shape),
            whole(fine_ok.shape),
            whole(far_ok.shape),
            by_pair(tokens),
            by_pair(tokens),
        ],
        out_specs=[
            by_pair(tokens),
            by_pair(padded_k.shape[0]),
            by_pair(padded_v.shape[0]),
            by_pair(coarse_k.shape[0]),
            by_pair(coarse_v.shape[0]),
        ],
        out_shape=[
            jax.ShapeDtypeStruct((tokens, width), jnp.bfloat16),
            wide(padded_k.shape[0]),
            wide(padded_v.shape[0]),
            wide(coarse_k.shape[0]),
            wide(coarse_v.shape[0]),
        ],
    )(query_rows, padded_k, padded_v, coarse_k, coarse_v, counts, fine_ok, far_ok, grad_rows,
      attended_rows)


def block_windows(padded, local_blocks):
    return jnp.concatenate(
        [padded[0:local_blocks], padded[1 : local_blocks + 1], padded[2 : local_blocks + 2]], axis=1
    )


def fold_windows(grads, local_blocks):
    parts = grads.reshape((local_blocks, 3, BLOCK) + grads.shape[2:])
    edge_zero = jnp.zeros((1,) + parts.shape[2:], jnp.float32)
    left_part = jnp.concatenate([parts[:, 0], edge_zero, edge_zero], axis=0)
    middle = jnp.concatenate([edge_zero, parts[:, 1], edge_zero], axis=0)
    right_part = jnp.concatenate([edge_zero, edge_zero, parts[:, 2]], axis=0)
    return left_part + middle + right_part


def per_device(queries, keys, values, out_weight, out_grad, pooled):
    query_rows = queries[0]
    key_rows = keys[0]
    value_rows = values[0]
    grad_out = out_grad[0]
    tokens, model_width = query_rows.shape
    local_blocks = tokens // BLOCK
    seq_devices = lax.axis_size("seq")
    seq_index = lax.axis_index("seq")
    all_blocks = local_blocks * seq_devices
    score_scale = 1.0 / math.sqrt(HEAD_DIM)
    pooled_mask = pooled[0].reshape(local_blocks, BLOCK).astype(jnp.float32)
    counts = jnp.sum(pooled_mask, axis=1)
    divisor = jnp.maximum(counts, 1.0)
    pooled_bf = pooled_mask.astype(jnp.bfloat16)
    key_sum = jnp.einsum(
        "nb,nbd->nd",
        pooled_bf,
        key_rows.reshape(local_blocks, BLOCK, model_width),
        preferred_element_type=jnp.float32,
    )
    value_sum = jnp.einsum(
        "nb,nbd->nd",
        pooled_bf,
        value_rows.reshape(local_blocks, BLOCK, model_width),
        preferred_element_type=jnp.float32,
    )
    coarse_keys = (key_sum / divisor[:, None]).astype(jnp.bfloat16)
    coarse_values = (value_sum / divisor[:, None]).astype(jnp.bfloat16)
    count_cols = jnp.broadcast_to(counts.astype(jnp.bfloat16)[:, None], (local_blocks, 128))
    packed = jnp.concatenate([coarse_keys, coarse_values, count_cols], axis=1)
    gathered = doubling_gather(packed, "seq").reshape(all_blocks, packed.shape[1])
    gathered_counts = gathered[:, 2 * model_width].astype(jnp.float32)
    paired = jnp.stack([key_rows, value_rows])
    extended = padded_2(paired, (("seq", 1),), BLOCK)
    padded_kv = extended.reshape(2, local_blocks + 2, BLOCK, HEADS, HEAD_DIM)
    local_ids = seq_index * local_blocks + jnp.arange(local_blocks)
    offsets = jnp.repeat(jnp.arange(3) - 1, BLOCK)
    key_blocks = local_ids[:, None] + offsets[None, :]
    fine_ok = (key_blocks >= 0) & (key_blocks < all_blocks)
    far_ok = jnp.abs(local_ids[:, None] - jnp.arange(all_blocks)[None, :]) >= 2
    padded_rows = extended.reshape(2, (local_blocks + 2) * BLOCK, model_width)
    grad_norm = 1.0 / math.sqrt(seq_devices * tokens)
    attended_rows, full_term = attention_forward(
        query_rows,
        padded_rows[0],
        padded_rows[1],
        gathered,
        gathered,
        gathered_counts[None, :],
        fine_ok.astype(jnp.float32),
        far_ok.astype(jnp.float32),
        grad_out.T,
        grad_norm,
    )
    attended_grad = jnp.dot(grad_out, out_weight, preferred_element_type=jnp.float32).astype(
        jnp.bfloat16
    )
    seq_part = lax.psum_scatter(full_term, "seq", scatter_dimension=0, tiled=True)
    full_term, attended_grad = lax.optimization_barrier((full_term, attended_grad))
    query_grad, key_pad, value_pad, coarse_key_all, coarse_value_all = attention_backward(
        query_rows,
        padded_rows[0],
        padded_rows[1],
        gathered,
        gathered,
        gathered_counts[None, :],
        fine_ok.astype(jnp.float32),
        far_ok.astype(jnp.float32),
        attended_grad,
        attended_rows,
    )
    query_grad = query_grad.reshape(1, tokens, model_width)
    key_ext = key_pad.reshape(local_blocks + 2, BLOCK, model_width)
    value_ext = value_pad.reshape(local_blocks + 2, BLOCK, model_width)
    edge_first = jnp.stack([key_ext[0], value_ext[0]])
    edge_last = jnp.stack([key_ext[local_blocks + 1], value_ext[local_blocks + 1]])
    from_right = from_behind(edge_first, "seq", -1)
    from_left = from_behind(edge_last, "seq", 1)
    zeros_mid = jnp.zeros((2, local_blocks - 1, BLOCK, model_width), jnp.float32)
    boundary = jnp.concatenate([from_left[:, None], zeros_mid], axis=1) + jnp.concatenate(
        [zeros_mid, from_right[:, None]], axis=1
    )
    coarse_all = jnp.concatenate(
        [
            coarse_key_all.reshape(all_blocks, model_width),
            coarse_value_all.reshape(all_blocks, model_width),
        ],
        axis=1,
    )
    owned_grads = halving_scatter(
        coarse_all.reshape(seq_devices, local_blocks, 2 * model_width), "seq"
    )
    owned_keys = owned_grads[:, :model_width] / divisor[:, None]
    owned_values = owned_grads[:, model_width:] / divisor[:, None]
    spread_keys = owned_keys[:, None, :] * pooled_mask[:, :, None]
    spread_values = owned_values[:, None, :] * pooled_mask[:, :, None]
    key_grad = (
        (key_ext[1 : local_blocks + 1] + boundary[0] + spread_keys)
        .astype(jnp.bfloat16)
        .reshape(1, tokens, model_width)
    )
    value_grad = (
        (value_ext[1 : local_blocks + 1] + boundary[1] + spread_values)
        .astype(jnp.bfloat16)
        .reshape(1, tokens, model_width)
    )
    seq_part, query_grad, key_grad, value_grad = lax.optimization_barrier(
        (seq_part, query_grad, key_grad, value_grad)
    )
    dp_devices = lax.axis_size("dp")
    dp_rows = halving_scatter(seq_part.reshape(dp_devices, -1, model_width), "dp")
    weight_grad = doubling_gather(dp_rows, "dp").reshape(-1, model_width)
    return (query_grad, key_grad, value_grad, weight_grad)


def solution(mesh):
    placed = (
        P("dp", "seq", None),
        P("dp", "seq", None),
        P("dp", "seq", None),
        P(),
        P("dp", "seq", None),
        P("dp", "seq"),
    )
    return jax.shard_map(
        per_device,
        mesh=mesh,
        in_specs=placed,
        out_specs=(
            P("dp", "seq", None),
            P("dp", "seq", None),
            P("dp", "seq", None),
            P("seq", None),
        ),
        check_vma=False,
    )
```
